32 devices in a mesh: axial: 16 (over z, y, x), radial: 2 (over core).
Axes of the slice: x: 2, y: 2, z: 4, core: 2. Of those that a mesh axis runs over, the one named last changes fastest.
Arguments:
- parcel_load: float32 [5, 524288], P(None, ('axial', 'radial')), may hold values from -6 to 6
- parcel_offset: float32 [3, 524288], P(None, ('axial', 'radial')), may hold values from 0 to 1
- parcel_cell: int32 [524288], P(('axial', 'radial')), may hold values from 0 to 63
- cross_rows: int32 [2, 262144], P(None, ('axial', 'radial')), may hold values from -1 to 16383, as said below
- block_brick: int32 [8192], P(('axial', 'radial')), may hold values from 0 to 1023
- gas: float32 [5, 64, 128, 256], P(None, 'axial', 'radial'), may hold values from -6 to 6
Outputs:
- source: float32 [5, 64, 128, 256], P(None, 'axial', 'radial')
- parcel_gas: bfloat16 [5, 1048576], P(None, ('axial', 'radial'))
The draws below stay inside these ranges and needn't reach their ends.
Inputs may be any that keep to these rules, and one draw needn't show every extreme that they name: `cross_rows`: on each half slab the non-empty entries of a list come first, and all rows named in both lists are distinct; the upward lists of some half slabs are full with 8192 rows in every draw.
All inputs are finite; a program needn't handle non-finite values.
Results may differ from the reference program's by a relative error of at most 0.001.
Values sent between devices are 32-bit elements; how exact they have to be, the bound alone decides.
No kernel may reach another device: no remote copies, remote signals or barrier semaphores. Data moves between devices by JAX's collectives and lax.ppermute only.
A program may use at most 64 MiB of HBM per device.

```python
import jax
import jax.numpy as jnp
from jax import lax

CX = 4
CY = 64
CZ = 256
PAR_DEV = 16384
MIG = 8192
NX = 64
NY = 128
BLK_DEV = 256
BRICKS_DEV = 1024
PARCELS = 524288
N_AXIAL = 16
DEVICES = 32


def draw_cross_rows(key, part):
    device_keys = jax.random.split(jax.random.fold_in(key, 11), DEVICES)

    def choose_rows(device_key):
        return jax.random.permutation(device_key, PAR_DEV)[:2 * MIG]
    chosen = jax.vmap(choose_rows)(device_keys).astype(jnp.int32).reshape(DEVICES, 2, MIG)
    axial_index = jnp.arange(DEVICES, dtype=jnp.int32) // (DEVICES // N_AXIAL)
    low_count = jax.random.randint(jax.random.fold_in(key, 12), (DEVICES,), MIG // 8, MIG // 4 + 1)
    up_count = jnp.where(axial_index < max(N_AXIAL // 8, 1), MIG, low_count)
    down_count = jax.random.randint(jax.random.fold_in(key, 13), (DEVICES,), MIG // 8, MIG // 4 + 1)
    slot_index = jnp.arange(MIG, dtype=jnp.int32)[None, :]
    upward = jnp.where(slot_index < up_count[:, None], chosen[:, 0], -1)
    downward = jnp.where(slot_index < down_count[:, None], chosen[:, 1], -1)
    return jnp.stack([upward, downward], 0).reshape(2, DEVICES * MIG).astype(jnp.int32)


def place_ends(values, rng, low, high):
    longest = values.shape.index(max(values.shape))
    spots = []
    for shift in (0, 1):
        where = [jax.random.randint(jax.random.fold_in(rng, axis), (), 0, length) for axis, length in enumerate(values.shape)]
        where[longest] = (where[longest] + shift) % values.shape[longest]
        spots.append(tuple(where))
    return values.at[spots[0]].set(low).at[spots[1]].set(high)


def block_levels(own_key, shape, shards, least, top_value):
    gain = 1.0
    for position, parts in shards:
        draws = jax.random.uniform(jax.random.fold_in(jax.random.fold_in(own_key, 6), position), (parts,), jnp.float32, least / len(shards), top_value / len(shards))
        gain = gain * jnp.repeat(jnp.exp(draws), shape[position] // parts).reshape((-1,) + (1,) * (len(shape) - 1 - position))
    return gain


def normal_values(key, dims, width, bound, cuts=(), kind=jnp.bfloat16):
    entries = jax.random.normal(key, dims, jnp.float32) * width
    if len(cuts) > 0:
        entries = block_levels(key, dims, cuts, -0.22, 0.18) * entries
    return jnp.clip(entries, min=-bound, max=bound).astype(kind)


def setup_inputs(seed: int = 0) -> dict:
    keys = jax.random.split(jax.random.key(seed), 7)
    parcel_load = normal_values(keys[0], (5, PARCELS), 1.0, 6.0, ((1, 32),), jnp.float32)
    parcel_offset = jnp.clip(1.0 * jax.random.uniform(keys[1], (3, PARCELS), jnp.float32) ** block_levels(keys[1], (3, PARCELS), ((1, 32),), -0.2, 0.2), 0.0, 1.0)
    parcel_cell = place_ends(jax.random.randint(keys[2], (PARCELS,), 0, 64), jax.random.fold_in(keys[2], 1), 0, 63).astype(jnp.int32)
    cross_rows = draw_cross_rows(jax.random.fold_in(keys[6], 71), 0)
    block_brick = place_ends(jax.random.randint(keys[4], (BLK_DEV * DEVICES,), 0, BRICKS_DEV), jax.random.fold_in(keys[4], 1), 0, BRICKS_DEV - 1).astype(jnp.int32)
    gas = normal_values(keys[5], (5, NX, NY, CZ), 1.0, 6.0, ((1, 16), (2, 2)), jnp.float32)
    return {"parcel_load": parcel_load, "parcel_offset": parcel_offset, "parcel_cell": parcel_cell, "cross_rows": cross_rows, "block_brick": block_brick, "gas": gas}


COUPLE = 0.5


def kernel_weights(cell_index, offsets):
    extent = jnp.arange(128, dtype=jnp.int32)
    brick_x = extent // 25
    brick_y = (extent // 5) % 5
    brick_z = extent % 5
    inside = (extent < 125).astype(jnp.float32)

    def factor(cell_coord, brick_coord, fraction):
        cell_coord = cell_coord[:, :, None]
        fraction = fraction[:, :, None]
        return jnp.where(brick_coord == cell_coord, 1.0 - fraction, jnp.where(brick_coord == cell_coord + 1, fraction, 0.0))

    cell_x = cell_index // 16
    cell_y = (cell_index // 4) % 4
    cell_z = cell_index % 4
    return factor(cell_x, brick_x, offsets[0]) * factor(cell_y, brick_y, offsets[1]) * factor(cell_z, brick_z, offsets[2]) * inside


def brick_index(brick_ids, span_y, span_z):
    row_bricks = span_z // 4
    plane_bricks = (span_y // 4) * row_bricks
    slab_x = brick_ids // plane_bricks
    slab_y = (brick_ids // row_bricks) % (span_y // 4)
    slab_z = brick_ids % row_bricks
    extent = jnp.arange(128, dtype=jnp.int32)
    coord_x = 4 * slab_x[:, None] + extent // 25
    coord_y = 4 * slab_y[:, None] + (extent // 5) % 5
    coord_z = 4 * slab_z[:, None] + extent % 5
    inside = (extent < 125) & (coord_z < span_z)
    flat_index = (coord_x * (span_y + 1) + coord_y) * span_z + coord_z
    return flat_index, inside


def deposit_blocks(parcel_part, brick_ids, span_y, span_z, deposit_grid):
    block_count = brick_ids.shape[0]
    block_rows = parcel_part.reshape(9, block_count, 128)
    weights = kernel_weights(block_rows[8].astype(jnp.int32), block_rows[5:8])
    spread = jnp.einsum("fgp,gpe->fge", block_rows[:5], weights, precision=lax.Precision.HIGHEST)
    flat_index, inside = brick_index(brick_ids, span_y, span_z)
    target_rows = jnp.where(inside, flat_index, deposit_grid.shape[1])
    return deposit_grid.at[:, target_rows.reshape(-1)].add(spread.reshape(5, -1), mode="drop")


def sample_blocks(parcel_part, brick_ids, span_y, span_z, gas_field):
    block_count = brick_ids.shape[0]
    block_rows = parcel_part.reshape(9, block_count, 128)
    weights = kernel_weights(block_rows[8].astype(jnp.int32), block_rows[5:8])
    flat_index, inside = brick_index(brick_ids, span_y, span_z)
    picked = gas_field[:, jnp.where(inside, flat_index, 0)] * inside.astype(jnp.float32)
    values = jnp.einsum("fge,gpe->fgp", picked, weights, precision=lax.Precision.HIGHEST)
    return values.reshape(5, block_count * 128)


def reference(parcel_load, parcel_offset, parcel_cell, cross_rows, block_brick, gas):
    device_count = DEVICES
    radial_count = DEVICES // N_AXIAL
    rows_total = PAR_DEV + 2 * MIG
    attributes = jnp.concatenate([parcel_load, parcel_offset, parcel_cell[None].astype(jnp.float32)], 0).reshape(9, device_count, PAR_DEV)
    row_lists = cross_rows.reshape(2, device_count, MIG)
    usable = row_lists >= 0
    safe_rows = jnp.maximum(row_lists, 0)
    upward = jnp.take_along_axis(attributes, safe_rows[0][None], axis=2) * usable[0][None].astype(jnp.float32)
    downward = jnp.take_along_axis(attributes, safe_rows[1][None], axis=2) * usable[1][None].astype(jnp.float32)
    hollow = jnp.zeros((9, radial_count, MIG), jnp.float32)
    from_lower = jnp.concatenate([hollow, upward[:, :device_count - radial_count]], 1)
    from_upper = jnp.concatenate([downward[:, radial_count:], hollow], 1)
    target_rows = jnp.where(usable, row_lists, PAR_DEV)
    owner_rows = jnp.broadcast_to(jnp.arange(device_count, dtype=jnp.int32)[:, None], (device_count, MIG))
    departed = jnp.zeros((device_count, PAR_DEV), jnp.float32)
    departed = departed.at[owner_rows, target_rows[0]].set(1.0, mode="drop")
    departed = departed.at[owner_rows, target_rows[1]].set(1.0, mode="drop")
    staying = jnp.concatenate([attributes[:8] * (1.0 - departed)[None], attributes[8:]], 0)
    parcels = jnp.concatenate([staying, from_lower, from_upper], 2)
    stacked = jnp.transpose(parcels, (1, 0, 2))
    brick_table = block_brick.reshape(device_count, rows_total // 128)
    device_ids = jnp.arange(device_count, dtype=jnp.int32)
    anchor = jnp.zeros((), jnp.int32)

    def deposit_device(accumulated, device_item):
        device_index, parcel_part, brick_ids = device_item
        local_grid = deposit_blocks(parcel_part, brick_ids, CY, CZ, jnp.zeros((5, (CX + 1) * (CY + 1) * CZ), jnp.float32))
        local_grid = local_grid.reshape(5, CX + 1, CY + 1, CZ)
        corner = (anchor, (device_index // radial_count) * CX, (device_index % radial_count) * CY, anchor)
        window = lax.dynamic_slice(accumulated, corner, (5, CX + 1, CY + 1, CZ))
        return lax.dynamic_update_slice(accumulated, window + local_grid, corner), None

    accumulated = jnp.zeros((5, NX + 1, NY + 1, CZ), jnp.float32)
    accumulated, _ = lax.scan(deposit_device, accumulated, (device_ids, stacked, brick_table))
    source = accumulated[:, :NX, :NY, :]
    updated_gas = gas + COUPLE * source
    padded = jnp.pad(updated_gas, ((0, 0), (0, 1), (0, 1), (0, 0)))

    def sample_device(device_item):
        device_index, parcel_part, brick_ids = device_item
        corner = (anchor, (device_index // radial_count) * CX, (device_index % radial_count) * CY, anchor)
        gas_field = lax.dynamic_slice(padded, corner, (5, CX + 1, CY + 1, CZ)).reshape(5, -1)
        return sample_blocks(parcel_part, brick_ids, CY, CZ, gas_field)

    sampled = lax.map(sample_device, (device_ids, stacked, brick_table))
    parcel_gas = jnp.transpose(sampled, (1, 0, 2)).reshape(5, device_count * rows_total).astype(jnp.bfloat16)
    return (source, parcel_gas)
```

```python
import math

import jax
import jax.numpy as jnp
from jax import lax
from jax.sharding import PartitionSpec as P

COUPLE = 0.5


def passed_along(block, axis, distance):
    devices = range(lax.axis_size(axis))
    route = [(i - distance, i) for i in devices if i - distance in devices]
    return lax.ppermute(block, axis, route)


def kernel_weights(cell_index, offsets):
    extent = jnp.arange(128, dtype=jnp.int32)
    brick_x = extent // 25
    brick_y = extent // 5 % 5
    brick_z = extent % 5
    inside = (extent < 125).astype(jnp.float32)

    def factor(cell_coord, brick_coord, fraction):
        cell_coord = cell_coord[:, :, None]
        fraction = fraction[:, :, None]
        return jnp.where(
            brick_coord == cell_coord,
            1.0 - fraction,
            jnp.where(brick_coord == cell_coord + 1, fraction, 0.0),
        )

    cell_x = cell_index // 16
    cell_y = cell_index // 4 % 4
    cell_z = cell_index % 4
    return (
        factor(cell_x, brick_x, offsets[0])
        * factor(cell_y, brick_y, offsets[1])
        * factor(cell_z, brick_z, offsets[2])
        * inside
    )


def split_windows(field, axis, count):
    core = lax.slice_in_dim(field, 0, 4 * count, axis=axis)
    core = core.reshape(field.shape[:axis] + (count, 4) + field.shape[axis + 1 :])
    tail = lax.slice_in_dim(field, 4, 4 * count + 1, stride=4, axis=axis)
    tail = jnp.expand_dims(tail, axis + 1)
    return jnp.concatenate([core, tail], axis + 1)


def merge_windows(field, axis, count, keep_tail):
    core = lax.slice_in_dim(field, 0, 4, axis=axis + 1)
    tail = lax.slice_in_dim(field, 4, 5, axis=axis + 1)
    zero_brick = jnp.zeros_like(lax.slice_in_dim(core, 0, 1, axis=axis))
    core = jnp.concatenate([core, zero_brick], axis)
    zero_tail = jnp.zeros_like(lax.slice_in_dim(tail, 0, 1, axis=axis))
    tail = jnp.concatenate([zero_tail, tail], axis)
    first = lax.slice_in_dim(core, 0, 1, axis=axis + 1) + tail
    rest = lax.slice_in_dim(core, 1, 4, axis=axis + 1)
    joined = jnp.concatenate([first, rest], axis + 1)
    joined = joined.reshape(field.shape[:axis] + (4 * (count + 1),) + field.shape[axis + 2 :])
    length = 4 * count + 1 if keep_tail else 4 * count
    return lax.slice_in_dim(joined, 0, length, axis=axis)


def radial_fold(layers):
    arrived = passed_along(layers[:, :, -1], "radial", 1)
    return layers.at[:, :, 0].add(arrived)


def departed_mask(cross_rows, resident):
    rows = cross_rows.reshape(-1)
    lanes = 128
    high = jnp.where(rows >= 0, rows // lanes, -1)
    low = jnp.where(rows >= 0, rows % lanes, -1)
    high_hot = (high[:, None] == jnp.arange(resident // lanes, dtype=jnp.int32)[None, :]).astype(jnp.bfloat16)
    low_hot = (low[:, None] == jnp.arange(lanes, dtype=jnp.int32)[None, :]).astype(jnp.bfloat16)
    counts = jnp.einsum("sh,sl->hl", high_hot, low_hot, preferred_element_type=jnp.float32)
    return counts.reshape(resident)


def per_device(parcel_load, parcel_offset, parcel_cell, cross_rows, block_brick, gas):
    span_x = gas.shape[1]
    span_y = gas.shape[2]
    span_z = gas.shape[3]
    count_x = span_x // 4
    count_y = span_y // 4
    count_z = span_z // 4
    brick_total = count_x * count_y * count_z
    resident = parcel_load.shape[1]
    block_count = block_brick.shape[0]
    group_size = math.gcd(block_count, 64)
    turn_count = block_count // group_size
    brick_numbers = jnp.arange(brick_total, dtype=jnp.int32)
    attributes = jnp.concatenate(
        [parcel_load, parcel_offset, parcel_cell[None].astype(jnp.float32)], 0
    )
    usable = cross_rows >= 0
    safe_rows = jnp.maximum(cross_rows, 0)
    upward = attributes[:, safe_rows[0]] * usable[0].astype(jnp.float32)
    downward = attributes[:, safe_rows[1]] * usable[1].astype(jnp.float32)
    from_lower = passed_along(upward, "axial", 1)
    from_upper = passed_along(downward, "axial", -1)
    departed = departed_mask(cross_rows, resident)
    staying = jnp.concatenate([attributes[:8] * (1.0 - departed)[None], attributes[8:]], 0)
    parcels = jnp.concatenate([staying, from_lower, from_upper], 1)

    def group_pieces(turn_index):
        first_block = turn_index * group_size
        parcel_part = lax.dynamic_slice_in_dim(parcels, first_block * 128, group_size * 128, 1)
        brick_ids = lax.dynamic_slice_in_dim(block_brick, first_block, group_size, 0)
        block_rows = parcel_part.reshape(9, group_size, 128)
        weights = kernel_weights(block_rows[8].astype(jnp.int32), block_rows[5:8])
        selector = (brick_ids[:, None] == brick_numbers[None, :]).astype(jnp.float32)
        return (block_rows, weights, selector)

    def deposit_turn(turn_index, brick_sums):
        block_rows, weights, selector = group_pieces(turn_index)
        spread = jnp.einsum(
            "fgp,gpe->fge", block_rows[:5], weights, precision=lax.Precision.HIGHEST
        )
        return brick_sums + jnp.einsum(
            "gb,fge->fbe", selector, spread, precision=lax.Precision.HIGHEST
        )

    brick_sums = lax.fori_loop(
        0, turn_count, deposit_turn, jnp.zeros((5, brick_total, 128), jnp.float32)
    )
    laid = brick_sums[:, :, :125].reshape(5, count_x, count_y, count_z, 5, 5, 5)
    laid = jnp.transpose(laid, (0, 1, 4, 2, 5, 3, 6))
    laid = merge_windows(laid, 1, count_x, True)
    laid = merge_windows(laid, 2, count_y, True)
    deposit_grid = merge_windows(laid, 3, count_z, False)
    incoming = passed_along(deposit_grid[:, span_x], "axial", 1)
    summed = deposit_grid[:, :span_x].at[:, 0].add(incoming)
    folded = radial_fold(summed)
    source = folded[:, :, :span_y]
    updated_gas = gas + COUPLE * source
    upper_face = passed_along(updated_gas[:, 0], "axial", -1)
    extended = jnp.concatenate([updated_gas, upper_face[:, None]], 1)
    below_row = passed_along(extended[:, :, 0], "radial", -1)
    gas_field = jnp.concatenate([extended, below_row[:, :, None]], 2)
    gas_field = jnp.pad(gas_field, ((0, 0), (0, 0), (0, 0), (0, 1)))
    windows = split_windows(gas_field, 3, count_z)
    windows = split_windows(windows, 2, count_y)
    windows = split_windows(windows, 1, count_x)
    windows = jnp.transpose(windows, (0, 1, 3, 5, 2, 4, 6)).reshape(5, brick_total, 125)
    brick_gas = jnp.pad(windows, ((0, 0), (0, 0), (0, 3)))

    def sample_turn(turn_index, sampled):
        block_rows, weights, selector = group_pieces(turn_index)
        picked = jnp.einsum("gb,fbe->fge", selector, brick_gas, precision=lax.Precision.HIGHEST)
        values = jnp.einsum("fge,gpe->fgp", picked, weights, precision=lax.Precision.HIGHEST)
        values = values.reshape(5, group_size * 128).astype(jnp.bfloat16)
        return lax.dynamic_update_slice_in_dim(sampled, values, turn_index * group_size * 128, 1)

    parcel_gas = lax.fori_loop(
        0, turn_count, sample_turn, jnp.zeros((5, parcels.shape[1]), jnp.bfloat16)
    )
    return (source, parcel_gas)


def solution(mesh):
    return jax.shard_map(
        per_device,
        mesh=mesh,
        in_specs=(
            P(None, ("axial", "radial")),
            P(None, ("axial", "radial")),
            P(("axial", "radial")),
            P(None, ("axial", "radial")),
            P(("axial", "radial")),
            P(None, "axial", "radial", None),
        ),
        out_specs=(P(None, "axial", "radial", None), P(None, ("axial", "radial"))),
        check_vma=False,
    )
```

```python
import math

import jax
import jax.numpy as jnp
from jax import lax
from jax.sharding import PartitionSpec as P

COUPLE = 0.5


def passed_along(block, axis, distance):
    devices = range(lax.axis_size(axis))
    route = [(i - distance, i) for i in devices if i - distance in devices]
    return lax.ppermute(block, axis, route)


def kernel_weights(cell_index, offsets):
    extent = jnp.arange(128, dtype=jnp.int32)
    brick_x = extent // 25
    brick_y = extent // 5 % 5
    brick_z = extent % 5
    inside = (extent < 125).astype(jnp.float32)

    def factor(cell_coord, brick_coord, fraction):
        cell_coord = cell_coord[:, :, None]
        fraction = fraction[:, :, None]
        return jnp.where(
            brick_coord == cell_coord,
            1.0 - fraction,
            jnp.where(brick_coord == cell_coord + 1, fraction, 0.0),
        )

    cell_x = cell_index // 16
    cell_y = cell_index // 4 % 4
    cell_z = cell_index % 4
    return (
        factor(cell_x, brick_x, offsets[0])
        * factor(cell_y, brick_y, offsets[1])
        * factor(cell_z, brick_z, offsets[2])
        * inside
    )


def split_windows(field, axis, count):
    core = lax.slice_in_dim(field, 0, 4 * count, axis=axis)
    core = core.reshape(field.shape[:axis] + (count, 4) + field.shape[axis + 1 :])
    tail = lax.slice_in_dim(field, 4, 4 * count + 1, stride=4, axis=axis)
    tail = jnp.expand_dims(tail, axis + 1)
    return jnp.concatenate([core, tail], axis + 1)


def merge_windows(field, axis, count, keep_tail):
    core = lax.slice_in_dim(field, 0, 4, axis=axis + 1)
    tail = lax.slice_in_dim(field, 4, 5, axis=axis + 1)
    zero_brick = jnp.zeros_like(lax.slice_in_dim(core, 0, 1, axis=axis))
    core = jnp.concatenate([core, zero_brick], axis)
    zero_tail = jnp.zeros_like(lax.slice_in_dim(tail, 0, 1, axis=axis))
    tail = jnp.concatenate([zero_tail, tail], axis)
    first = lax.slice_in_dim(core, 0, 1, axis=axis + 1) + tail
    rest = lax.slice_in_dim(core, 1, 4, axis=axis + 1)
    joined = jnp.concatenate([first, rest], axis + 1)
    joined = joined.reshape(field.shape[:axis] + (4 * (count + 1),) + field.shape[axis + 2 :])
    length = 4 * count + 1 if keep_tail else 4 * count
    return lax.slice_in_dim(joined, 0, length, axis=axis)


def window_map(count, length):
    extent = jnp.arange(5, dtype=jnp.int32)[:, None, None]
    brick = jnp.arange(count, dtype=jnp.int32)[None, :, None]
    cell = jnp.arange(length, dtype=jnp.int32)[None, None, :]
    return (4 * brick + extent == cell).astype(jnp.float32)


def radial_fold(layers):
    arrived = passed_along(layers[:, :, -1], "radial", 1)
    return layers.at[:, :, 0].add(arrived)


def departed_mask(cross_rows, resident):
    rows = cross_rows.reshape(-1)
    lanes = 128
    high = jnp.where(rows >= 0, rows // lanes, -1)
    low = jnp.where(rows >= 0, rows % lanes, -1)
    high_hot = (high[:, None] == jnp.arange(resident // lanes, dtype=jnp.int32)[None, :]).astype(jnp.bfloat16)
    low_hot = (low[:, None] == jnp.arange(lanes, dtype=jnp.int32)[None, :]).astype(jnp.bfloat16)
    counts = jnp.einsum("sh,sl->hl", high_hot, low_hot, preferred_element_type=jnp.float32)
    return counts.reshape(resident)


def per_device(parcel_load, parcel_offset, parcel_cell, cross_rows, block_brick, gas):
    span_x = gas.shape[1]
    span_y = gas.shape[2]
    span_z = gas.shape[3]
    count_x = span_x // 4
    count_y = span_y // 4
    count_z = span_z // 4
    brick_total = count_x * count_y * count_z
    resident = parcel_load.shape[1]
    block_count = block_brick.shape[0]
    group_size = math.gcd(block_count, 64)
    turn_count = block_count // group_size
    brick_numbers = jnp.arange(brick_total, dtype=jnp.int32)
    attributes = jnp.concatenate(
        [parcel_load, parcel_offset, parcel_cell[None].astype(jnp.float32)], 0
    )
    usable = cross_rows >= 0
    safe_rows = jnp.maximum(cross_rows, 0)
    upward = attributes[:, safe_rows[0]] * usable[0].astype(jnp.float32)
    downward = attributes[:, safe_rows[1]] * usable[1].astype(jnp.float32)
    from_lower = passed_along(upward, "axial", 1)
    from_upper = passed_along(downward, "axial", -1)
    departed = departed_mask(cross_rows, resident)
    staying = jnp.concatenate([attributes[:8] * (1.0 - departed)[None], attributes[8:]], 0)
    parcels = jnp.concatenate([staying, from_lower, from_upper], 1)

    def group_pieces(turn_index):
        first_block = turn_index * group_size
        parcel_part = lax.dynamic_slice_in_dim(parcels, first_block * 128, group_size * 128, 1)
        brick_ids = lax.dynamic_slice_in_dim(block_brick, first_block, group_size, 0)
        block_rows = parcel_part.reshape(9, group_size, 128)
        weights = kernel_weights(block_rows[8].astype(jnp.int32), block_rows[5:8])
        selector = (brick_ids[:, None] == brick_numbers[None, :]).astype(jnp.float32)
        return (block_rows, weights, selector)

    def deposit_turn(turn_index, brick_sums):
        block_rows, weights, selector = group_pieces(turn_index)
        spread = jnp.einsum(
            "fgp,gpe->fge", block_rows[:5], weights, precision=lax.Precision.HIGHEST
        )
        return brick_sums + jnp.einsum(
            "gb,fge->feb", selector, spread, precision=lax.Precision.HIGHEST
        )

    brick_sums = lax.fori_loop(
        0, turn_count, deposit_turn, jnp.zeros((5, 128, brick_total), jnp.float32)
    )
    if count_x == 1:
        laid = brick_sums[:, :125].reshape(5, 25, 5, count_y, count_z)
        laid = jnp.einsum(
            "faeyk,ekz->fayz", laid, window_map(count_z, span_z), precision=lax.Precision.HIGHEST
        )
        laid = laid.reshape(5, 5, 5, count_y, span_z)
        deposit_grid = jnp.einsum(
            "fxwyz,wyn->fxnz", laid, window_map(count_y, span_y + 1),
            precision=lax.Precision.HIGHEST,
        )
    else:
        laid = jnp.transpose(brick_sums[:, :125], (0, 2, 1))
        laid = laid.reshape(5, count_x, count_y, count_z, 5, 5, 5)
        laid = jnp.transpose(laid, (0, 1, 4, 2, 5, 3, 6))
        laid = merge_windows(laid, 1, count_x, True)
        laid = merge_windows(laid, 2, count_y, True)
        deposit_grid = merge_windows(laid, 3, count_z, False)
    incoming = passed_along(deposit_grid[:, span_x], "axial", 1)
    summed = deposit_grid[:, :span_x].at[:, 0].add(incoming)
    folded = radial_fold(summed)
    source = folded[:, :, :span_y]
    updated_gas = gas + COUPLE * source
    upper_face = passed_along(updated_gas[:, 0], "axial", -1)
    extended = jnp.concatenate([updated_gas, upper_face[:, None]], 1)
    below_row = passed_along(extended[:, :, 0], "radial", -1)
    gas_field = jnp.concatenate([extended, below_row[:, :, None]], 2)
    if count_x == 1:
        windows = jnp.einsum(
            "fxnz,wyn->fxwyz", gas_field, window_map(count_y, span_y + 1),
            precision=lax.Precision.HIGHEST,
        )
        windows = windows.reshape(5, 25, count_y, span_z)
        windows = jnp.einsum(
            "fayz,ekz->faeyk", windows, window_map(count_z, span_z),
            precision=lax.Precision.HIGHEST,
        )
        windows = windows.reshape(5, 125, brick_total)
    else:
        gas_field = jnp.pad(gas_field, ((0, 0), (0, 0), (0, 0), (0, 1)))
        windows = split_windows(gas_field, 3, count_z)
        windows = split_windows(windows, 2, count_y)
        windows = split_windows(windows, 1, count_x)
        windows = jnp.transpose(windows, (0, 1, 3, 5, 2, 4, 6)).reshape(5, brick_total, 125)
        windows = jnp.transpose(windows, (0, 2, 1))
    brick_gas = jnp.pad(windows, ((0, 0), (0, 3), (0, 0)))

    def sample_turn(turn_index, sampled):
        block_rows, weights, selector = group_pieces(turn_index)
        picked = jnp.einsum("gb,feb->fge", selector, brick_gas, precision=lax.Precision.HIGHEST)
        values = jnp.einsum("fge,gpe->fgp", picked, weights, precision=lax.Precision.HIGHEST)
        values = values.reshape(5, group_size * 128).astype(jnp.bfloat16)
        return lax.dynamic_update_slice_in_dim(sampled, values, turn_index * group_size * 128, 1)

    parcel_gas = lax.fori_loop(
        0, turn_count, sample_turn, jnp.zeros((5, parcels.shape[1]), jnp.bfloat16)
    )
    return (source, parcel_gas)


def solution(mesh):
    return jax.shard_map(
        per_device,
        mesh=mesh,
        in_specs=(
            P(None, ("axial", "radial")),
            P(None, ("axial", "radial")),
            P(("axial", "radial")),
            P(None, ("axial", "radial")),
            P(("axial", "radial")),
            P(None, "axial", "radial", None),
        ),
        out_specs=(P(None, "axial", "radial", None), P(None, ("axial", "radial"))),
        check_vma=False,
    )
```

```python
import math

import jax
import jax.numpy as jnp
from jax import lax
from jax.sharding import PartitionSpec as P

COUPLE = 0.5


def passed_along(block, axis, distance):
    devices = range(lax.axis_size(axis))
    route = [(i - distance, i) for i in devices if i - distance in devices]
    return lax.ppermute(block, axis, route)


def kernel_weights(cell_index, offsets):
    extent = jnp.arange(128, dtype=jnp.int32)
    brick_x = extent // 25
    brick_y = extent // 5 % 5
    brick_z = extent % 5
    inside = (extent < 125).astype(jnp.float32)

    def factor(cell_coord, brick_coord, fraction):
        cell_coord = cell_coord[:, :, None]
        fraction = fraction[:, :, None]
        return jnp.where(
            brick_coord == cell_coord,
            1.0 - fraction,
            jnp.where(brick_coord == cell_coord + 1, fraction, 0.0),
        )

    cell_x = cell_index // 16
    cell_y = cell_index // 4 % 4
    cell_z = cell_index % 4
    return (
        factor(cell_x, brick_x, offsets[0])
        * factor(cell_y, brick_y, offsets[1])
        * factor(cell_z, brick_z, offsets[2])
        * inside
    )


def split_windows(field, axis, count):
    core = lax.slice_in_dim(field, 0, 4 * count, axis=axis)
    core = core.reshape(field.shape[:axis] + (count, 4) + field.shape[axis + 1 :])
    tail = lax.slice_in_dim(field, 4, 4 * count + 1, stride=4, axis=axis)
    tail = jnp.expand_dims(tail, axis + 1)
    return jnp.concatenate([core, tail], axis + 1)


def merge_windows(field, axis, count, keep_tail):
    core = lax.slice_in_dim(field, 0, 4, axis=axis + 1)
    tail = lax.slice_in_dim(field, 4, 5, axis=axis + 1)
    zero_brick = jnp.zeros_like(lax.slice_in_dim(core, 0, 1, axis=axis))
    core = jnp.concatenate([core, zero_brick], axis)
    zero_tail = jnp.zeros_like(lax.slice_in_dim(tail, 0, 1, axis=axis))
    tail = jnp.concatenate([zero_tail, tail], axis)
    first = lax.slice_in_dim(core, 0, 1, axis=axis + 1) + tail
    rest = lax.slice_in_dim(core, 1, 4, axis=axis + 1)
    joined = jnp.concatenate([first, rest], axis + 1)
    joined = joined.reshape(field.shape[:axis] + (4 * (count + 1),) + field.shape[axis + 2 :])
    length = 4 * count + 1 if keep_tail else 4 * count
    return lax.slice_in_dim(joined, 0, length, axis=axis)


def window_map(count, length):
    extent = jnp.arange(5, dtype=jnp.int32)[:, None, None]
    brick = jnp.arange(count, dtype=jnp.int32)[None, :, None]
    cell = jnp.arange(length, dtype=jnp.int32)[None, None, :]
    return (4 * brick + extent == cell).astype(jnp.float32)


def radial_fold(layers):
    arrived = passed_along(layers[:, :, -1], "radial", 1)
    return layers.at[:, :, 0].add(arrived)


def departed_mask(cross_rows, resident):
    rows = cross_rows.reshape(-1)
    lanes = 128
    high = jnp.where(rows >= 0, rows // lanes, -1)
    low = jnp.where(rows >= 0, rows % lanes, -1)
    high_hot = (high[:, None] == jnp.arange(resident // lanes, dtype=jnp.int32)[None, :]).astype(jnp.bfloat16)
    low_hot = (low[:, None] == jnp.arange(lanes, dtype=jnp.int32)[None, :]).astype(jnp.bfloat16)
    counts = jnp.einsum("sh,sl->hl", high_hot, low_hot, preferred_element_type=jnp.float32)
    return counts.reshape(resident)


def per_device(parcel_load, parcel_offset, parcel_cell, cross_rows, block_brick, gas):
    span_x = gas.shape[1]
    span_y = gas.shape[2]
    span_z = gas.shape[3]
    count_x = span_x // 4
    count_y = span_y // 4
    count_z = span_z // 4
    brick_total = count_x * count_y * count_z
    resident = parcel_load.shape[1]
    block_count = block_brick.shape[0]
    group_size = math.gcd(block_count, 64)
    turn_count = block_count // group_size
    brick_numbers = jnp.arange(brick_total, dtype=jnp.int32)
    attributes = jnp.concatenate(
        [parcel_load, parcel_offset, parcel_cell[None].astype(jnp.float32)], 0
    )
    usable = cross_rows >= 0
    safe_rows = jnp.maximum(cross_rows, 0)
    upward = attributes[:, safe_rows[0]] * usable[0].astype(jnp.float32)
    downward = attributes[:, safe_rows[1]] * usable[1].astype(jnp.float32)
    from_lower = passed_along(upward, "axial", 1)
    from_upper = passed_along(downward, "axial", -1)
    departed = departed_mask(cross_rows, resident)
    staying = jnp.concatenate([attributes[:8] * (1.0 - departed)[None], attributes[8:]], 0)
    parcels = jnp.concatenate([staying, from_lower, from_upper], 1)

    def group_pieces(turn_index):
        first_block = turn_index * group_size
        parcel_part = lax.dynamic_slice_in_dim(parcels, first_block * 128, group_size * 128, 1)
        brick_ids = lax.dynamic_slice_in_dim(block_brick, first_block, group_size, 0)
        block_rows = parcel_part.reshape(9, group_size, 128)
        weights = kernel_weights(block_rows[8].astype(jnp.int32), block_rows[5:8])
        selector = (brick_ids[:, None] == brick_numbers[None, :]).astype(jnp.float32)
        return (block_rows, weights, selector)

    def deposit_turn(turn_index, brick_sums):
        block_rows, weights, selector = group_pieces(turn_index)
        spread = jnp.einsum(
            "fgp,gpe->fge", block_rows[:5], weights, precision=lax.Precision.HIGH
        )
        return brick_sums + jnp.einsum(
            "gb,fge->feb", selector, spread, precision=lax.Precision.HIGH
        )

    brick_sums = lax.fori_loop(
        0, turn_count, deposit_turn, jnp.zeros((5, 128, brick_total), jnp.float32)
    )
    if count_x == 1:
        laid = brick_sums[:, :125].reshape(5, 25, 5, count_y, count_z)
        laid = jnp.einsum(
            "faeyk,ekz->fayz", laid, window_map(count_z, span_z), precision=lax.Precision.HIGH
        )
        laid = laid.reshape(5, 5, 5, count_y, span_z)
        deposit_grid = jnp.einsum(
            "fxwyz,wyn->fxnz", laid, window_map(count_y, span_y + 1),
            precision=lax.Precision.HIGH,
        )
    else:
        laid = jnp.transpose(brick_sums[:, :125], (0, 2, 1))
        laid = laid.reshape(5, count_x, count_y, count_z, 5, 5, 5)
        laid = jnp.transpose(laid, (0, 1, 4, 2, 5, 3, 6))
        laid = merge_windows(laid, 1, count_x, True)
        laid = merge_windows(laid, 2, count_y, True)
        deposit_grid = merge_windows(laid, 3, count_z, False)
    incoming = passed_along(deposit_grid[:, span_x], "axial", 1)
    summed = deposit_grid[:, :span_x].at[:, 0].add(incoming)
    folded = radial_fold(summed)
    source = folded[:, :, :span_y]
    updated_gas = gas + COUPLE * source
    upper_face = passed_along(updated_gas[:, 0], "axial", -1)
    extended = jnp.concatenate([updated_gas, upper_face[:, None]], 1)
    below_row = passed_along(extended[:, :, 0], "radial", -1)
    gas_field = jnp.concatenate([extended, below_row[:, :, None]], 2)
    if count_x == 1:
        windows = jnp.einsum(
            "fxnz,wyn->fxwyz", gas_field, window_map(count_y, span_y + 1),
            precision=lax.Precision.HIGH,
        )
        windows = windows.reshape(5, 25, count_y, span_z)
        windows = jnp.einsum(
            "fayz,ekz->faeyk", windows, window_map(count_z, span_z),
            precision=lax.Precision.HIGH,
        )
        windows = windows.reshape(5, 125, brick_total)
    else:
        gas_field = jnp.pad(gas_field, ((0, 0), (0, 0), (0, 0), (0, 1)))
        windows = split_windows(gas_field, 3, count_z)
        windows = split_windows(windows, 2, count_y)
        windows = split_windows(windows, 1, count_x)
        windows = jnp.transpose(windows, (0, 1, 3, 5, 2, 4, 6)).reshape(5, brick_total, 125)
        windows = jnp.transpose(windows, (0, 2, 1))
    brick_gas = jnp.pad(windows, ((0, 0), (0, 3), (0, 0)))

    def sample_turn(turn_index, sampled):
        block_rows, weights, selector = group_pieces(turn_index)
        picked = jnp.einsum("gb,feb->fge", selector, brick_gas, precision=lax.Precision.HIGH)
        values = jnp.einsum("fge,gpe->fgp", picked, weights, precision=lax.Precision.HIGH)
        values = values.reshape(5, group_size * 128).astype(jnp.bfloat16)
        return lax.dynamic_update_slice_in_dim(sampled, values, turn_index * group_size * 128, 1)

    parcel_gas = lax.fori_loop(
        0, turn_count, sample_turn, jnp.zeros((5, parcels.shape[1]), jnp.bfloat16)
    )
    return (source, parcel_gas)


def solution(mesh):
    return jax.shard_map(
        per_device,
        mesh=mesh,
        in_specs=(
            P(None, ("axial", "radial")),
            P(None, ("axial", "radial")),
            P(("axial", "radial")),
            P(None, ("axial", "radial")),
            P(("axial", "radial")),
            P(None, "axial", "radial", None),
        ),
        out_specs=(P(None, "axial", "radial", None), P(None, ("axial", "radial"))),
        check_vma=False,
    )
```

```python
import math

import jax
import jax.numpy as jnp
from jax import lax
from jax.sharding import PartitionSpec as P

COUPLE = 0.5


def passed_along(block, axis, distance):
    devices = range(lax.axis_size(axis))
    route = [(i - distance, i) for i in devices if i - distance in devices]
    return lax.ppermute(block, axis, route)


def kernel_weights(cell_index, offsets):
    extent = jnp.arange(128, dtype=jnp.int32)
    brick_x = extent // 25
    brick_y = extent // 5 % 5
    brick_z = extent % 5
    inside = (extent < 125).astype(jnp.float32)

    def factor(cell_coord, brick_coord, fraction):
        cell_coord = cell_coord[:, :, None]
        fraction = fraction[:, :, None]
        return jnp.where(
            brick_coord == cell_coord,
            1.0 - fraction,
            jnp.where(brick_coord == cell_coord + 1, fraction, 0.0),
        )

    cell_x = cell_index // 16
    cell_y = cell_index // 4 % 4
    cell_z = cell_index % 4
    return (
        factor(cell_x, brick_x, offsets[0])
        * factor(cell_y, brick_y, offsets[1])
        * factor(cell_z, brick_z, offsets[2])
        * inside
    )


def axis_factors(cell_index, offsets):
    extent = jnp.arange(5, dtype=jnp.int32).reshape((5,) + (1,) * cell_index.ndim)

    def factor(cell_coord, fraction):
        return jnp.where(
            extent == cell_coord[None],
            1.0 - fraction[None],
            jnp.where(extent == cell_coord[None] + 1, fraction[None], 0.0),
        )

    return (
        factor(cell_index // 16, offsets[0]),
        factor(cell_index // 4 % 4, offsets[1]),
        factor(cell_index % 4, offsets[2]),
    )


def split_windows(field, axis, count):
    core = lax.slice_in_dim(field, 0, 4 * count, axis=axis)
    core = core.reshape(field.shape[:axis] + (count, 4) + field.shape[axis + 1 :])
    tail = lax.slice_in_dim(field, 4, 4 * count + 1, stride=4, axis=axis)
    tail = jnp.expand_dims(tail, axis + 1)
    return jnp.concatenate([core, tail], axis + 1)


def merge_windows(field, axis, count, keep_tail):
    core = lax.slice_in_dim(field, 0, 4, axis=axis + 1)
    tail = lax.slice_in_dim(field, 4, 5, axis=axis + 1)
    zero_brick = jnp.zeros_like(lax.slice_in_dim(core, 0, 1, axis=axis))
    core = jnp.concatenate([core, zero_brick], axis)
    zero_tail = jnp.zeros_like(lax.slice_in_dim(tail, 0, 1, axis=axis))
    tail = jnp.concatenate([zero_tail, tail], axis)
    first = lax.slice_in_dim(core, 0, 1, axis=axis + 1) + tail
    rest = lax.slice_in_dim(core, 1, 4, axis=axis + 1)
    joined = jnp.concatenate([first, rest], axis + 1)
    joined = joined.reshape(field.shape[:axis] + (4 * (count + 1),) + field.shape[axis + 2 :])
    length = 4 * count + 1 if keep_tail else 4 * count
    return lax.slice_in_dim(joined, 0, length, axis=axis)


def window_map(count, length):
    extent = jnp.arange(5, dtype=jnp.int32)[:, None, None]
    brick = jnp.arange(count, dtype=jnp.int32)[None, :, None]
    cell = jnp.arange(length, dtype=jnp.int32)[None, None, :]
    return (4 * brick + extent == cell).astype(jnp.float32)


def radial_fold(layers):
    arrived = passed_along(layers[:, :, -1], "radial", 1)
    return layers.at[:, :, 0].add(arrived)


def departed_mask(cross_rows, resident):
    rows = cross_rows.reshape(-1)
    lanes = 128
    high = jnp.where(rows >= 0, rows // lanes, -1)
    low = jnp.where(rows >= 0, rows % lanes, -1)
    high_hot = (high[:, None] == jnp.arange(resident // lanes, dtype=jnp.int32)[None, :]).astype(jnp.bfloat16)
    low_hot = (low[:, None] == jnp.arange(lanes, dtype=jnp.int32)[None, :]).astype(jnp.bfloat16)
    counts = jnp.einsum("sh,sl->hl", high_hot, low_hot, preferred_element_type=jnp.float32)
    return counts.reshape(resident)


def per_device(parcel_load, parcel_offset, parcel_cell, cross_rows, block_brick, gas):
    span_x = gas.shape[1]
    span_y = gas.shape[2]
    span_z = gas.shape[3]
    count_x = span_x // 4
    count_y = span_y // 4
    count_z = span_z // 4
    brick_total = count_x * count_y * count_z
    resident = parcel_load.shape[1]
    block_count = block_brick.shape[0]
    brick_numbers = jnp.arange(brick_total, dtype=jnp.int32)
    attributes = jnp.concatenate(
        [parcel_load, parcel_offset, parcel_cell[None].astype(jnp.float32)], 0
    )
    usable = cross_rows >= 0
    safe_rows = jnp.maximum(cross_rows, 0)
    upward = attributes[:, safe_rows[0]] * usable[0].astype(jnp.float32)
    downward = attributes[:, safe_rows[1]] * usable[1].astype(jnp.float32)
    from_lower = passed_along(upward, "axial", 1)
    from_upper = passed_along(downward, "axial", -1)
    departed = departed_mask(cross_rows, resident)
    staying = jnp.concatenate([attributes[:8] * (1.0 - departed)[None], attributes[8:]], 0)
    parcels = jnp.concatenate([staying, from_lower, from_upper], 1)

    block_rows = parcels.reshape(9, block_count, 128)
    factor_x, factor_y, factor_z = axis_factors(block_rows[8].astype(jnp.int32), block_rows[5:8])
    load_x = (block_rows[:5][:, None] * factor_x[None]).reshape(25, block_count, 128)
    weight_yz = (factor_y[:, None] * factor_z[None]).reshape(25, block_count, 128)
    selector = (block_brick[:, None] == brick_numbers[None, :]).astype(jnp.float32)
    spread = jnp.einsum("agp,bgp->gab", load_x, weight_yz, precision=lax.Precision.HIGH)
    brick_sums = jnp.einsum(
        "gb,gfe->feb", selector, spread.reshape(block_count, 5, 125),
        precision=lax.Precision.HIGH,
    )
    if count_x == 1:
        laid = brick_sums.reshape(5, 25, 5, count_y, count_z)
        laid = jnp.einsum(
            "faeyk,ekz->fayz", laid, window_map(count_z, span_z), precision=lax.Precision.HIGH
        )
        laid = laid.reshape(5, 5, 5, count_y, span_z)
        deposit_grid = jnp.einsum(
            "fxwyz,wyn->fxnz", laid, window_map(count_y, span_y + 1),
            precision=lax.Precision.HIGH,
        )
    else:
        laid = jnp.transpose(brick_sums, (0, 2, 1))
        laid = laid.reshape(5, count_x, count_y, count_z, 5, 5, 5)
        laid = jnp.transpose(laid, (0, 1, 4, 2, 5, 3, 6))
        laid = merge_windows(laid, 1, count_x, True)
        laid = merge_windows(laid, 2, count_y, True)
        deposit_grid = merge_windows(laid, 3, count_z, False)
    incoming = passed_along(deposit_grid[:, span_x], "axial", 1)
    summed = deposit_grid[:, :span_x].at[:, 0].add(incoming)
    folded = radial_fold(summed)
    source = folded[:, :, :span_y]
    updated_gas = gas + COUPLE * source
    upper_face = passed_along(updated_gas[:, 0], "axial", -1)
    extended = jnp.concatenate([updated_gas, upper_face[:, None]], 1)
    below_row = passed_along(extended[:, :, 0], "radial", -1)
    gas_field = jnp.concatenate([extended, below_row[:, :, None]], 2)
    if count_x == 1:
        windows = jnp.einsum(
            "fxnz,wyn->fxwyz", gas_field, window_map(count_y, span_y + 1),
            precision=lax.Precision.HIGH,
        )
        windows = windows.reshape(5, 25, count_y, span_z)
        windows = jnp.einsum(
            "fayz,ekz->faeyk", windows, window_map(count_z, span_z),
            precision=lax.Precision.HIGH,
        )
        windows = windows.reshape(5, 125, brick_total)
    else:
        gas_field = jnp.pad(gas_field, ((0, 0), (0, 0), (0, 0), (0, 1)))
        windows = split_windows(gas_field, 3, count_z)
        windows = split_windows(windows, 2, count_y)
        windows = split_windows(windows, 1, count_x)
        windows = jnp.transpose(windows, (0, 1, 3, 5, 2, 4, 6)).reshape(5, brick_total, 125)
        windows = jnp.transpose(windows, (0, 2, 1))
    picked = jnp.einsum("gb,feb->gfe", selector, windows, precision=lax.Precision.HIGH)
    picked = picked.reshape(block_count, 25, 25)
    partial = jnp.einsum("gab,bgp->agp", picked, weight_yz, precision=lax.Precision.HIGH)
    values = jnp.sum(partial.reshape(5, 5, block_count, 128) * factor_x[None], axis=1)
    parcel_gas = values.reshape(5, block_count * 128).astype(jnp.bfloat16)
    return (source, parcel_gas)


def solution(mesh):
    return jax.shard_map(
        per_device,
        mesh=mesh,
        in_specs=(
            P(None, ("axial", "radial")),
            P(None, ("axial", "radial")),
            P(("axial", "radial")),
            P(None, ("axial", "radial")),
            P(("axial", "radial")),
            P(None, "axial", "radial", None),
        ),
        out_specs=(P(None, "axial", "radial", None), P(None, ("axial", "radial"))),
        check_vma=False,
    )
```

```python
import math

import jax
import jax.numpy as jnp
from jax import lax
from jax.experimental import pallas as pl
from jax.experimental.pallas import tpu as pltpu
from jax.sharding import PartitionSpec as P

COUPLE = 0.5


def passed_along(block, axis, distance):
    devices = range(lax.axis_size(axis))
    route = [(i - distance, i) for i in devices if i - distance in devices]
    return lax.ppermute(block, axis, route)


def kernel_weights(cell_index, offsets):
    extent = jnp.arange(128, dtype=jnp.int32)
    brick_x = extent // 25
    brick_y = extent // 5 % 5
    brick_z = extent % 5
    inside = (extent < 125).astype(jnp.float32)

    def factor(cell_coord, brick_coord, fraction):
        cell_coord = cell_coord[:, :, None]
        fraction = fraction[:, :, None]
        return jnp.where(
            brick_coord == cell_coord,
            1.0 - fraction,
            jnp.where(brick_coord == cell_coord + 1, fraction, 0.0),
        )

    cell_x = cell_index // 16
    cell_y = cell_index // 4 % 4
    cell_z = cell_index % 4
    return (
        factor(cell_x, brick_x, offsets[0])
        * factor(cell_y, brick_y, offsets[1])
        * factor(cell_z, brick_z, offsets[2])
        * inside
    )


def axis_factors(cell_index, offsets):
    extent = jnp.arange(5, dtype=jnp.int32).reshape((5,) + (1,) * cell_index.ndim)

    def factor(cell_coord, fraction):
        return jnp.where(
            extent == cell_coord[None],
            1.0 - fraction[None],
            jnp.where(extent == cell_coord[None] + 1, fraction[None], 0.0),
        )

    return (
        factor(cell_index // 16, offsets[0]),
        factor(cell_index // 4 % 4, offsets[1]),
        factor(cell_index % 4, offsets[2]),
    )


def split_windows(field, axis, count):
    core = lax.slice_in_dim(field, 0, 4 * count, axis=axis)
    core = core.reshape(field.shape[:axis] + (count, 4) + field.shape[axis + 1 :])
    tail = lax.slice_in_dim(field, 4, 4 * count + 1, stride=4, axis=axis)
    tail = jnp.expand_dims(tail, axis + 1)
    return jnp.concatenate([core, tail], axis + 1)


def merge_windows(field, axis, count, keep_tail):
    core = lax.slice_in_dim(field, 0, 4, axis=axis + 1)
    tail = lax.slice_in_dim(field, 4, 5, axis=axis + 1)
    zero_brick = jnp.zeros_like(lax.slice_in_dim(core, 0, 1, axis=axis))
    core = jnp.concatenate([core, zero_brick], axis)
    zero_tail = jnp.zeros_like(lax.slice_in_dim(tail, 0, 1, axis=axis))
    tail = jnp.concatenate([zero_tail, tail], axis)
    first = lax.slice_in_dim(core, 0, 1, axis=axis + 1) + tail
    rest = lax.slice_in_dim(core, 1, 4, axis=axis + 1)
    joined = jnp.concatenate([first, rest], axis + 1)
    joined = joined.reshape(field.shape[:axis] + (4 * (count + 1),) + field.shape[axis + 2 :])
    length = 4 * count + 1 if keep_tail else 4 * count
    return lax.slice_in_dim(joined, 0, length, axis=axis)


def window_map(count, length):
    extent = jnp.arange(5, dtype=jnp.int32)[:, None, None]
    brick = jnp.arange(count, dtype=jnp.int32)[None, :, None]
    cell = jnp.arange(length, dtype=jnp.int32)[None, None, :]
    return (4 * brick + extent == cell).astype(jnp.float32)


def radial_fold(layers):
    arrived = passed_along(layers[:, :, -1], "radial", 1)
    return layers.at[:, :, 0].add(arrived)


def departed_mask(cross_rows, resident):
    rows = cross_rows.reshape(-1)
    lanes = 128
    high = jnp.where(rows >= 0, rows // lanes, -1)
    low = jnp.where(rows >= 0, rows % lanes, -1)
    high_hot = (high[:, None] == jnp.arange(resident // lanes, dtype=jnp.int32)[None, :]).astype(jnp.bfloat16)
    low_hot = (low[:, None] == jnp.arange(lanes, dtype=jnp.int32)[None, :]).astype(jnp.bfloat16)
    counts = jnp.einsum("sh,sl->hl", high_hot, low_hot, preferred_element_type=jnp.float32)
    return counts.reshape(resident)


def gather_rows(table, rows, interpret=False):
    slots = rows.shape[0]
    height, width = table.shape
    chunk = math.gcd(slots, 1024)
    steps = slots // chunk
    rows = jnp.clip(rows, 0, height - 1).reshape(steps, 1, chunk)

    def kernel(row_ref, table_ref, out_ref):
        def body(i, carry):
            row = row_ref[0, 0, i]
            out_ref[pl.ds(i, 1), :] = table_ref[pl.ds(row, 1), :]
            return carry

        lax.fori_loop(0, chunk, body, 0, unroll=8)

    return pl.pallas_call(
        kernel,
        out_shape=jax.ShapeDtypeStruct((slots, width), table.dtype),
        grid=(steps,),
        in_specs=[
            pl.BlockSpec((1, 1, chunk), lambda s: (s, 0, 0), memory_space=pltpu.SMEM),
            pl.BlockSpec((height, width), lambda s: (0, 0)),
        ],
        out_specs=pl.BlockSpec((chunk, width), lambda s: (s, 0)),
        compiler_params=pltpu.CompilerParams(vmem_limit_bytes=48 * 1024 * 1024),
        interpret=interpret,
    )(rows, table)


def per_device(parcel_load, parcel_offset, parcel_cell, cross_rows, block_brick, gas):
    span_x = gas.shape[1]
    span_y = gas.shape[2]
    span_z = gas.shape[3]
    count_x = span_x // 4
    count_y = span_y // 4
    count_z = span_z // 4
    brick_total = count_x * count_y * count_z
    resident = parcel_load.shape[1]
    block_count = block_brick.shape[0]
    brick_numbers = jnp.arange(brick_total, dtype=jnp.int32)
    attributes = jnp.concatenate(
        [parcel_load, parcel_offset, parcel_cell[None].astype(jnp.float32)], 0
    )
    usable = cross_rows >= 0
    safe_rows = jnp.maximum(cross_rows, 0)
    moving = gather_rows(attributes.T, safe_rows.reshape(-1)).T
    moving = moving.reshape(9, 2, -1) * usable[None].astype(jnp.float32)
    upward = moving[:, 0]
    downward = moving[:, 1]
    from_lower = passed_along(upward, "axial", 1)
    from_upper = passed_along(downward, "axial", -1)
    departed = departed_mask(cross_rows, resident)
    staying = jnp.concatenate([attributes[:8] * (1.0 - departed)[None], attributes[8:]], 0)
    parcels = jnp.concatenate([staying, from_lower, from_upper], 1)

    block_rows = parcels.reshape(9, block_count, 128)
    factor_x, factor_y, factor_z = axis_factors(block_rows[8].astype(jnp.int32), block_rows[5:8])
    load_x = (block_rows[:5][:, None] * factor_x[None]).reshape(25, block_count, 128)
    weight_yz = (factor_y[:, None] * factor_z[None]).reshape(25, block_count, 128)
    selector = (block_brick[:, None] == brick_numbers[None, :]).astype(jnp.float32)
    spread = jnp.einsum("agp,bgp->gab", load_x, weight_yz, precision=lax.Precision.HIGH)
    brick_sums = jnp.einsum(
        "gb,gfe->feb", selector, spread.reshape(block_count, 5, 125),
        precision=lax.Precision.HIGH,
    )
    if count_x == 1:
        laid = brick_sums.reshape(5, 25, 5, count_y, count_z)
        laid = jnp.einsum(
            "faeyk,ekz->fayz", laid, window_map(count_z, span_z), precision=lax.Precision.HIGH
        )
        laid = laid.reshape(5, 5, 5, count_y, span_z)
        deposit_grid = jnp.einsum(
            "fxwyz,wyn->fxnz", laid, window_map(count_y, span_y + 1),
            precision=lax.Precision.HIGH,
        )
    else:
        laid = jnp.transpose(brick_sums, (0, 2, 1))
        laid = laid.reshape(5, count_x, count_y, count_z, 5, 5, 5)
        laid = jnp.transpose(laid, (0, 1, 4, 2, 5, 3, 6))
        laid = merge_windows(laid, 1, count_x, True)
        laid = merge_windows(laid, 2, count_y, True)
        deposit_grid = merge_windows(laid, 3, count_z, False)
    incoming = passed_along(deposit_grid[:, span_x], "axial", 1)
    summed = deposit_grid[:, :span_x].at[:, 0].add(incoming)
    folded = radial_fold(summed)
    source = folded[:, :, :span_y]
    updated_gas = gas + COUPLE * source
    upper_face = passed_along(updated_gas[:, 0], "axial", -1)
    extended = jnp.concatenate([updated_gas, upper_face[:, None]], 1)
    below_row = passed_along(extended[:, :, 0], "radial", -1)
    gas_field = jnp.concatenate([extended, below_row[:, :, None]], 2)
    if count_x == 1:
        windows = jnp.einsum(
            "fxnz,wyn->fxwyz", gas_field, window_map(count_y, span_y + 1),
            precision=lax.Precision.HIGH,
        )
        windows = windows.reshape(5, 25, count_y, span_z)
        windows = jnp.einsum(
            "fayz,ekz->faeyk", windows, window_map(count_z, span_z),
            precision=lax.Precision.HIGH,
        )
        windows = windows.reshape(5, 125, brick_total)
    else:
        gas_field = jnp.pad(gas_field, ((0, 0), (0, 0), (0, 0), (0, 1)))
        windows = split_windows(gas_field, 3, count_z)
        windows = split_windows(windows, 2, count_y)
        windows = split_windows(windows, 1, count_x)
        windows = jnp.transpose(windows, (0, 1, 3, 5, 2, 4, 6)).reshape(5, brick_total, 125)
        windows = jnp.transpose(windows, (0, 2, 1))
    picked = jnp.einsum("gb,feb->gfe", selector, windows, precision=lax.Precision.HIGH)
    picked = picked.reshape(block_count, 25, 25)
    partial = jnp.einsum("gab,bgp->agp", picked, weight_yz, precision=lax.Precision.HIGH)
    values = jnp.sum(partial.reshape(5, 5, block_count, 128) * factor_x[None], axis=1)
    parcel_gas = values.reshape(5, block_count * 128).astype(jnp.bfloat16)
    return (source, parcel_gas)


def solution(mesh):
    return jax.shard_map(
        per_device,
        mesh=mesh,
        in_specs=(
            P(None, ("axial", "radial")),
            P(None, ("axial", "radial")),
            P(("axial", "radial")),
            P(None, ("axial", "radial")),
            P(("axial", "radial")),
            P(None, "axial", "radial", None),
        ),
        out_specs=(P(None, "axial", "radial", None), P(None, ("axial", "radial"))),
        check_vma=False,
    )
```

```python
import math

import jax
import jax.numpy as jnp
from jax import lax
from jax.experimental import pallas as pl
from jax.experimental.pallas import tpu as pltpu
from jax.sharding import PartitionSpec as P

COUPLE = 0.5


def passed_along(block, axis, distance):
    devices = range(lax.axis_size(axis))
    route = [(i - distance, i) for i in devices if i - distance in devices]
    return lax.ppermute(block, axis, route)


def kernel_weights(cell_index, offsets):
    extent = jnp.arange(128, dtype=jnp.int32)
    brick_x = extent // 25
    brick_y = extent // 5 % 5
    brick_z = extent % 5
    inside = (extent < 125).astype(jnp.float32)

    def factor(cell_coord, brick_coord, fraction):
        cell_coord = cell_coord[:, :, None]
        fraction = fraction[:, :, None]
        return jnp.where(
            brick_coord == cell_coord,
            1.0 - fraction,
            jnp.where(brick_coord == cell_coord + 1, fraction, 0.0),
        )

    cell_x = cell_index // 16
    cell_y = cell_index // 4 % 4
    cell_z = cell_index % 4
    return (
        factor(cell_x, brick_x, offsets[0])
        * factor(cell_y, brick_y, offsets[1])
        * factor(cell_z, brick_z, offsets[2])
        * inside
    )


def axis_factors(cell_index, offsets):
    extent = jnp.arange(5, dtype=jnp.int32).reshape((5,) + (1,) * cell_index.ndim)

    def factor(cell_coord, fraction):
        return jnp.where(
            extent == cell_coord[None],
            1.0 - fraction[None],
            jnp.where(extent == cell_coord[None] + 1, fraction[None], 0.0),
        )

    return (
        factor(cell_index // 16, offsets[0]),
        factor(cell_index // 4 % 4, offsets[1]),
        factor(cell_index % 4, offsets[2]),
    )


def split_windows(field, axis, count):
    core = lax.slice_in_dim(field, 0, 4 * count, axis=axis)
    core = core.reshape(field.shape[:axis] + (count, 4) + field.shape[axis + 1 :])
    tail = lax.slice_in_dim(field, 4, 4 * count + 1, stride=4, axis=axis)
    tail = jnp.expand_dims(tail, axis + 1)
    return jnp.concatenate([core, tail], axis + 1)


def merge_windows(field, axis, count, keep_tail):
    core = lax.slice_in_dim(field, 0, 4, axis=axis + 1)
    tail = lax.slice_in_dim(field, 4, 5, axis=axis + 1)
    zero_brick = jnp.zeros_like(lax.slice_in_dim(core, 0, 1, axis=axis))
    core = jnp.concatenate([core, zero_brick], axis)
    zero_tail = jnp.zeros_like(lax.slice_in_dim(tail, 0, 1, axis=axis))
    tail = jnp.concatenate([zero_tail, tail], axis)
    first = lax.slice_in_dim(core, 0, 1, axis=axis + 1) + tail
    rest = lax.slice_in_dim(core, 1, 4, axis=axis + 1)
    joined = jnp.concatenate([first, rest], axis + 1)
    joined = joined.reshape(field.shape[:axis] + (4 * (count + 1),) + field.shape[axis + 2 :])
    length = 4 * count + 1 if keep_tail else 4 * count
    return lax.slice_in_dim(joined, 0, length, axis=axis)


def window_map(count, length):
    extent = jnp.arange(5, dtype=jnp.int32)[:, None, None]
    brick = jnp.arange(count, dtype=jnp.int32)[None, :, None]
    cell = jnp.arange(length, dtype=jnp.int32)[None, None, :]
    return (4 * brick + extent == cell).astype(jnp.float32)


def radial_fold(layers):
    arrived = passed_along(layers[:, :, -1], "radial", 1)
    return layers.at[:, :, 0].add(arrived)


def departed_mask(cross_rows, resident):
    rows = cross_rows.reshape(-1)
    lanes = 128
    high = jnp.where(rows >= 0, rows // lanes, -1)
    low = jnp.where(rows >= 0, rows % lanes, -1)
    high_hot = (high[:, None] == jnp.arange(resident // lanes, dtype=jnp.int32)[None, :]).astype(jnp.bfloat16)
    low_hot = (low[:, None] == jnp.arange(lanes, dtype=jnp.int32)[None, :]).astype(jnp.bfloat16)
    counts = jnp.einsum("sh,sl->hl", high_hot, low_hot, preferred_element_type=jnp.float32)
    return counts.reshape(resident)


def gather_rows(table, rows, interpret=False):
    slots = rows.shape[0]
    height, width = table.shape
    chunk = math.gcd(slots, 4096)
    steps = slots // chunk
    rows = jnp.clip(rows, 0, height - 1).reshape(steps, 1, chunk)

    def kernel(row_ref, table_ref, out_ref):
        def body(i, carry):
            row = row_ref[0, 0, i]
            out_ref[pl.ds(i, 1), :] = table_ref[pl.ds(row, 1), :]
            return carry

        lax.fori_loop(0, chunk, body, 0, unroll=16)

    return pl.pallas_call(
        kernel,
        out_shape=jax.ShapeDtypeStruct((slots, width), table.dtype),
        grid=(steps,),
        in_specs=[
            pl.BlockSpec((1, 1, chunk), lambda s: (s, 0, 0), memory_space=pltpu.SMEM),
            pl.BlockSpec((height, width), lambda s: (0, 0)),
        ],
        out_specs=pl.BlockSpec((chunk, width), lambda s: (s, 0)),
        compiler_params=pltpu.CompilerParams(vmem_limit_bytes=48 * 1024 * 1024),
        interpret=interpret,
    )(rows, table)


def per_device(parcel_load, parcel_offset, parcel_cell, cross_rows, block_brick, gas):
    span_x = gas.shape[1]
    span_y = gas.shape[2]
    span_z = gas.shape[3]
    count_x = span_x // 4
    count_y = span_y // 4
    count_z = span_z // 4
    brick_total = count_x * count_y * count_z
    resident = parcel_load.shape[1]
    block_count = block_brick.shape[0]
    brick_numbers = jnp.arange(brick_total, dtype=jnp.int32)
    attributes = jnp.concatenate(
        [parcel_load, parcel_offset, parcel_cell[None].astype(jnp.float32)], 0
    )
    usable = cross_rows >= 0
    safe_rows = jnp.maximum(cross_rows, 0)
    moving = gather_rows(attributes.T, safe_rows.reshape(-1)).T
    moving = moving.reshape(9, 2, -1) * usable[None].astype(jnp.float32)
    upward = moving[:, 0]
    downward = moving[:, 1]
    from_lower = passed_along(upward, "axial", 1)
    from_upper = passed_along(downward, "axial", -1)
    departed = departed_mask(cross_rows, resident)
    staying = jnp.concatenate([attributes[:8] * (1.0 - departed)[None], attributes[8:]], 0)
    staying_blocks = resident // 128
    selector = (block_brick[:, None] == brick_numbers[None, :]).astype(jnp.float32)

    def deposit_part(part_rows, part_selector):
        part_blocks = part_rows.shape[1] // 128
        part_rows = part_rows.reshape(9, part_blocks, 128)
        factor_x, factor_y, factor_z = axis_factors(part_rows[8].astype(jnp.int32), part_rows[5:8])
        load_x = (part_rows[:5][:, None] * factor_x[None]).reshape(25, part_blocks, 128)
        weight_yz = (factor_y[:, None] * factor_z[None]).reshape(25, part_blocks, 128)
        spread = jnp.einsum("agp,bgp->gab", load_x, weight_yz, precision=lax.Precision.HIGH)
        part_sums = jnp.einsum(
            "gb,gfe->feb", part_selector, spread.reshape(part_blocks, 5, 125),
            precision=lax.Precision.HIGH,
        )
        return part_sums, factor_x, weight_yz

    stay_sums, stay_x, stay_yz = deposit_part(staying, selector[:staying_blocks])
    moved = jnp.concatenate([from_lower, from_upper], 1)
    moved_sums, moved_x, moved_yz = deposit_part(moved, selector[staying_blocks:])
    brick_sums = stay_sums + moved_sums
    factor_x = jnp.concatenate([stay_x, moved_x], 1)
    weight_yz = jnp.concatenate([stay_yz, moved_yz], 1)
    if count_x == 1:
        laid = brick_sums.reshape(5, 25, 5, count_y, count_z)
        laid = jnp.einsum(
            "faeyk,ekz->fayz", laid, window_map(count_z, span_z), precision=lax.Precision.HIGH
        )
        laid = laid.reshape(5, 5, 5, count_y, span_z)
        deposit_grid = jnp.einsum(
            "fxwyz,wyn->fxnz", laid, window_map(count_y, span_y + 1),
            precision=lax.Precision.HIGH,
        )
    else:
        laid = jnp.transpose(brick_sums, (0, 2, 1))
        laid = laid.reshape(5, count_x, count_y, count_z, 5, 5, 5)
        laid = jnp.transpose(laid, (0, 1, 4, 2, 5, 3, 6))
        laid = merge_windows(laid, 1, count_x, True)
        laid = merge_windows(laid, 2, count_y, True)
        deposit_grid = merge_windows(laid, 3, count_z, False)
    incoming = passed_along(deposit_grid[:, span_x], "axial", 1)
    summed = deposit_grid[:, :span_x].at[:, 0].add(incoming)
    folded = radial_fold(summed)
    source = folded[:, :, :span_y]
    updated_gas = gas + COUPLE * source
    upper_face = passed_along(updated_gas[:, 0], "axial", -1)
    if count_x == 1:
        below_inner = passed_along(updated_gas[:, :, 0], "radial", -1)
        field_inner = jnp.concatenate([updated_gas, below_inner[:, :, None]], 2)
        below_face = passed_along(upper_face[:, 0], "radial", -1)
        field_face = jnp.concatenate([upper_face, below_face[:, None]], 1)[:, None]

        def window_part(field):
            layers = field.shape[1]
            part = jnp.einsum(
                "fxnz,wyn->fxwyz", field, window_map(count_y, span_y + 1),
                precision=lax.Precision.HIGH,
            )
            part = part.reshape(5, layers * 5, count_y, span_z)
            part = jnp.einsum(
                "fayz,ekz->faeyk", part, window_map(count_z, span_z),
                precision=lax.Precision.HIGH,
            )
            part = part.reshape(5, layers * 25, brick_total)
            return jnp.einsum("gb,feb->gfe", selector, part, precision=lax.Precision.HIGH)

        picked = jnp.concatenate([window_part(field_inner), window_part(field_face)], 2)
    else:
        extended = jnp.concatenate([updated_gas, upper_face[:, None]], 1)
        below_row = passed_along(extended[:, :, 0], "radial", -1)
        gas_field = jnp.concatenate([extended, below_row[:, :, None]], 2)
        gas_field = jnp.pad(gas_field, ((0, 0), (0, 0), (0, 0), (0, 1)))
        windows = split_windows(gas_field, 3, count_z)
        windows = split_windows(windows, 2, count_y)
        windows = split_windows(windows, 1, count_x)
        windows = jnp.transpose(windows, (0, 1, 3, 5, 2, 4, 6)).reshape(5, brick_total, 125)
        picked = jnp.einsum("gb,fbe->gfe", selector, windows, precision=lax.Precision.HIGH)
    picked = picked.reshape(block_count, 25, 25)
    partial = jnp.einsum("gab,bgp->agp", picked, weight_yz, precision=lax.Precision.HIGH)
    values = jnp.sum(partial.reshape(5, 5, block_count, 128) * factor_x[None], axis=1)
    parcel_gas = values.reshape(5, block_count * 128).astype(jnp.bfloat16)
    return (source, parcel_gas)


def solution(mesh):
    return jax.shard_map(
        per_device,
        mesh=mesh,
        in_specs=(
            P(None, ("axial", "radial")),
            P(None, ("axial", "radial")),
            P(("axial", "radial")),
            P(None, ("axial", "radial")),
            P(("axial", "radial")),
            P(None, "axial", "radial", None),
        ),
        out_specs=(P(None, "axial", "radial", None), P(None, ("axial", "radial"))),
        check_vma=False,
    )
```

```python
import math

import jax
import jax.numpy as jnp
from jax import lax
from jax.experimental import pallas as pl
from jax.experimental.pallas import tpu as pltpu
from jax.sharding import PartitionSpec as P

COUPLE = 0.5


def passed_along(block, axis, distance):
    devices = range(lax.axis_size(axis))
    route = [(i - distance, i) for i in devices if i - distance in devices]
    return lax.ppermute(block, axis, route)


def kernel_weights(cell_index, offsets):
    extent = jnp.arange(128, dtype=jnp.int32)
    brick_x = extent // 25
    brick_y = extent // 5 % 5
    brick_z = extent % 5
    inside = (extent < 125).astype(jnp.float32)

    def factor(cell_coord, brick_coord, fraction):
        cell_coord = cell_coord[:, :, None]
        fraction = fraction[:, :, None]
        return jnp.where(
            brick_coord == cell_coord,
            1.0 - fraction,
            jnp.where(brick_coord == cell_coord + 1, fraction, 0.0),
        )

    cell_x = cell_index // 16
    cell_y = cell_index // 4 % 4
    cell_z = cell_index % 4
    return (
        factor(cell_x, brick_x, offsets[0])
        * factor(cell_y, brick_y, offsets[1])
        * factor(cell_z, brick_z, offsets[2])
        * inside
    )


def axis_factors(cell_index, offsets):
    extent = jnp.arange(5, dtype=jnp.int32).reshape((5,) + (1,) * cell_index.ndim)

    def factor(cell_coord, fraction):
        return jnp.where(
            extent == cell_coord[None],
            1.0 - fraction[None],
            jnp.where(extent == cell_coord[None] + 1, fraction[None], 0.0),
        )

    return (
        factor(cell_index // 16, offsets[0]),
        factor(cell_index // 4 % 4, offsets[1]),
        factor(cell_index % 4, offsets[2]),
    )


def split_windows(field, axis, count):
    core = lax.slice_in_dim(field, 0, 4 * count, axis=axis)
    core = core.reshape(field.shape[:axis] + (count, 4) + field.shape[axis + 1 :])
    tail = lax.slice_in_dim(field, 4, 4 * count + 1, stride=4, axis=axis)
    tail = jnp.expand_dims(tail, axis + 1)
    return jnp.concatenate([core, tail], axis + 1)


def merge_windows(field, axis, count, keep_tail):
    core = lax.slice_in_dim(field, 0, 4, axis=axis + 1)
    tail = lax.slice_in_dim(field, 4, 5, axis=axis + 1)
    zero_brick = jnp.zeros_like(lax.slice_in_dim(core, 0, 1, axis=axis))
    core = jnp.concatenate([core, zero_brick], axis)
    zero_tail = jnp.zeros_like(lax.slice_in_dim(tail, 0, 1, axis=axis))
    tail = jnp.concatenate([zero_tail, tail], axis)
    first = lax.slice_in_dim(core, 0, 1, axis=axis + 1) + tail
    rest = lax.slice_in_dim(core, 1, 4, axis=axis + 1)
    joined = jnp.concatenate([first, rest], axis + 1)
    joined = joined.reshape(field.shape[:axis] + (4 * (count + 1),) + field.shape[axis + 2 :])
    length = 4 * count + 1 if keep_tail else 4 * count
    return lax.slice_in_dim(joined, 0, length, axis=axis)


def window_map(count, length):
    extent = jnp.arange(5, dtype=jnp.int32)[:, None, None]
    brick = jnp.arange(count, dtype=jnp.int32)[None, :, None]
    cell = jnp.arange(length, dtype=jnp.int32)[None, None, :]
    return (4 * brick + extent == cell).astype(jnp.float32)


def radial_fold(layers):
    arrived = passed_along(layers[:, :, -1], "radial", 1)
    return layers.at[:, :, 0].add(arrived)


def departed_mask(cross_rows, resident):
    rows = cross_rows.reshape(-1)
    lanes = 128
    high = jnp.where(rows >= 0, rows // lanes, -1)
    low = jnp.where(rows >= 0, rows % lanes, -1)
    high_hot = (high[:, None] == jnp.arange(resident // lanes, dtype=jnp.int32)[None, :]).astype(jnp.bfloat16)
    low_hot = (low[:, None] == jnp.arange(lanes, dtype=jnp.int32)[None, :]).astype(jnp.bfloat16)
    counts = jnp.einsum("sh,sl->hl", high_hot, low_hot, preferred_element_type=jnp.float32)
    return counts.reshape(resident)


def gather_rows(table, rows, interpret=False):
    slots = rows.shape[0]
    height, width = table.shape
    chunk = math.gcd(slots, 4096)
    steps = slots // chunk
    rows = jnp.clip(rows, 0, height - 1).reshape(steps, 1, chunk)

    def kernel(row_ref, table_ref, out_ref):
        def body(i, carry):
            row = row_ref[0, 0, i]
            out_ref[pl.ds(i, 1), :] = table_ref[pl.ds(row, 1), :]
            return carry

        lax.fori_loop(0, chunk, body, 0, unroll=16)

    return pl.pallas_call(
        kernel,
        out_shape=jax.ShapeDtypeStruct((slots, width), table.dtype),
        grid=(steps,),
        in_specs=[
            pl.BlockSpec((1, 1, chunk), lambda s: (s, 0, 0), memory_space=pltpu.SMEM),
            pl.BlockSpec((height, width), lambda s: (0, 0)),
        ],
        out_specs=pl.BlockSpec((chunk, width), lambda s: (s, 0)),
        compiler_params=pltpu.CompilerParams(vmem_limit_bytes=48 * 1024 * 1024),
        interpret=interpret,
    )(rows, table)


def per_device(parcel_load, parcel_offset, parcel_cell, cross_rows, block_brick, gas):
    span_x = gas.shape[1]
    span_y = gas.shape[2]
    span_z = gas.shape[3]
    count_x = span_x // 4
    count_y = span_y // 4
    count_z = span_z // 4
    brick_total = count_x * count_y * count_z
    resident = parcel_load.shape[1]
    block_count = block_brick.shape[0]
    brick_numbers = jnp.arange(brick_total, dtype=jnp.int32)
    attributes = jnp.concatenate(
        [parcel_load, parcel_offset, parcel_cell[None].astype(jnp.float32)], 0
    )
    usable = cross_rows >= 0
    safe_rows = jnp.maximum(cross_rows, 0)
    table = attributes.T
    upward = gather_rows(table, safe_rows[0]).T * usable[0].astype(jnp.float32)
    from_lower = passed_along(upward, "axial", 1)
    downward = gather_rows(table, safe_rows[1]).T * usable[1].astype(jnp.float32)
    from_upper = passed_along(downward, "axial", -1)
    departed = departed_mask(cross_rows, resident)
    staying = jnp.concatenate([attributes[:8] * (1.0 - departed)[None], attributes[8:]], 0)
    staying_blocks = resident // 128
    selector = (block_brick[:, None] == brick_numbers[None, :]).astype(jnp.float32)

    def deposit_part(part_rows, part_selector):
        part_blocks = part_rows.shape[1] // 128
        part_rows = part_rows.reshape(9, part_blocks, 128)
        factor_x, factor_y, factor_z = axis_factors(part_rows[8].astype(jnp.int32), part_rows[5:8])
        load_x = (part_rows[:5][:, None] * factor_x[None]).reshape(25, part_blocks, 128)
        weight_yz = (factor_y[:, None] * factor_z[None]).reshape(25, part_blocks, 128)
        spread = jnp.einsum("agp,bgp->gab", load_x, weight_yz, precision=lax.Precision.HIGH)
        part_sums = jnp.einsum(
            "gb,gfe->feb", part_selector, spread.reshape(part_blocks, 5, 125),
            precision=lax.Precision.HIGH,
        )
        return part_sums, factor_x, weight_yz

    stay_sums, stay_x, stay_yz = deposit_part(staying, selector[:staying_blocks])
    from_lower, from_upper, stay_sums = lax.optimization_barrier((from_lower, from_upper, stay_sums))
    moved = jnp.concatenate([from_lower, from_upper], 1)
    moved_sums, moved_x, moved_yz = deposit_part(moved, selector[staying_blocks:])
    brick_sums = stay_sums + moved_sums
    factor_x = jnp.concatenate([stay_x, moved_x], 1)
    weight_yz = jnp.concatenate([stay_yz, moved_yz], 1)
    if count_x == 1:
        laid = brick_sums.reshape(5, 25, 5, count_y, count_z)
        laid = jnp.einsum(
            "faeyk,ekz->fayz", laid, window_map(count_z, span_z), precision=lax.Precision.HIGH
        )
        laid = laid.reshape(5, 5, 5, count_y, span_z)
        deposit_grid = jnp.einsum(
            "fxwyz,wyn->fxnz", laid, window_map(count_y, span_y + 1),
            precision=lax.Precision.HIGH,
        )
    else:
        laid = jnp.transpose(brick_sums, (0, 2, 1))
        laid = laid.reshape(5, count_x, count_y, count_z, 5, 5, 5)
        laid = jnp.transpose(laid, (0, 1, 4, 2, 5, 3, 6))
        laid = merge_windows(laid, 1, count_x, True)
        laid = merge_windows(laid, 2, count_y, True)
        deposit_grid = merge_windows(laid, 3, count_z, False)
    incoming = passed_along(deposit_grid[:, span_x], "axial", 1)
    summed = deposit_grid[:, :span_x].at[:, 0].add(incoming)
    folded = radial_fold(summed)
    source = folded[:, :, :span_y]
    updated_gas = gas + COUPLE * source
    upper_face = passed_along(updated_gas[:, 0], "axial", -1)
    if count_x == 1:
        below_inner = passed_along(updated_gas[:, :, 0], "radial", -1)
        field_inner = jnp.concatenate([updated_gas, below_inner[:, :, None]], 2)
        below_face = passed_along(upper_face[:, 0], "radial", -1)
        field_face = jnp.concatenate([upper_face, below_face[:, None]], 1)[:, None]

        def window_part(field):
            layers = field.shape[1]
            part = jnp.einsum(
                "fxnz,wyn->fxwyz", field, window_map(count_y, span_y + 1),
                precision=lax.Precision.HIGH,
            )
            part = part.reshape(5, layers * 5, count_y, span_z)
            part = jnp.einsum(
                "fayz,ekz->faeyk", part, window_map(count_z, span_z),
                precision=lax.Precision.HIGH,
            )
            part = part.reshape(5, layers * 25, brick_total)
            return jnp.einsum("gb,feb->gfe", selector, part, precision=lax.Precision.HIGH)

        picked = jnp.concatenate([window_part(field_inner), window_part(field_face)], 2)
    else:
        extended = jnp.concatenate([updated_gas, upper_face[:, None]], 1)
        below_row = passed_along(extended[:, :, 0], "radial", -1)
        gas_field = jnp.concatenate([extended, below_row[:, :, None]], 2)
        gas_field = jnp.pad(gas_field, ((0, 0), (0, 0), (0, 0), (0, 1)))
        windows = split_windows(gas_field, 3, count_z)
        windows = split_windows(windows, 2, count_y)
        windows = split_windows(windows, 1, count_x)
        windows = jnp.transpose(windows, (0, 1, 3, 5, 2, 4, 6)).reshape(5, brick_total, 125)
        picked = jnp.einsum("gb,fbe->gfe", selector, windows, precision=lax.Precision.HIGH)
    picked = picked.reshape(block_count, 25, 25)
    partial = jnp.einsum("gab,bgp->agp", picked, weight_yz, precision=lax.Precision.HIGH)
    values = jnp.sum(partial.reshape(5, 5, block_count, 128) * factor_x[None], axis=1)
    parcel_gas = values.reshape(5, block_count * 128).astype(jnp.bfloat16)
    return (source, parcel_gas)


def solution(mesh):
    return jax.shard_map(
        per_device,
        mesh=mesh,
        in_specs=(
            P(None, ("axial", "radial")),
            P(None, ("axial", "radial")),
            P(("axial", "radial")),
            P(None, ("axial", "radial")),
            P(("axial", "radial")),
            P(None, "axial", "radial", None),
        ),
        out_specs=(P(None, "axial", "radial", None), P(None, ("axial", "radial"))),
        check_vma=False,
    )
```

```python
import math

import jax
import jax.numpy as jnp
from jax import lax
from jax.experimental import pallas as pl
from jax.experimental.pallas import tpu as pltpu
from jax.sharding import PartitionSpec as P

COUPLE = 0.5


def passed_along(block, axis, distance):
    devices = range(lax.axis_size(axis))
    route = [(i - distance, i) for i in devices if i - distance in devices]
    return lax.ppermute(block, axis, route)


def kernel_weights(cell_index, offsets):
    extent = jnp.arange(128, dtype=jnp.int32)
    brick_x = extent // 25
    brick_y = extent // 5 % 5
    brick_z = extent % 5
    inside = (extent < 125).astype(jnp.float32)

    def factor(cell_coord, brick_coord, fraction):
        cell_coord = cell_coord[:, :, None]
        fraction = fraction[:, :, None]
        return jnp.where(
            brick_coord == cell_coord,
            1.0 - fraction,
            jnp.where(brick_coord == cell_coord + 1, fraction, 0.0),
        )

    cell_x = cell_index // 16
    cell_y = cell_index // 4 % 4
    cell_z = cell_index % 4
    return (
        factor(cell_x, brick_x, offsets[0])
        * factor(cell_y, brick_y, offsets[1])
        * factor(cell_z, brick_z, offsets[2])
        * inside
    )


def axis_factors(cell_index, offsets):
    extent = jnp.arange(5, dtype=jnp.int32).reshape((5,) + (1,) * cell_index.ndim)

    def factor(cell_coord, fraction):
        return jnp.where(
            extent == cell_coord[None],
            1.0 - fraction[None],
            jnp.where(extent == cell_coord[None] + 1, fraction[None], 0.0),
        )

    return (
        factor(cell_index // 16, offsets[0]),
        factor(cell_index // 4 % 4, offsets[1]),
        factor(cell_index % 4, offsets[2]),
    )


def split_windows(field, axis, count):
    core = lax.slice_in_dim(field, 0, 4 * count, axis=axis)
    core = core.reshape(field.shape[:axis] + (count, 4) + field.shape[axis + 1 :])
    tail = lax.slice_in_dim(field, 4, 4 * count + 1, stride=4, axis=axis)
    tail = jnp.expand_dims(tail, axis + 1)
    return jnp.concatenate([core, tail], axis + 1)


def merge_windows(field, axis, count, keep_tail):
    core = lax.slice_in_dim(field, 0, 4, axis=axis + 1)
    tail = lax.slice_in_dim(field, 4, 5, axis=axis + 1)
    zero_brick = jnp.zeros_like(lax.slice_in_dim(core, 0, 1, axis=axis))
    core = jnp.concatenate([core, zero_brick], axis)
    zero_tail = jnp.zeros_like(lax.slice_in_dim(tail, 0, 1, axis=axis))
    tail = jnp.concatenate([zero_tail, tail], axis)
    first = lax.slice_in_dim(core, 0, 1, axis=axis + 1) + tail
    rest = lax.slice_in_dim(core, 1, 4, axis=axis + 1)
    joined = jnp.concatenate([first, rest], axis + 1)
    joined = joined.reshape(field.shape[:axis] + (4 * (count + 1),) + field.shape[axis + 2 :])
    length = 4 * count + 1 if keep_tail else 4 * count
    return lax.slice_in_dim(joined, 0, length, axis=axis)


def window_map(count, length):
    extent = jnp.arange(5, dtype=jnp.int32)[:, None, None]
    brick = jnp.arange(count, dtype=jnp.int32)[None, :, None]
    cell = jnp.arange(length, dtype=jnp.int32)[None, None, :]
    return (4 * brick + extent == cell).astype(jnp.float32)


def radial_fold(layers):
    arrived = passed_along(layers[:, :, -1], "radial", 1)
    return layers.at[:, :, 0].add(arrived)


def departed_mask(cross_rows, resident):
    rows = cross_rows.reshape(-1)
    lanes = 128
    high = jnp.where(rows >= 0, rows // lanes, -1)
    low = jnp.where(rows >= 0, rows % lanes, -1)
    high_hot = (high[:, None] == jnp.arange(resident // lanes, dtype=jnp.int32)[None, :]).astype(jnp.bfloat16)
    low_hot = (low[:, None] == jnp.arange(lanes, dtype=jnp.int32)[None, :]).astype(jnp.bfloat16)
    counts = jnp.einsum("sh,sl->hl", high_hot, low_hot, preferred_element_type=jnp.float32)
    return counts.reshape(resident)


def gather_rows(table, rows, interpret=False):
    slots = rows.shape[0]
    height, width = table.shape
    tile = 128
    chunk = math.gcd(slots, 4096)
    steps = slots // chunk
    keep = (rows >= 0).astype(jnp.float32).reshape(steps, 1, chunk)
    rows = jnp.clip(rows, 0, height - 1).reshape(steps, 1, chunk)

    def kernel(row_ref, keep_ref, table_ref, out_ref, tile_ref):
        tile_ref[...] = jnp.zeros_like(tile_ref)

        def tile_body(c, carry):
            def row_body(i, carry):
                slot = c * tile + i
                row = row_ref[0, 0, slot]
                tile_ref[pl.ds(i, 1), pl.ds(0, width)] = (
                    table_ref[pl.ds(row, 1), :] * keep_ref[0, 0, slot]
                )
                return carry

            lax.fori_loop(0, tile, row_body, 0, unroll=16)
            start = pl.multiple_of(c * tile, tile)
            out_ref[:, pl.ds(start, tile)] = tile_ref[...].T[:width, :]
            return carry

        lax.fori_loop(0, chunk // tile, tile_body, 0)

    return pl.pallas_call(
        kernel,
        out_shape=jax.ShapeDtypeStruct((width, slots), table.dtype),
        grid=(steps,),
        in_specs=[
            pl.BlockSpec((1, 1, chunk), lambda s: (s, 0, 0), memory_space=pltpu.SMEM),
            pl.BlockSpec((1, 1, chunk), lambda s: (s, 0, 0), memory_space=pltpu.SMEM),
            pl.BlockSpec((height, width), lambda s: (0, 0)),
        ],
        out_specs=pl.BlockSpec((width, chunk), lambda s: (0, s)),
        scratch_shapes=[pltpu.VMEM((tile, tile), jnp.float32)],
        compiler_params=pltpu.CompilerParams(vmem_limit_bytes=48 * 1024 * 1024),
        interpret=interpret,
    )(rows, keep, table)


def per_device(parcel_load, parcel_offset, parcel_cell, cross_rows, block_brick, gas):
    span_x = gas.shape[1]
    span_y = gas.shape[2]
    span_z = gas.shape[3]
    count_x = span_x // 4
    count_y = span_y // 4
    count_z = span_z // 4
    brick_total = count_x * count_y * count_z
    resident = parcel_load.shape[1]
    block_count = block_brick.shape[0]
    brick_numbers = jnp.arange(brick_total, dtype=jnp.int32)
    attributes = jnp.concatenate(
        [parcel_load, parcel_offset, parcel_cell[None].astype(jnp.float32)], 0
    )
    table = attributes.T
    upward = gather_rows(table, cross_rows[0])
    from_lower = passed_along(upward, "axial", 1)
    downward = gather_rows(table, cross_rows[1])
    from_upper = passed_along(downward, "axial", -1)
    departed = departed_mask(cross_rows, resident)
    staying = jnp.concatenate([attributes[:8] * (1.0 - departed)[None], attributes[8:]], 0)
    staying_blocks = resident // 128
    selector = (block_brick[:, None] == brick_numbers[None, :]).astype(jnp.float32)

    def deposit_part(part_rows, part_selector):
        part_blocks = part_rows.shape[1] // 128
        part_rows = part_rows.reshape(9, part_blocks, 128)
        factor_x, factor_y, factor_z = axis_factors(part_rows[8].astype(jnp.int32), part_rows[5:8])
        load_x = (part_rows[:5][:, None] * factor_x[None]).reshape(25, part_blocks, 128)
        weight_yz = (factor_y[:, None] * factor_z[None]).reshape(25, part_blocks, 128)
        spread = jnp.einsum("agp,bgp->gab", load_x, weight_yz, precision=lax.Precision.HIGH)
        part_sums = jnp.einsum(
            "gb,gfe->feb", part_selector, spread.reshape(part_blocks, 5, 125),
            precision=lax.Precision.HIGH,
        )
        return part_sums, factor_x, weight_yz

    stay_sums, stay_x, stay_yz = deposit_part(staying, selector[:staying_blocks])
    from_lower, from_upper, stay_sums = lax.optimization_barrier((from_lower, from_upper, stay_sums))
    moved = jnp.concatenate([from_lower, from_upper], 1)
    moved_sums, moved_x, moved_yz = deposit_part(moved, selector[staying_blocks:])
    brick_sums = stay_sums + moved_sums
    factor_x = jnp.concatenate([stay_x, moved_x], 1)
    weight_yz = jnp.concatenate([stay_yz, moved_yz], 1)
    if count_x == 1:
        laid = brick_sums.reshape(5, 25, 5, count_y, count_z)
        laid = jnp.einsum(
            "faeyk,ekz->fayz", laid, window_map(count_z, span_z), precision=lax.Precision.HIGH
        )
        laid = laid.reshape(5, 5, 5, count_y, span_z)
        deposit_grid = jnp.einsum(
            "fxwyz,wyn->fxnz", laid, window_map(count_y, span_y + 1),
            precision=lax.Precision.HIGH,
        )
    else:
        laid = jnp.transpose(brick_sums, (0, 2, 1))
        laid = laid.reshape(5, count_x, count_y, count_z, 5, 5, 5)
        laid = jnp.transpose(laid, (0, 1, 4, 2, 5, 3, 6))
        laid = merge_windows(laid, 1, count_x, True)
        laid = merge_windows(laid, 2, count_y, True)
        deposit_grid = merge_windows(laid, 3, count_z, False)
    incoming = passed_along(deposit_grid[:, span_x], "axial", 1)
    summed = deposit_grid[:, :span_x].at[:, 0].add(incoming)
    folded = radial_fold(summed)
    source = folded[:, :, :span_y]
    updated_gas = gas + COUPLE * source
    upper_face = passed_along(updated_gas[:, 0], "axial", -1)
    if count_x == 1:
        below_inner = passed_along(updated_gas[:, :, 0], "radial", -1)
        field_inner = jnp.concatenate([updated_gas, below_inner[:, :, None]], 2)
        below_face = passed_along(upper_face[:, 0], "radial", -1)
        field_face = jnp.concatenate([upper_face, below_face[:, None]], 1)[:, None]

        def window_part(field):
            layers = field.shape[1]
            part = jnp.einsum(
                "fxnz,wyn->fxwyz", field, window_map(count_y, span_y + 1),
                precision=lax.Precision.HIGH,
            )
            part = part.reshape(5, layers * 5, count_y, span_z)
            part = jnp.einsum(
                "fayz,ekz->faeyk", part, window_map(count_z, span_z),
                precision=lax.Precision.HIGH,
            )
            part = part.reshape(5, layers * 25, brick_total)
            return jnp.einsum("gb,feb->gfe", selector, part, precision=lax.Precision.HIGH)

        picked = jnp.concatenate([window_part(field_inner), window_part(field_face)], 2)
    else:
        extended = jnp.concatenate([updated_gas, upper_face[:, None]], 1)
        below_row = passed_along(extended[:, :, 0], "radial", -1)
        gas_field = jnp.concatenate([extended, below_row[:, :, None]], 2)
        gas_field = jnp.pad(gas_field, ((0, 0), (0, 0), (0, 0), (0, 1)))
        windows = split_windows(gas_field, 3, count_z)
        windows = split_windows(windows, 2, count_y)
        windows = split_windows(windows, 1, count_x)
        windows = jnp.transpose(windows, (0, 1, 3, 5, 2, 4, 6)).reshape(5, brick_total, 125)
        picked = jnp.einsum("gb,fbe->gfe", selector, windows, precision=lax.Precision.HIGH)
    picked = picked.reshape(block_count, 25, 25)
    partial = jnp.einsum("gab,bgp->agp", picked, weight_yz, precision=lax.Precision.HIGH)
    values = jnp.sum(partial.reshape(5, 5, block_count, 128) * factor_x[None], axis=1)
    parcel_gas = values.reshape(5, block_count * 128).astype(jnp.bfloat16)
    return (source, parcel_gas)


def solution(mesh):
    return jax.shard_map(
        per_device,
        mesh=mesh,
        in_specs=(
            P(None, ("axial", "radial")),
            P(None, ("axial", "radial")),
            P(("axial", "radial")),
            P(None, ("axial", "radial")),
            P(("axial", "radial")),
            P(None, "axial", "radial", None),
        ),
        out_specs=(P(None, "axial", "radial", None), P(None, ("axial", "radial"))),
        check_vma=False,
    )
```

```python
import math

import jax
import jax.numpy as jnp
from jax import lax
from jax.experimental import pallas as pl
from jax.experimental.pallas import tpu as pltpu
from jax.sharding import PartitionSpec as P

COUPLE = 0.5


def passed_along(block, axis, distance):
    devices = range(lax.axis_size(axis))
    route = [(i - distance, i) for i in devices if i - distance in devices]
    return lax.ppermute(block, axis, route)


def kernel_weights(cell_index, offsets):
    extent = jnp.arange(128, dtype=jnp.int32)
    brick_x = extent // 25
    brick_y = extent // 5 % 5
    brick_z = extent % 5
    inside = (extent < 125).astype(jnp.float32)

    def factor(cell_coord, brick_coord, fraction):
        cell_coord = cell_coord[:, :, None]
        fraction = fraction[:, :, None]
        return jnp.where(
            brick_coord == cell_coord,
            1.0 - fraction,
            jnp.where(brick_coord == cell_coord + 1, fraction, 0.0),
        )

    cell_x = cell_index // 16
    cell_y = cell_index // 4 % 4
    cell_z = cell_index % 4
    return (
        factor(cell_x, brick_x, offsets[0])
        * factor(cell_y, brick_y, offsets[1])
        * factor(cell_z, brick_z, offsets[2])
        * inside
    )


def axis_factors(cell_index, offsets):
    extent = jnp.arange(5, dtype=jnp.int32).reshape((5,) + (1,) * cell_index.ndim)

    def factor(cell_coord, fraction):
        return jnp.where(
            extent == cell_coord[None],
            1.0 - fraction[None],
            jnp.where(extent == cell_coord[None] + 1, fraction[None], 0.0),
        )

    return (
        factor(cell_index // 16, offsets[0]),
        factor(cell_index // 4 % 4, offsets[1]),
        factor(cell_index % 4, offsets[2]),
    )


def split_windows(field, axis, count):
    core = lax.slice_in_dim(field, 0, 4 * count, axis=axis)
    core = core.reshape(field.shape[:axis] + (count, 4) + field.shape[axis + 1 :])
    tail = lax.slice_in_dim(field, 4, 4 * count + 1, stride=4, axis=axis)
    tail = jnp.expand_dims(tail, axis + 1)
    return jnp.concatenate([core, tail], axis + 1)


def merge_windows(field, axis, count, keep_tail):
    core = lax.slice_in_dim(field, 0, 4, axis=axis + 1)
    tail = lax.slice_in_dim(field, 4, 5, axis=axis + 1)
    zero_brick = jnp.zeros_like(lax.slice_in_dim(core, 0, 1, axis=axis))
    core = jnp.concatenate([core, zero_brick], axis)
    zero_tail = jnp.zeros_like(lax.slice_in_dim(tail, 0, 1, axis=axis))
    tail = jnp.concatenate([zero_tail, tail], axis)
    first = lax.slice_in_dim(core, 0, 1, axis=axis + 1) + tail
    rest = lax.slice_in_dim(core, 1, 4, axis=axis + 1)
    joined = jnp.concatenate([first, rest], axis + 1)
    joined = joined.reshape(field.shape[:axis] + (4 * (count + 1),) + field.shape[axis + 2 :])
    length = 4 * count + 1 if keep_tail else 4 * count
    return lax.slice_in_dim(joined, 0, length, axis=axis)


def hot_dot(spec, hot, data):
    scaled = data * 65537.0
    high = scaled - (scaled - data)
    low = data - high
    terms, result = spec.split("->")
    hot_terms, data_terms = terms.split(",")
    both = jnp.einsum(
        hot_terms + ",s" + data_terms + "->s" + result,
        hot.astype(jnp.bfloat16),
        jnp.stack([high, low]).astype(jnp.bfloat16),
        preferred_element_type=jnp.float32,
    )
    return both[0] + both[1]


def window_map(count, length):
    extent = jnp.arange(5, dtype=jnp.int32)[:, None, None]
    brick = jnp.arange(count, dtype=jnp.int32)[None, :, None]
    cell = jnp.arange(length, dtype=jnp.int32)[None, None, :]
    return (4 * brick + extent == cell).astype(jnp.float32)


def radial_fold(layers):
    arrived = passed_along(layers[:, :, -1], "radial", 1)
    return layers.at[:, :, 0].add(arrived)


def departed_mask(cross_rows, resident):
    rows = cross_rows.reshape(-1)
    lanes = 128
    high = jnp.where(rows >= 0, rows // lanes, -1)
    low = jnp.where(rows >= 0, rows % lanes, -1)
    high_hot = (high[:, None] == jnp.arange(resident // lanes, dtype=jnp.int32)[None, :]).astype(jnp.bfloat16)
    low_hot = (low[:, None] == jnp.arange(lanes, dtype=jnp.int32)[None, :]).astype(jnp.bfloat16)
    counts = jnp.einsum("sh,sl->hl", high_hot, low_hot, preferred_element_type=jnp.float32)
    return counts.reshape(resident)


def gather_rows(table, rows, interpret=False):
    slots = rows.shape[0]
    height, width = table.shape
    chunk = math.gcd(slots, 4096)
    steps = slots // chunk
    rows = jnp.clip(rows, 0, height - 1).reshape(steps, 1, chunk)

    def kernel(row_ref, table_ref, out_ref):
        def body(i, carry):
            row = row_ref[0, 0, i]
            out_ref[pl.ds(i, 1), :] = table_ref[pl.ds(row, 1), :]
            return carry

        lax.fori_loop(0, chunk, body, 0, unroll=16)

    return pl.pallas_call(
        kernel,
        out_shape=jax.ShapeDtypeStruct((slots, width), table.dtype),
        grid=(steps,),
        in_specs=[
            pl.BlockSpec((1, 1, chunk), lambda s: (s, 0, 0), memory_space=pltpu.SMEM),
            pl.BlockSpec((height, width), lambda s: (0, 0)),
        ],
        out_specs=pl.BlockSpec((chunk, width), lambda s: (s, 0)),
        compiler_params=pltpu.CompilerParams(vmem_limit_bytes=48 * 1024 * 1024),
        interpret=interpret,
    )(rows, table)


def per_device(parcel_load, parcel_offset, parcel_cell, cross_rows, block_brick, gas):
    span_x = gas.shape[1]
    span_y = gas.shape[2]
    span_z = gas.shape[3]
    count_x = span_x // 4
    count_y = span_y // 4
    count_z = span_z // 4
    brick_total = count_x * count_y * count_z
    resident = parcel_load.shape[1]
    block_count = block_brick.shape[0]
    brick_numbers = jnp.arange(brick_total, dtype=jnp.int32)
    attributes = jnp.concatenate(
        [parcel_load, parcel_offset, parcel_cell[None].astype(jnp.float32)], 0
    )
    usable = cross_rows >= 0
    safe_rows = jnp.maximum(cross_rows, 0)
    table = attributes.T
    upward = gather_rows(table, safe_rows[0]).T * usable[0].astype(jnp.float32)
    from_lower = passed_along(upward, "axial", 1)
    downward = gather_rows(table, safe_rows[1]).T * usable[1].astype(jnp.float32)
    from_upper = passed_along(downward, "axial", -1)
    departed = departed_mask(cross_rows, resident)
    staying = jnp.concatenate([attributes[:8] * (1.0 - departed)[None], attributes[8:]], 0)
    staying_blocks = resident // 128
    selector = (block_brick[:, None] == brick_numbers[None, :]).astype(jnp.float32)

    def deposit_part(part_rows, part_selector):
        part_blocks = part_rows.shape[1] // 128
        part_rows = part_rows.reshape(9, part_blocks, 128)
        factor_x, factor_y, factor_z = axis_factors(part_rows[8].astype(jnp.int32), part_rows[5:8])
        load_x = (part_rows[:5][:, None] * factor_x[None]).reshape(25, part_blocks, 128)
        weight_yz = (factor_y[:, None] * factor_z[None]).reshape(25, part_blocks, 128)
        spread = jnp.einsum("agp,bgp->gab", load_x, weight_yz, precision=lax.Precision.HIGH)
        part_sums = hot_dot("gb,gfe->feb", part_selector, spread.reshape(part_blocks, 5, 125))
        return part_sums, factor_x, weight_yz

    stay_sums, stay_x, stay_yz = deposit_part(staying, selector[:staying_blocks])
    from_lower, from_upper, stay_sums = lax.optimization_barrier((from_lower, from_upper, stay_sums))
    moved = jnp.concatenate([from_lower, from_upper], 1)
    moved_sums, moved_x, moved_yz = deposit_part(moved, selector[staying_blocks:])
    brick_sums = stay_sums + moved_sums
    factor_x = jnp.concatenate([stay_x, moved_x], 1)
    weight_yz = jnp.concatenate([stay_yz, moved_yz], 1)
    if count_x == 1:
        laid = brick_sums.reshape(5, 25, 5, count_y, count_z)
        laid = hot_dot("ekz,faeyk->fayz", window_map(count_z, span_z), laid)
        laid = laid.reshape(5, 5, 5, count_y, span_z)
        deposit_grid = hot_dot("wyn,fxwyz->fxnz", window_map(count_y, span_y + 1), laid)
    else:
        laid = jnp.transpose(brick_sums, (0, 2, 1))
        laid = laid.reshape(5, count_x, count_y, count_z, 5, 5, 5)
        laid = jnp.transpose(laid, (0, 1, 4, 2, 5, 3, 6))
        laid = merge_windows(laid, 1, count_x, True)
        laid = merge_windows(laid, 2, count_y, True)
        deposit_grid = merge_windows(laid, 3, count_z, False)
    incoming = passed_along(deposit_grid[:, span_x], "axial", 1)
    summed = deposit_grid[:, :span_x].at[:, 0].add(incoming)
    folded = radial_fold(summed)
    source = folded[:, :, :span_y]
    updated_gas = gas + COUPLE * source
    upper_face = passed_along(updated_gas[:, 0], "axial", -1)
    if count_x == 1:
        below_inner = passed_along(updated_gas[:, :, 0], "radial", -1)
        field_inner = jnp.concatenate([updated_gas, below_inner[:, :, None]], 2)
        below_face = passed_along(upper_face[:, 0], "radial", -1)
        field_face = jnp.concatenate([upper_face, below_face[:, None]], 1)[:, None]

        def window_part(field):
            layers = field.shape[1]
            part = hot_dot("wyn,fxnz->fxwyz", window_map(count_y, span_y + 1), field)
            part = part.reshape(5, layers * 5, count_y, span_z)
            part = hot_dot("ekz,fayz->faeyk", window_map(count_z, span_z), part)
            part = part.reshape(5, layers * 25, brick_total)
            return hot_dot("gb,feb->gfe", selector, part)

        picked = jnp.concatenate([window_part(field_inner), window_part(field_face)], 2)
    else:
        extended = jnp.concatenate([updated_gas, upper_face[:, None]], 1)
        below_row = passed_along(extended[:, :, 0], "radial", -1)
        gas_field = jnp.concatenate([extended, below_row[:, :, None]], 2)
        gas_field = jnp.pad(gas_field, ((0, 0), (0, 0), (0, 0), (0, 1)))
        windows = split_windows(gas_field, 3, count_z)
        windows = split_windows(windows, 2, count_y)
        windows = split_windows(windows, 1, count_x)
        windows = jnp.transpose(windows, (0, 1, 3, 5, 2, 4, 6)).reshape(5, brick_total, 125)
        picked = jnp.einsum("gb,fbe->gfe", selector, windows, precision=lax.Precision.HIGH)
    picked = picked.reshape(block_count, 25, 25)
    partial = jnp.einsum("gab,bgp->agp", picked, weight_yz, precision=lax.Precision.HIGH)
    values = jnp.sum(partial.reshape(5, 5, block_count, 128) * factor_x[None], axis=1)
    parcel_gas = values.reshape(5, block_count * 128).astype(jnp.bfloat16)
    return (source, parcel_gas)


def solution(mesh):
    return jax.shard_map(
        per_device,
        mesh=mesh,
        in_specs=(
            P(None, ("axial", "radial")),
            P(None, ("axial", "radial")),
            P(("axial", "radial")),
            P(None, ("axial", "radial")),
            P(("axial", "radial")),
            P(None, "axial", "radial", None),
        ),
        out_specs=(P(None, "axial", "radial", None), P(None, ("axial", "radial"))),
        check_vma=False,
    )
```

```python
import math

import jax
import jax.numpy as jnp
from jax import lax
from jax.experimental import pallas as pl
from jax.experimental.pallas import tpu as pltpu
from jax.sharding import PartitionSpec as P

COUPLE = 0.5


def passed_along(block, axis, distance):
    devices = range(lax.axis_size(axis))
    route = [(i - distance, i) for i in devices if i - distance in devices]
    return lax.ppermute(block, axis, route)


def kernel_weights(cell_index, offsets):
    extent = jnp.arange(128, dtype=jnp.int32)
    brick_x = extent // 25
    brick_y = extent // 5 % 5
    brick_z = extent % 5
    inside = (extent < 125).astype(jnp.float32)

    def factor(cell_coord, brick_coord, fraction):
        cell_coord = cell_coord[:, :, None]
        fraction = fraction[:, :, None]
        return jnp.where(
            brick_coord == cell_coord,
            1.0 - fraction,
            jnp.where(brick_coord == cell_coord + 1, fraction, 0.0),
        )

    cell_x = cell_index // 16
    cell_y = cell_index // 4 % 4
    cell_z = cell_index % 4
    return (
        factor(cell_x, brick_x, offsets[0])
        * factor(cell_y, brick_y, offsets[1])
        * factor(cell_z, brick_z, offsets[2])
        * inside
    )


def axis_factors(cell_index, offsets):
    extent = jnp.arange(5, dtype=jnp.int32).reshape((5,) + (1,) * cell_index.ndim)

    def factor(cell_coord, fraction):
        return jnp.where(
            extent == cell_coord[None],
            1.0 - fraction[None],
            jnp.where(extent == cell_coord[None] + 1, fraction[None], 0.0),
        )

    return (
        factor(cell_index // 16, offsets[0]),
        factor(cell_index // 4 % 4, offsets[1]),
        factor(cell_index % 4, offsets[2]),
    )


def split_windows(field, axis, count):
    core = lax.slice_in_dim(field, 0, 4 * count, axis=axis)
    core = core.reshape(field.shape[:axis] + (count, 4) + field.shape[axis + 1 :])
    tail = lax.slice_in_dim(field, 4, 4 * count + 1, stride=4, axis=axis)
    tail = jnp.expand_dims(tail, axis + 1)
    return jnp.concatenate([core, tail], axis + 1)


def merge_windows(field, axis, count, keep_tail):
    core = lax.slice_in_dim(field, 0, 4, axis=axis + 1)
    tail = lax.slice_in_dim(field, 4, 5, axis=axis + 1)
    zero_brick = jnp.zeros_like(lax.slice_in_dim(core, 0, 1, axis=axis))
    core = jnp.concatenate([core, zero_brick], axis)
    zero_tail = jnp.zeros_like(lax.slice_in_dim(tail, 0, 1, axis=axis))
    tail = jnp.concatenate([zero_tail, tail], axis)
    first = lax.slice_in_dim(core, 0, 1, axis=axis + 1) + tail
    rest = lax.slice_in_dim(core, 1, 4, axis=axis + 1)
    joined = jnp.concatenate([first, rest], axis + 1)
    joined = joined.reshape(field.shape[:axis] + (4 * (count + 1),) + field.shape[axis + 2 :])
    length = 4 * count + 1 if keep_tail else 4 * count
    return lax.slice_in_dim(joined, 0, length, axis=axis)


def window_map(count, length):
    extent = jnp.arange(5, dtype=jnp.int32)[:, None, None]
    brick = jnp.arange(count, dtype=jnp.int32)[None, :, None]
    cell = jnp.arange(length, dtype=jnp.int32)[None, None, :]
    return (4 * brick + extent == cell).astype(jnp.float32)


def radial_fold(layers):
    arrived = passed_along(layers[:, :, -1], "radial", 1)
    return layers.at[:, :, 0].add(arrived)


def departed_mask(cross_rows, resident):
    rows = cross_rows.reshape(-1)
    lanes = 128
    high = jnp.where(rows >= 0, rows // lanes, -1)
    low = jnp.where(rows >= 0, rows % lanes, -1)
    high_hot = (high[:, None] == jnp.arange(resident // lanes, dtype=jnp.int32)[None, :]).astype(jnp.bfloat16)
    low_hot = (low[:, None] == jnp.arange(lanes, dtype=jnp.int32)[None, :]).astype(jnp.bfloat16)
    counts = jnp.einsum("sh,sl->hl", high_hot, low_hot, preferred_element_type=jnp.float32)
    return counts.reshape(resident)


def gather_columns(table, rows, interpret=False):
    slots = rows.shape[0]
    width, length = table.shape
    lanes = 128
    chunk = math.gcd(slots, 4096)
    steps = slots // chunk
    keep = (rows >= 0).astype(jnp.float32).reshape(steps, 1, chunk)
    rows = jnp.clip(rows, 0, length - 1).reshape(steps, 1, chunk)

    def kernel(row_ref, keep_ref, table_ref, out_ref):
        lane = lax.broadcasted_iota(jnp.int32, (width, lanes), 1)

        def tile_body(c, carry):
            def slot_body(i, acc):
                slot = c * lanes + i
                row = row_ref[0, 0, slot]
                start = pl.multiple_of((row // lanes) * lanes, lanes)
                column = table_ref[:, pl.ds(start, lanes)] * keep_ref[0, 0, slot]
                shift = (i - row % lanes + lanes) % lanes
                return jnp.where(lane == i, pltpu.roll(column, shift, 1), acc)

            acc = lax.fori_loop(0, lanes, slot_body, jnp.zeros((width, lanes), jnp.float32), unroll=8)
            out_ref[:, pl.ds(pl.multiple_of(c * lanes, lanes), lanes)] = acc
            return carry

        lax.fori_loop(0, chunk // lanes, tile_body, 0)

    return pl.pallas_call(
        kernel,
        out_shape=jax.ShapeDtypeStruct((width, slots), table.dtype),
        grid=(steps,),
        in_specs=[
            pl.BlockSpec((1, 1, chunk), lambda s: (s, 0, 0), memory_space=pltpu.SMEM),
            pl.BlockSpec((1, 1, chunk), lambda s: (s, 0, 0), memory_space=pltpu.SMEM),
            pl.BlockSpec((width, length), lambda s: (0, 0)),
        ],
        out_specs=pl.BlockSpec((width, chunk), lambda s: (0, s)),
        compiler_params=pltpu.CompilerParams(vmem_limit_bytes=48 * 1024 * 1024),
        interpret=interpret,
    )(rows, keep, table)


def per_device(parcel_load, parcel_offset, parcel_cell, cross_rows, block_brick, gas):
    span_x = gas.shape[1]
    span_y = gas.shape[2]
    span_z = gas.shape[3]
    count_x = span_x // 4
    count_y = span_y // 4
    count_z = span_z // 4
    brick_total = count_x * count_y * count_z
    resident = parcel_load.shape[1]
    block_count = block_brick.shape[0]
    brick_numbers = jnp.arange(brick_total, dtype=jnp.int32)
    attributes = jnp.concatenate(
        [parcel_load, parcel_offset, parcel_cell[None].astype(jnp.float32)], 0
    )
    upward = gather_columns(attributes, cross_rows[0])
    from_lower = passed_along(upward, "axial", 1)
    downward = gather_columns(attributes, cross_rows[1])
    from_upper = passed_along(downward, "axial", -1)
    departed = departed_mask(cross_rows, resident)
    staying = jnp.concatenate([attributes[:8] * (1.0 - departed)[None], attributes[8:]], 0)
    staying_blocks = resident // 128
    selector = (block_brick[:, None] == brick_numbers[None, :]).astype(jnp.float32)

    def deposit_part(part_rows, part_selector):
        part_blocks = part_rows.shape[1] // 128
        part_rows = part_rows.reshape(9, part_blocks, 128)
        factor_x, factor_y, factor_z = axis_factors(part_rows[8].astype(jnp.int32), part_rows[5:8])
        load_x = (part_rows[:5][:, None] * factor_x[None]).reshape(25, part_blocks, 128)
        weight_yz = (factor_y[:, None] * factor_z[None]).reshape(25, part_blocks, 128)
        spread = jnp.einsum("agp,bgp->gab", load_x, weight_yz, precision=lax.Precision.HIGH)
        part_sums = jnp.einsum(
            "gb,gfe->feb", part_selector, spread.reshape(part_blocks, 5, 125),
            precision=lax.Precision.HIGH,
        )
        return part_sums, factor_x, weight_yz

    stay_sums, stay_x, stay_yz = deposit_part(staying, selector[:staying_blocks])
    from_lower, from_upper, stay_sums = lax.optimization_barrier((from_lower, from_upper, stay_sums))
    moved = jnp.concatenate([from_lower, from_upper], 1)
    moved_sums, moved_x, moved_yz = deposit_part(moved, selector[staying_blocks:])
    brick_sums = stay_sums + moved_sums
    factor_x = jnp.concatenate([stay_x, moved_x], 1)
    weight_yz = jnp.concatenate([stay_yz, moved_yz], 1)
    if count_x == 1:
        laid = brick_sums.reshape(5, 25, 5, count_y, count_z)
        laid = jnp.einsum(
            "faeyk,ekz->fayz", laid, window_map(count_z, span_z), precision=lax.Precision.HIGH
        )
        laid = laid.reshape(5, 5, 5, count_y, span_z)
        deposit_grid = jnp.einsum(
            "fxwyz,wyn->fxnz", laid, window_map(count_y, span_y + 1),
            precision=lax.Precision.HIGH,
        )
    else:
        laid = jnp.transpose(brick_sums, (0, 2, 1))
        laid = laid.reshape(5, count_x, count_y, count_z, 5, 5, 5)
        laid = jnp.transpose(laid, (0, 1, 4, 2, 5, 3, 6))
        laid = merge_windows(laid, 1, count_x, True)
        laid = merge_windows(laid, 2, count_y, True)
        deposit_grid = merge_windows(laid, 3, count_z, False)
    incoming = passed_along(deposit_grid[:, span_x], "axial", 1)
    summed = deposit_grid[:, :span_x].at[:, 0].add(incoming)
    folded = radial_fold(summed)
    source = folded[:, :, :span_y]
    updated_gas = gas + COUPLE * source
    upper_face = passed_along(updated_gas[:, 0], "axial", -1)
    if count_x == 1:
        below_inner = passed_along(updated_gas[:, :, 0], "radial", -1)
        field_inner = jnp.concatenate([updated_gas, below_inner[:, :, None]], 2)
        below_face = passed_along(upper_face[:, 0], "radial", -1)
        field_face = jnp.concatenate([upper_face, below_face[:, None]], 1)[:, None]

        def window_part(field):
            layers = field.shape[1]
            part = jnp.einsum(
                "fxnz,wyn->fxwyz", field, window_map(count_y, span_y + 1),
                precision=lax.Precision.HIGH,
            )
            part = part.reshape(5, layers * 5, count_y, span_z)
            part = jnp.einsum(
                "fayz,ekz->faeyk", part, window_map(count_z, span_z),
                precision=lax.Precision.HIGH,
            )
            part = part.reshape(5, layers * 25, brick_total)
            return jnp.einsum("gb,feb->gfe", selector, part, precision=lax.Precision.HIGH)

        picked = jnp.concatenate([window_part(field_inner), window_part(field_face)], 2)
    else:
        extended = jnp.concatenate([updated_gas, upper_face[:, None]], 1)
        below_row = passed_along(extended[:, :, 0], "radial", -1)
        gas_field = jnp.concatenate([extended, below_row[:, :, None]], 2)
        gas_field = jnp.pad(gas_field, ((0, 0), (0, 0), (0, 0), (0, 1)))
        windows = split_windows(gas_field, 3, count_z)
        windows = split_windows(windows, 2, count_y)
        windows = split_windows(windows, 1, count_x)
        windows = jnp.transpose(windows, (0, 1, 3, 5, 2, 4, 6)).reshape(5, brick_total, 125)
        picked = jnp.einsum("gb,fbe->gfe", selector, windows, precision=lax.Precision.HIGH)
    picked = picked.reshape(block_count, 25, 25)
    partial = jnp.einsum("gab,bgp->agp", picked, weight_yz, precision=lax.Precision.HIGH)
    values = jnp.sum(partial.reshape(5, 5, block_count, 128) * factor_x[None], axis=1)
    parcel_gas = values.reshape(5, block_count * 128).astype(jnp.bfloat16)
    return (source, parcel_gas)


def solution(mesh):
    return jax.shard_map(
        per_device,
        mesh=mesh,
        in_specs=(
            P(None, ("axial", "radial")),
            P(None, ("axial", "radial")),
            P(("axial", "radial")),
            P(None, ("axial", "radial")),
            P(("axial", "radial")),
            P(None, "axial", "radial", None),
        ),
        out_specs=(P(None, "axial", "radial", None), P(None, ("axial", "radial"))),
        check_vma=False,
    )
```

```python
import math

import jax
import jax.numpy as jnp
from jax import lax
from jax.experimental import pallas as pl
from jax.experimental.pallas import tpu as pltpu
from jax.sharding import PartitionSpec as P

COUPLE = 0.5


def passed_along(block, axis, distance):
    devices = range(lax.axis_size(axis))
    route = [(i - distance, i) for i in devices if i - distance in devices]
    return lax.ppermute(block, axis, route)


def kernel_weights(cell_index, offsets):
    extent = jnp.arange(128, dtype=jnp.int32)
    brick_x = extent // 25
    brick_y = extent // 5 % 5
    brick_z = extent % 5
    inside = (extent < 125).astype(jnp.float32)

    def factor(cell_coord, brick_coord, fraction):
        cell_coord = cell_coord[:, :, None]
        fraction = fraction[:, :, None]
        return jnp.where(
            brick_coord == cell_coord,
            1.0 - fraction,
            jnp.where(brick_coord == cell_coord + 1, fraction, 0.0),
        )

    cell_x = cell_index // 16
    cell_y = cell_index // 4 % 4
    cell_z = cell_index % 4
    return (
        factor(cell_x, brick_x, offsets[0])
        * factor(cell_y, brick_y, offsets[1])
        * factor(cell_z, brick_z, offsets[2])
        * inside
    )


def axis_factors(cell_index, offsets):
    extent = jnp.arange(5, dtype=jnp.int32).reshape((5,) + (1,) * cell_index.ndim)

    def factor(cell_coord, fraction):
        return jnp.where(
            extent == cell_coord[None],
            1.0 - fraction[None],
            jnp.where(extent == cell_coord[None] + 1, fraction[None], 0.0),
        )

    return (
        factor(cell_index // 16, offsets[0]),
        factor(cell_index // 4 % 4, offsets[1]),
        factor(cell_index % 4, offsets[2]),
    )


def split_windows(field, axis, count):
    core = lax.slice_in_dim(field, 0, 4 * count, axis=axis)
    core = core.reshape(field.shape[:axis] + (count, 4) + field.shape[axis + 1 :])
    tail = lax.slice_in_dim(field, 4, 4 * count + 1, stride=4, axis=axis)
    tail = jnp.expand_dims(tail, axis + 1)
    return jnp.concatenate([core, tail], axis + 1)


def merge_windows(field, axis, count, keep_tail):
    core = lax.slice_in_dim(field, 0, 4, axis=axis + 1)
    tail = lax.slice_in_dim(field, 4, 5, axis=axis + 1)
    zero_brick = jnp.zeros_like(lax.slice_in_dim(core, 0, 1, axis=axis))
    core = jnp.concatenate([core, zero_brick], axis)
    zero_tail = jnp.zeros_like(lax.slice_in_dim(tail, 0, 1, axis=axis))
    tail = jnp.concatenate([zero_tail, tail], axis)
    first = lax.slice_in_dim(core, 0, 1, axis=axis + 1) + tail
    rest = lax.slice_in_dim(core, 1, 4, axis=axis + 1)
    joined = jnp.concatenate([first, rest], axis + 1)
    joined = joined.reshape(field.shape[:axis] + (4 * (count + 1),) + field.shape[axis + 2 :])
    length = 4 * count + 1 if keep_tail else 4 * count
    return lax.slice_in_dim(joined, 0, length, axis=axis)


def window_map(count, length):
    extent = jnp.arange(5, dtype=jnp.int32)[:, None, None]
    brick = jnp.arange(count, dtype=jnp.int32)[None, :, None]
    cell = jnp.arange(length, dtype=jnp.int32)[None, None, :]
    return (4 * brick + extent == cell).astype(jnp.float32)


def radial_fold(layers):
    arrived = passed_along(layers[:, :, -1], "radial", 1)
    return layers.at[:, :, 0].add(arrived)


def departed_mask(cross_rows, resident):
    rows = cross_rows.reshape(-1)
    lanes = 128
    high = jnp.where(rows >= 0, rows // lanes, -1)
    low = jnp.where(rows >= 0, rows % lanes, -1)
    high_hot = (high[:, None] == jnp.arange(resident // lanes, dtype=jnp.int32)[None, :]).astype(jnp.bfloat16)
    low_hot = (low[:, None] == jnp.arange(lanes, dtype=jnp.int32)[None, :]).astype(jnp.bfloat16)
    counts = jnp.einsum("sh,sl->hl", high_hot, low_hot, preferred_element_type=jnp.float32)
    return counts.reshape(resident)


def gather_rows(table, rows, interpret=False):
    slots = rows.shape[0]
    height, width = table.shape
    chunk = math.gcd(slots, 4096)
    steps = slots // chunk
    rows = jnp.clip(rows, 0, height - 1).reshape(steps, 1, chunk)

    def kernel(row_ref, table_ref, out_ref):
        def body(i, carry):
            row = row_ref[0, 0, i]
            out_ref[pl.ds(i, 1), :] = table_ref[pl.ds(row, 1), :]
            return carry

        lax.fori_loop(0, chunk, body, 0, unroll=16)

    return pl.pallas_call(
        kernel,
        out_shape=jax.ShapeDtypeStruct((slots, width), table.dtype),
        grid=(steps,),
        in_specs=[
            pl.BlockSpec((1, 1, chunk), lambda s: (s, 0, 0), memory_space=pltpu.SMEM),
            pl.BlockSpec((height, width), lambda s: (0, 0)),
        ],
        out_specs=pl.BlockSpec((chunk, width), lambda s: (s, 0)),
        compiler_params=pltpu.CompilerParams(vmem_limit_bytes=48 * 1024 * 1024),
        interpret=interpret,
    )(rows, table)


def per_device(parcel_load, parcel_offset, parcel_cell, cross_rows, block_brick, gas):
    span_x = gas.shape[1]
    span_y = gas.shape[2]
    span_z = gas.shape[3]
    count_x = span_x // 4
    count_y = span_y // 4
    count_z = span_z // 4
    brick_total = count_x * count_y * count_z
    resident = parcel_load.shape[1]
    block_count = block_brick.shape[0]
    brick_numbers = jnp.arange(brick_total, dtype=jnp.int32)
    attributes = jnp.concatenate(
        [parcel_load, parcel_offset, parcel_cell[None].astype(jnp.float32)], 0
    )
    usable = cross_rows >= 0
    safe_rows = jnp.maximum(cross_rows, 0)
    table = attributes.T
    flip = jnp.eye(table.shape[1], dtype=jnp.float32)

    def moving(side):
        picked = gather_rows(table, safe_rows[side])
        picked = jnp.einsum("fc,sc->fs", flip, picked, precision=lax.Precision.HIGHEST)
        return picked * usable[side].astype(jnp.float32)

    upward = moving(0)
    from_lower = passed_along(upward, "axial", 1)
    downward = moving(1)
    from_upper = passed_along(downward, "axial", -1)
    departed = departed_mask(cross_rows, resident)
    staying = jnp.concatenate([attributes[:8] * (1.0 - departed)[None], attributes[8:]], 0)
    staying_blocks = resident // 128
    selector = (block_brick[:, None] == brick_numbers[None, :]).astype(jnp.float32)

    def deposit_part(part_rows, part_selector):
        part_blocks = part_rows.shape[1] // 128
        part_rows = part_rows.reshape(9, part_blocks, 128)
        factor_x, factor_y, factor_z = axis_factors(part_rows[8].astype(jnp.int32), part_rows[5:8])
        load_x = (part_rows[:5][:, None] * factor_x[None]).reshape(25, part_blocks, 128)
        weight_yz = (factor_y[:, None] * factor_z[None]).reshape(25, part_blocks, 128)
        spread = jnp.einsum("agp,bgp->gab", load_x, weight_yz, precision=lax.Precision.HIGH)
        part_sums = jnp.einsum(
            "gb,gfe->feb", part_selector, spread.reshape(part_blocks, 5, 125),
            precision=lax.Precision.HIGH,
        )
        return part_sums, factor_x, weight_yz

    stay_sums, stay_x, stay_yz = deposit_part(staying, selector[:staying_blocks])
    from_lower, from_upper, stay_sums = lax.optimization_barrier((from_lower, from_upper, stay_sums))
    moved = jnp.concatenate([from_lower, from_upper], 1)
    moved_sums, moved_x, moved_yz = deposit_part(moved, selector[staying_blocks:])
    brick_sums = stay_sums + moved_sums
    factor_x = jnp.concatenate([stay_x, moved_x], 1)
    weight_yz = jnp.concatenate([stay_yz, moved_yz], 1)
    if count_x == 1:
        laid = brick_sums.reshape(5, 25, 5, count_y, count_z)
        laid = jnp.einsum(
            "faeyk,ekz->fayz", laid, window_map(count_z, span_z), precision=lax.Precision.HIGH
        )
        laid = laid.reshape(5, 5, 5, count_y, span_z)
        deposit_grid = jnp.einsum(
            "fxwyz,wyn->fxnz", laid, window_map(count_y, span_y + 1),
            precision=lax.Precision.HIGH,
        )
    else:
        laid = jnp.transpose(brick_sums, (0, 2, 1))
        laid = laid.reshape(5, count_x, count_y, count_z, 5, 5, 5)
        laid = jnp.transpose(laid, (0, 1, 4, 2, 5, 3, 6))
        laid = merge_windows(laid, 1, count_x, True)
        laid = merge_windows(laid, 2, count_y, True)
        deposit_grid = merge_windows(laid, 3, count_z, False)
    incoming = passed_along(deposit_grid[:, span_x], "axial", 1)
    summed = deposit_grid[:, :span_x].at[:, 0].add(incoming)
    folded = radial_fold(summed)
    source = folded[:, :, :span_y]
    updated_gas = gas + COUPLE * source
    upper_face = passed_along(updated_gas[:, 0], "axial", -1)
    if count_x == 1:
        below_inner = passed_along(updated_gas[:, :, 0], "radial", -1)
        field_inner = jnp.concatenate([updated_gas, below_inner[:, :, None]], 2)
        below_face = passed_along(upper_face[:, 0], "radial", -1)
        field_face = jnp.concatenate([upper_face, below_face[:, None]], 1)[:, None]

        def window_part(field):
            layers = field.shape[1]
            part = jnp.einsum(
                "fxnz,wyn->fxwyz", field, window_map(count_y, span_y + 1),
                precision=lax.Precision.HIGH,
            )
            part = part.reshape(5, layers * 5, count_y, span_z)
            part = jnp.einsum(
                "fayz,ekz->faeyk", part, window_map(count_z, span_z),
                precision=lax.Precision.HIGH,
            )
            part = part.reshape(5, layers * 25, brick_total)
            return jnp.einsum("gb,feb->gfe", selector, part, precision=lax.Precision.HIGH)

        picked = jnp.concatenate([window_part(field_inner), window_part(field_face)], 2)
    else:
        extended = jnp.concatenate([updated_gas, upper_face[:, None]], 1)
        below_row = passed_along(extended[:, :, 0], "radial", -1)
        gas_field = jnp.concatenate([extended, below_row[:, :, None]], 2)
        gas_field = jnp.pad(gas_field, ((0, 0), (0, 0), (0, 0), (0, 1)))
        windows = split_windows(gas_field, 3, count_z)
        windows = split_windows(windows, 2, count_y)
        windows = split_windows(windows, 1, count_x)
        windows = jnp.transpose(windows, (0, 1, 3, 5, 2, 4, 6)).reshape(5, brick_total, 125)
        picked = jnp.einsum("gb,fbe->gfe", selector, windows, precision=lax.Precision.HIGH)
    picked = picked.reshape(block_count, 25, 25)
    partial = jnp.einsum("gab,bgp->agp", picked, weight_yz, precision=lax.Precision.HIGH)
    values = jnp.sum(partial.reshape(5, 5, block_count, 128) * factor_x[None], axis=1)
    parcel_gas = values.reshape(5, block_count * 128).astype(jnp.bfloat16)
    return (source, parcel_gas)


def solution(mesh):
    return jax.shard_map(
        per_device,
        mesh=mesh,
        in_specs=(
            P(None, ("axial", "radial")),
            P(None, ("axial", "radial")),
            P(("axial", "radial")),
            P(None, ("axial", "radial")),
            P(("axial", "radial")),
            P(None, "axial", "radial", None),
        ),
        out_specs=(P(None, "axial", "radial", None), P(None, ("axial", "radial"))),
        check_vma=False,
    )
```

```python
import math

import jax
import jax.numpy as jnp
from jax import lax
from jax.experimental import pallas as pl
from jax.experimental.pallas import tpu as pltpu
from jax.sharding import PartitionSpec as P

COUPLE = 0.5


def passed_along(block, axis, distance):
    devices = range(lax.axis_size(axis))
    route = [(i - distance, i) for i in devices if i - distance in devices]
    return lax.ppermute(block, axis, route)


def kernel_weights(cell_index, offsets):
    extent = jnp.arange(128, dtype=jnp.int32)
    brick_x = extent // 25
    brick_y = extent // 5 % 5
    brick_z = extent % 5
    inside = (extent < 125).astype(jnp.float32)

    def factor(cell_coord, brick_coord, fraction):
        cell_coord = cell_coord[:, :, None]
        fraction = fraction[:, :, None]
        return jnp.where(
            brick_coord == cell_coord,
            1.0 - fraction,
            jnp.where(brick_coord == cell_coord + 1, fraction, 0.0),
        )

    cell_x = cell_index // 16
    cell_y = cell_index // 4 % 4
    cell_z = cell_index % 4
    return (
        factor(cell_x, brick_x, offsets[0])
        * factor(cell_y, brick_y, offsets[1])
        * factor(cell_z, brick_z, offsets[2])
        * inside
    )


def axis_factors(cell_index, offsets):
    extent = jnp.arange(5, dtype=jnp.int32).reshape((5,) + (1,) * cell_index.ndim)

    def factor(cell_coord, fraction):
        return jnp.where(
            extent == cell_coord[None],
            1.0 - fraction[None],
            jnp.where(extent == cell_coord[None] + 1, fraction[None], 0.0),
        )

    return (
        factor(cell_index // 16, offsets[0]),
        factor(cell_index // 4 % 4, offsets[1]),
        factor(cell_index % 4, offsets[2]),
    )


def split_windows(field, axis, count):
    core = lax.slice_in_dim(field, 0, 4 * count, axis=axis)
    core = core.reshape(field.shape[:axis] + (count, 4) + field.shape[axis + 1 :])
    tail = lax.slice_in_dim(field, 4, 4 * count + 1, stride=4, axis=axis)
    tail = jnp.expand_dims(tail, axis + 1)
    return jnp.concatenate([core, tail], axis + 1)


def merge_windows(field, axis, count, keep_tail):
    core = lax.slice_in_dim(field, 0, 4, axis=axis + 1)
    tail = lax.slice_in_dim(field, 4, 5, axis=axis + 1)
    zero_brick = jnp.zeros_like(lax.slice_in_dim(core, 0, 1, axis=axis))
    core = jnp.concatenate([core, zero_brick], axis)
    zero_tail = jnp.zeros_like(lax.slice_in_dim(tail, 0, 1, axis=axis))
    tail = jnp.concatenate([zero_tail, tail], axis)
    first = lax.slice_in_dim(core, 0, 1, axis=axis + 1) + tail
    rest = lax.slice_in_dim(core, 1, 4, axis=axis + 1)
    joined = jnp.concatenate([first, rest], axis + 1)
    joined = joined.reshape(field.shape[:axis] + (4 * (count + 1),) + field.shape[axis + 2 :])
    length = 4 * count + 1 if keep_tail else 4 * count
    return lax.slice_in_dim(joined, 0, length, axis=axis)


def window_map(count, length):
    extent = jnp.arange(5, dtype=jnp.int32)[:, None, None]
    brick = jnp.arange(count, dtype=jnp.int32)[None, :, None]
    cell = jnp.arange(length, dtype=jnp.int32)[None, None, :]
    return (4 * brick + extent == cell).astype(jnp.float32)


def radial_fold(layers):
    arrived = passed_along(layers[:, :, -1], "radial", 1)
    return layers.at[:, :, 0].add(arrived)


def departed_mask(cross_rows, resident):
    rows = cross_rows.reshape(-1)
    lanes = 128
    high = jnp.where(rows >= 0, rows // lanes, -1)
    low = jnp.where(rows >= 0, rows % lanes, -1)
    high_hot = (high[:, None] == jnp.arange(resident // lanes, dtype=jnp.int32)[None, :]).astype(jnp.bfloat16)
    low_hot = (low[:, None] == jnp.arange(lanes, dtype=jnp.int32)[None, :]).astype(jnp.bfloat16)
    counts = jnp.einsum("sh,sl->hl", high_hot, low_hot, preferred_element_type=jnp.float32)
    return counts.reshape(resident)


def gather_rows(table, rows, interpret=False):
    slots = rows.shape[0]
    height, width = table.shape
    chunk = math.gcd(slots, 4096)
    steps = slots // chunk
    rows = jnp.clip(rows, 0, height - 1).reshape(steps, 1, chunk)

    def kernel(row_ref, table_ref, out_ref):
        def body(i, carry):
            row = row_ref[0, 0, i]
            out_ref[pl.ds(i, 1), :] = table_ref[pl.ds(row, 1), :]
            return carry

        lax.fori_loop(0, chunk, body, 0, unroll=16)

    return pl.pallas_call(
        kernel,
        out_shape=jax.ShapeDtypeStruct((slots, width), table.dtype),
        grid=(steps,),
        in_specs=[
            pl.BlockSpec((1, 1, chunk), lambda s: (s, 0, 0), memory_space=pltpu.SMEM),
            pl.BlockSpec((height, width), lambda s: (0, 0)),
        ],
        out_specs=pl.BlockSpec((chunk, width), lambda s: (s, 0)),
        compiler_params=pltpu.CompilerParams(vmem_limit_bytes=48 * 1024 * 1024),
        interpret=interpret,
    )(rows, table)


def per_device(parcel_load, parcel_offset, parcel_cell, cross_rows, block_brick, gas):
    span_x = gas.shape[1]
    span_y = gas.shape[2]
    span_z = gas.shape[3]
    count_x = span_x // 4
    count_y = span_y // 4
    count_z = span_z // 4
    brick_total = count_x * count_y * count_z
    resident = parcel_load.shape[1]
    block_count = block_brick.shape[0]
    brick_numbers = jnp.arange(brick_total, dtype=jnp.int32)
    attributes = jnp.concatenate(
        [parcel_load, parcel_offset, parcel_cell[None].astype(jnp.float32)], 0
    )
    usable = cross_rows >= 0
    safe_rows = jnp.maximum(cross_rows, 0)
    flip = jnp.eye(attributes.shape[0], dtype=jnp.float32)
    table = jnp.einsum("cr,cf->rf", attributes, flip, precision=lax.Precision.HIGHEST)

    def moving(side):
        picked = gather_rows(table, safe_rows[side])
        picked = jnp.einsum("fc,sc->fs", flip, picked, precision=lax.Precision.HIGHEST)
        return picked * usable[side].astype(jnp.float32)

    upward = moving(0)
    from_lower = passed_along(upward, "axial", 1)
    downward = moving(1)
    from_upper = passed_along(downward, "axial", -1)
    departed = departed_mask(cross_rows, resident)
    staying = jnp.concatenate([attributes[:8] * (1.0 - departed)[None], attributes[8:]], 0)
    staying_blocks = resident // 128
    selector = (block_brick[:, None] == brick_numbers[None, :]).astype(jnp.float32)

    def deposit_part(part_rows, part_selector):
        part_blocks = part_rows.shape[1] // 128
        part_rows = part_rows.reshape(9, part_blocks, 128)
        factor_x, factor_y, factor_z = axis_factors(part_rows[8].astype(jnp.int32), part_rows[5:8])
        load_x = (part_rows[:5][:, None] * factor_x[None]).reshape(25, part_blocks, 128)
        weight_yz = (factor_y[:, None] * factor_z[None]).reshape(25, part_blocks, 128)
        spread = jnp.einsum("agp,bgp->gab", load_x, weight_yz, precision=lax.Precision.HIGH)
        part_sums = jnp.einsum(
            "gb,gfe->feb", part_selector, spread.reshape(part_blocks, 5, 125),
            precision=lax.Precision.HIGH,
        )
        return part_sums, factor_x, weight_yz

    stay_sums, stay_x, stay_yz = deposit_part(staying, selector[:staying_blocks])
    from_lower, from_upper, stay_sums = lax.optimization_barrier((from_lower, from_upper, stay_sums))
    moved = jnp.concatenate([from_lower, from_upper], 1)
    moved_sums, moved_x, moved_yz = deposit_part(moved, selector[staying_blocks:])
    brick_sums = stay_sums + moved_sums
    factor_x = jnp.concatenate([stay_x, moved_x], 1)
    weight_yz = jnp.concatenate([stay_yz, moved_yz], 1)
    if count_x == 1:
        laid = brick_sums.reshape(5, 25, 5, count_y, count_z)
        laid = jnp.einsum(
            "faeyk,ekz->fayz", laid, window_map(count_z, span_z), precision=lax.Precision.HIGH
        )
        laid = laid.reshape(5, 5, 5, count_y, span_z)
        deposit_grid = jnp.einsum(
            "fxwyz,wyn->fxnz", laid, window_map(count_y, span_y + 1),
            precision=lax.Precision.HIGH,
        )
    else:
        laid = jnp.transpose(brick_sums, (0, 2, 1))
        laid = laid.reshape(5, count_x, count_y, count_z, 5, 5, 5)
        laid = jnp.transpose(laid, (0, 1, 4, 2, 5, 3, 6))
        laid = merge_windows(laid, 1, count_x, True)
        laid = merge_windows(laid, 2, count_y, True)
        deposit_grid = merge_windows(laid, 3, count_z, False)
    incoming = passed_along(deposit_grid[:, span_x], "axial", 1)
    summed = deposit_grid[:, :span_x].at[:, 0].add(incoming)
    folded = radial_fold(summed)
    source = folded[:, :, :span_y]
    updated_gas = gas + COUPLE * source
    upper_face = passed_along(updated_gas[:, 0], "axial", -1)
    if count_x == 1:
        below_inner = passed_along(updated_gas[:, :, 0], "radial", -1)
        field_inner = jnp.concatenate([updated_gas, below_inner[:, :, None]], 2)
        below_face = passed_along(upper_face[:, 0], "radial", -1)
        field_face = jnp.concatenate([upper_face, below_face[:, None]], 1)[:, None]

        def window_part(field):
            layers = field.shape[1]
            part = jnp.einsum(
                "fxnz,wyn->fxwyz", field, window_map(count_y, span_y + 1),
                precision=lax.Precision.HIGH,
            )
            part = part.reshape(5, layers * 5, count_y, span_z)
            part = jnp.einsum(
                "fayz,ekz->faeyk", part, window_map(count_z, span_z),
                precision=lax.Precision.HIGH,
            )
            part = part.reshape(5, layers * 25, brick_total)
            return jnp.einsum("gb,feb->gfe", selector, part, precision=lax.Precision.HIGH)

        picked = jnp.concatenate([window_part(field_inner), window_part(field_face)], 2)
    else:
        extended = jnp.concatenate([updated_gas, upper_face[:, None]], 1)
        below_row = passed_along(extended[:, :, 0], "radial", -1)
        gas_field = jnp.concatenate([extended, below_row[:, :, None]], 2)
        gas_field = jnp.pad(gas_field, ((0, 0), (0, 0), (0, 0), (0, 1)))
        windows = split_windows(gas_field, 3, count_z)
        windows = split_windows(windows, 2, count_y)
        windows = split_windows(windows, 1, count_x)
        windows = jnp.transpose(windows, (0, 1, 3, 5, 2, 4, 6)).reshape(5, brick_total, 125)
        picked = jnp.einsum("gb,fbe->gfe", selector, windows, precision=lax.Precision.HIGH)
    picked = picked.reshape(block_count, 25, 25)
    partial = jnp.einsum("gab,bgp->agp", picked, weight_yz, precision=lax.Precision.HIGH)
    values = jnp.sum(partial.reshape(5, 5, block_count, 128) * factor_x[None], axis=1)
    parcel_gas = values.reshape(5, block_count * 128).astype(jnp.bfloat16)
    return (source, parcel_gas)


def solution(mesh):
    return jax.shard_map(
        per_device,
        mesh=mesh,
        in_specs=(
            P(None, ("axial", "radial")),
            P(None, ("axial", "radial")),
            P(("axial", "radial")),
            P(None, ("axial", "radial")),
            P(("axial", "radial")),
            P(None, "axial", "radial", None),
        ),
        out_specs=(P(None, "axial", "radial", None), P(None, ("axial", "radial"))),
        check_vma=False,
    )
```

```python
import math

import jax
import jax.numpy as jnp
from jax import lax
from jax.experimental import pallas as pl
from jax.experimental.pallas import tpu as pltpu
from jax.sharding import PartitionSpec as P

COUPLE = 0.5


def passed_along(block, axis, distance):
    devices = range(lax.axis_size(axis))
    route = [(i - distance, i) for i in devices if i - distance in devices]
    return lax.ppermute(block, axis, route)


def kernel_weights(cell_index, offsets):
    extent = jnp.arange(128, dtype=jnp.int32)
    brick_x = extent // 25
    brick_y = extent // 5 % 5
    brick_z = extent % 5
    inside = (extent < 125).astype(jnp.float32)

    def factor(cell_coord, brick_coord, fraction):
        cell_coord = cell_coord[:, :, None]
        fraction = fraction[:, :, None]
        return jnp.where(
            brick_coord == cell_coord,
            1.0 - fraction,
            jnp.where(brick_coord == cell_coord + 1, fraction, 0.0),
        )

    cell_x = cell_index // 16
    cell_y = cell_index // 4 % 4
    cell_z = cell_index % 4
    return (
        factor(cell_x, brick_x, offsets[0])
        * factor(cell_y, brick_y, offsets[1])
        * factor(cell_z, brick_z, offsets[2])
        * inside
    )


def axis_factors(cell_index, offsets):
    extent = jnp.arange(5, dtype=jnp.int32).reshape((5,) + (1,) * cell_index.ndim)

    def factor(cell_coord, fraction):
        return jnp.where(
            extent == cell_coord[None],
            1.0 - fraction[None],
            jnp.where(extent == cell_coord[None] + 1, fraction[None], 0.0),
        )

    return (
        factor(cell_index // 16, offsets[0]),
        factor(cell_index // 4 % 4, offsets[1]),
        factor(cell_index % 4, offsets[2]),
    )


def split_windows(field, axis, count):
    core = lax.slice_in_dim(field, 0, 4 * count, axis=axis)
    core = core.reshape(field.shape[:axis] + (count, 4) + field.shape[axis + 1 :])
    tail = lax.slice_in_dim(field, 4, 4 * count + 1, stride=4, axis=axis)
    tail = jnp.expand_dims(tail, axis + 1)
    return jnp.concatenate([core, tail], axis + 1)


def merge_windows(field, axis, count, keep_tail):
    core = lax.slice_in_dim(field, 0, 4, axis=axis + 1)
    tail = lax.slice_in_dim(field, 4, 5, axis=axis + 1)
    zero_brick = jnp.zeros_like(lax.slice_in_dim(core, 0, 1, axis=axis))
    core = jnp.concatenate([core, zero_brick], axis)
    zero_tail = jnp.zeros_like(lax.slice_in_dim(tail, 0, 1, axis=axis))
    tail = jnp.concatenate([zero_tail, tail], axis)
    first = lax.slice_in_dim(core, 0, 1, axis=axis + 1) + tail
    rest = lax.slice_in_dim(core, 1, 4, axis=axis + 1)
    joined = jnp.concatenate([first, rest], axis + 1)
    joined = joined.reshape(field.shape[:axis] + (4 * (count + 1),) + field.shape[axis + 2 :])
    length = 4 * count + 1 if keep_tail else 4 * count
    return lax.slice_in_dim(joined, 0, length, axis=axis)


def window_map(count, length):
    extent = jnp.arange(5, dtype=jnp.int32)[:, None, None]
    brick = jnp.arange(count, dtype=jnp.int32)[None, :, None]
    cell = jnp.arange(length, dtype=jnp.int32)[None, None, :]
    return (4 * brick + extent == cell).astype(jnp.float32)


def radial_fold(layers):
    arrived = passed_along(layers[:, :, -1], "radial", 1)
    return layers.at[:, :, 0].add(arrived)


def departed_mask(cross_rows, resident):
    rows = cross_rows.reshape(-1)
    lanes = 128
    high = jnp.where(rows >= 0, rows // lanes, -1)
    low = jnp.where(rows >= 0, rows % lanes, -1)
    high_hot = (high[:, None] == jnp.arange(resident // lanes, dtype=jnp.int32)[None, :]).astype(jnp.bfloat16)
    low_hot = (low[:, None] == jnp.arange(lanes, dtype=jnp.int32)[None, :]).astype(jnp.bfloat16)
    counts = jnp.einsum("sh,sl->hl", high_hot, low_hot, preferred_element_type=jnp.float32)
    return counts.reshape(resident)


def gather_rows(table, rows, interpret=False):
    slots = rows.shape[0]
    height, width = table.shape
    chunk = math.gcd(slots, 4096)
    steps = slots // chunk
    rows = jnp.clip(rows, 0, height - 1).reshape(steps, 1, chunk)

    def kernel(row_ref, table_ref, out_ref):
        def body(i, carry):
            row = row_ref[0, 0, i]
            out_ref[pl.ds(i, 1), :] = table_ref[pl.ds(row, 1), :]
            return carry

        lax.fori_loop(0, chunk, body, 0, unroll=64)

    return pl.pallas_call(
        kernel,
        out_shape=jax.ShapeDtypeStruct((slots, width), table.dtype),
        grid=(steps,),
        in_specs=[
            pl.BlockSpec((1, 1, chunk), lambda s: (s, 0, 0), memory_space=pltpu.SMEM),
            pl.BlockSpec((height, width), lambda s: (0, 0)),
        ],
        out_specs=pl.BlockSpec((chunk, width), lambda s: (s, 0)),
        compiler_params=pltpu.CompilerParams(vmem_limit_bytes=48 * 1024 * 1024),
        interpret=interpret,
    )(rows, table)


def per_device(parcel_load, parcel_offset, parcel_cell, cross_rows, block_brick, gas):
    span_x = gas.shape[1]
    span_y = gas.shape[2]
    span_z = gas.shape[3]
    count_x = span_x // 4
    count_y = span_y // 4
    count_z = span_z // 4
    brick_total = count_x * count_y * count_z
    resident = parcel_load.shape[1]
    block_count = block_brick.shape[0]
    brick_numbers = jnp.arange(brick_total, dtype=jnp.int32)
    attributes = jnp.concatenate(
        [parcel_load, parcel_offset, parcel_cell[None].astype(jnp.float32)], 0
    )
    usable = cross_rows >= 0
    safe_rows = jnp.maximum(cross_rows, 0)
    table = attributes.T
    flip = jnp.eye(table.shape[1], dtype=jnp.float32)

    def moving(side):
        picked = gather_rows(table, safe_rows[side])
        picked = jnp.einsum("fc,sc->fs", flip, picked, precision=lax.Precision.HIGHEST)
        return picked * usable[side].astype(jnp.float32)

    upward = moving(0)
    from_lower = passed_along(upward, "axial", 1)
    downward = moving(1)
    from_upper = passed_along(downward, "axial", -1)
    departed = departed_mask(cross_rows, resident)
    staying = jnp.concatenate([attributes[:8] * (1.0 - departed)[None], attributes[8:]], 0)
    staying_blocks = resident // 128
    selector = (block_brick[:, None] == brick_numbers[None, :]).astype(jnp.float32)

    def deposit_part(part_rows, part_selector):
        part_blocks = part_rows.shape[1] // 128
        part_rows = part_rows.reshape(9, part_blocks, 128)
        factor_x, factor_y, factor_z = axis_factors(part_rows[8].astype(jnp.int32), part_rows[5:8])
        load_x = (part_rows[:5][:, None] * factor_x[None]).reshape(25, part_blocks, 128)
        weight_yz = (factor_y[:, None] * factor_z[None]).reshape(25, part_blocks, 128)
        spread = jnp.einsum("agp,bgp->gab", load_x, weight_yz, precision=lax.Precision.HIGH)
        part_sums = jnp.einsum(
            "gb,gfe->feb", part_selector, spread.reshape(part_blocks, 5, 125),
            precision=lax.Precision.HIGH,
        )
        return part_sums, factor_x, weight_yz

    stay_sums, stay_x, stay_yz = deposit_part(staying, selector[:staying_blocks])
    from_lower, from_upper, stay_sums = lax.optimization_barrier((from_lower, from_upper, stay_sums))
    moved = jnp.concatenate([from_lower, from_upper], 1)
    moved_sums, moved_x, moved_yz = deposit_part(moved, selector[staying_blocks:])
    brick_sums = stay_sums + moved_sums
    factor_x = jnp.concatenate([stay_x, moved_x], 1)
    weight_yz = jnp.concatenate([stay_yz, moved_yz], 1)
    if count_x == 1:
        laid = brick_sums.reshape(5, 25, 5, count_y, count_z)
        laid = jnp.einsum(
            "faeyk,ekz->fayz", laid, window_map(count_z, span_z), precision=lax.Precision.HIGH
        )
        laid = laid.reshape(5, 5, 5, count_y, span_z)
        deposit_grid = jnp.einsum(
            "fxwyz,wyn->fxnz", laid, window_map(count_y, span_y + 1),
            precision=lax.Precision.HIGH,
        )
    else:
        laid = jnp.transpose(brick_sums, (0, 2, 1))
        laid = laid.reshape(5, count_x, count_y, count_z, 5, 5, 5)
        laid = jnp.transpose(laid, (0, 1, 4, 2, 5, 3, 6))
        laid = merge_windows(laid, 1, count_x, True)
        laid = merge_windows(laid, 2, count_y, True)
        deposit_grid = merge_windows(laid, 3, count_z, False)
    incoming = passed_along(deposit_grid[:, span_x], "axial", 1)
    summed = deposit_grid[:, :span_x].at[:, 0].add(incoming)
    folded = radial_fold(summed)
    source = folded[:, :, :span_y]
    updated_gas = gas + COUPLE * source
    upper_face = passed_along(updated_gas[:, 0], "axial", -1)
    if count_x == 1:
        below_inner = passed_along(updated_gas[:, :, 0], "radial", -1)
        field_inner = jnp.concatenate([updated_gas, below_inner[:, :, None]], 2)
        below_face = passed_along(upper_face[:, 0], "radial", -1)
        field_face = jnp.concatenate([upper_face, below_face[:, None]], 1)[:, None]

        def window_part(field):
            layers = field.shape[1]
            part = jnp.einsum(
                "fxnz,wyn->fxwyz", field, window_map(count_y, span_y + 1),
                precision=lax.Precision.HIGH,
            )
            part = part.reshape(5, layers * 5, count_y, span_z)
            part = jnp.einsum(
                "fayz,ekz->faeyk", part, window_map(count_z, span_z),
                precision=lax.Precision.HIGH,
            )
            part = part.reshape(5, layers * 25, brick_total)
            return jnp.einsum("gb,feb->gfe", selector, part, precision=lax.Precision.HIGH)

        picked = jnp.concatenate([window_part(field_inner), window_part(field_face)], 2)
    else:
        extended = jnp.concatenate([updated_gas, upper_face[:, None]], 1)
        below_row = passed_along(extended[:, :, 0], "radial", -1)
        gas_field = jnp.concatenate([extended, below_row[:, :, None]], 2)
        gas_field = jnp.pad(gas_field, ((0, 0), (0, 0), (0, 0), (0, 1)))
        windows = split_windows(gas_field, 3, count_z)
        windows = split_windows(windows, 2, count_y)
        windows = split_windows(windows, 1, count_x)
        windows = jnp.transpose(windows, (0, 1, 3, 5, 2, 4, 6)).reshape(5, brick_total, 125)
        picked = jnp.einsum("gb,fbe->gfe", selector, windows, precision=lax.Precision.HIGH)
    picked = picked.reshape(block_count, 25, 25)
    partial = jnp.einsum("gab,bgp->agp", picked, weight_yz, precision=lax.Precision.HIGH)
    values = jnp.sum(partial.reshape(5, 5, block_count, 128) * factor_x[None], axis=1)
    parcel_gas = values.reshape(5, block_count * 128).astype(jnp.bfloat16)
    return (source, parcel_gas)


def solution(mesh):
    return jax.shard_map(
        per_device,
        mesh=mesh,
        in_specs=(
            P(None, ("axial", "radial")),
            P(None, ("axial", "radial")),
            P(("axial", "radial")),
            P(None, ("axial", "radial")),
            P(("axial", "radial")),
            P(None, "axial", "radial", None),
        ),
        out_specs=(P(None, "axial", "radial", None), P(None, ("axial", "radial"))),
        check_vma=False,
    )
```

```python
import math

import jax
import jax.numpy as jnp
from jax import lax
from jax.experimental import pallas as pl
from jax.experimental.pallas import tpu as pltpu
from jax.sharding import PartitionSpec as P

COUPLE = 0.5


def passed_along(block, axis, distance):
    devices = range(lax.axis_size(axis))
    route = [(i - distance, i) for i in devices if i - distance in devices]
    return lax.ppermute(block, axis, route)


def kernel_weights(cell_index, offsets):
    extent = jnp.arange(128, dtype=jnp.int32)
    brick_x = extent // 25
    brick_y = extent // 5 % 5
    brick_z = extent % 5
    inside = (extent < 125).astype(jnp.float32)

    def factor(cell_coord, brick_coord, fraction):
        cell_coord = cell_coord[:, :, None]
        fraction = fraction[:, :, None]
        return jnp.where(
            brick_coord == cell_coord,
            1.0 - fraction,
            jnp.where(brick_coord == cell_coord + 1, fraction, 0.0),
        )

    cell_x = cell_index // 16
    cell_y = cell_index // 4 % 4
    cell_z = cell_index % 4
    return (
        factor(cell_x, brick_x, offsets[0])
        * factor(cell_y, brick_y, offsets[1])
        * factor(cell_z, brick_z, offsets[2])
        * inside
    )


def axis_factors(cell_index, offsets):
    extent = jnp.arange(5, dtype=jnp.int32).reshape((5,) + (1,) * cell_index.ndim)

    def factor(cell_coord, fraction):
        return jnp.where(
            extent == cell_coord[None],
            1.0 - fraction[None],
            jnp.where(extent == cell_coord[None] + 1, fraction[None], 0.0),
        )

    return (
        factor(cell_index // 16, offsets[0]),
        factor(cell_index // 4 % 4, offsets[1]),
        factor(cell_index % 4, offsets[2]),
    )


def split_windows(field, axis, count):
    core = lax.slice_in_dim(field, 0, 4 * count, axis=axis)
    core = core.reshape(field.shape[:axis] + (count, 4) + field.shape[axis + 1 :])
    tail = lax.slice_in_dim(field, 4, 4 * count + 1, stride=4, axis=axis)
    tail = jnp.expand_dims(tail, axis + 1)
    return jnp.concatenate([core, tail], axis + 1)


def merge_windows(field, axis, count, keep_tail):
    core = lax.slice_in_dim(field, 0, 4, axis=axis + 1)
    tail = lax.slice_in_dim(field, 4, 5, axis=axis + 1)
    zero_brick = jnp.zeros_like(lax.slice_in_dim(core, 0, 1, axis=axis))
    core = jnp.concatenate([core, zero_brick], axis)
    zero_tail = jnp.zeros_like(lax.slice_in_dim(tail, 0, 1, axis=axis))
    tail = jnp.concatenate([zero_tail, tail], axis)
    first = lax.slice_in_dim(core, 0, 1, axis=axis + 1) + tail
    rest = lax.slice_in_dim(core, 1, 4, axis=axis + 1)
    joined = jnp.concatenate([first, rest], axis + 1)
    joined = joined.reshape(field.shape[:axis] + (4 * (count + 1),) + field.shape[axis + 2 :])
    length = 4 * count + 1 if keep_tail else 4 * count
    return lax.slice_in_dim(joined, 0, length, axis=axis)


def window_map(count, length):
    extent = jnp.arange(5, dtype=jnp.int32)[:, None, None]
    brick = jnp.arange(count, dtype=jnp.int32)[None, :, None]
    cell = jnp.arange(length, dtype=jnp.int32)[None, None, :]
    return (4 * brick + extent == cell).astype(jnp.float32)


def radial_fold(layers):
    arrived = passed_along(layers[:, :, -1], "radial", 1)
    return layers.at[:, :, 0].add(arrived)


def departed_mask(cross_rows, resident):
    rows = cross_rows.reshape(-1)
    lanes = 128
    high = jnp.where(rows >= 0, rows // lanes, -1)
    low = jnp.where(rows >= 0, rows % lanes, -1)
    high_hot = (high[None, :] == jnp.arange(resident // lanes, dtype=jnp.int32)[:, None]).astype(jnp.bfloat16)
    low_hot = (low[None, :] == jnp.arange(lanes, dtype=jnp.int32)[:, None]).astype(jnp.bfloat16)
    counts = jnp.einsum("hs,ls->hl", high_hot, low_hot, preferred_element_type=jnp.float32)
    return counts.reshape(resident)


def gather_rows(table, rows, interpret=False):
    slots = rows.shape[0]
    height, width = table.shape
    chunk = math.gcd(slots, 4096)
    steps = slots // chunk
    rows = jnp.clip(rows, 0, height - 1).reshape(steps, 1, chunk)

    def kernel(row_ref, table_ref, out_ref):
        def body(i, carry):
            row = row_ref[0, 0, i]
            out_ref[pl.ds(i, 1), :] = table_ref[pl.ds(row, 1), :]
            return carry

        lax.fori_loop(0, chunk, body, 0, unroll=64)

    return pl.pallas_call(
        kernel,
        out_shape=jax.ShapeDtypeStruct((slots, width), table.dtype),
        grid=(steps,),
        in_specs=[
            pl.BlockSpec((1, 1, chunk), lambda s: (s, 0, 0), memory_space=pltpu.SMEM),
            pl.BlockSpec((height, width), lambda s: (0, 0)),
        ],
        out_specs=pl.BlockSpec((chunk, width), lambda s: (s, 0)),
        compiler_params=pltpu.CompilerParams(vmem_limit_bytes=48 * 1024 * 1024),
        interpret=interpret,
    )(rows, table)


def per_device(parcel_load, parcel_offset, parcel_cell, cross_rows, block_brick, gas):
    span_x = gas.shape[1]
    span_y = gas.shape[2]
    span_z = gas.shape[3]
    count_x = span_x // 4
    count_y = span_y // 4
    count_z = span_z // 4
    brick_total = count_x * count_y * count_z
    resident = parcel_load.shape[1]
    block_count = block_brick.shape[0]
    brick_numbers = jnp.arange(brick_total, dtype=jnp.int32)
    attributes = jnp.concatenate(
        [parcel_load, parcel_offset, parcel_cell[None].astype(jnp.float32)], 0
    )
    usable = cross_rows >= 0
    safe_rows = jnp.maximum(cross_rows, 0)
    table = attributes.T
    flip = jnp.eye(table.shape[1], dtype=jnp.float32)

    def moving(side):
        picked = gather_rows(table, safe_rows[side])
        picked = jnp.einsum("fc,sc->fs", flip, picked, precision=lax.Precision.HIGHEST)
        return picked * usable[side].astype(jnp.float32)

    upward = moving(0)
    from_lower = passed_along(upward, "axial", 1)
    downward = moving(1)
    from_upper = passed_along(downward, "axial", -1)
    departed = departed_mask(cross_rows, resident)
    staying = jnp.concatenate([attributes[:8] * (1.0 - departed)[None], attributes[8:]], 0)
    staying_blocks = resident // 128
    selector = (block_brick[:, None] == brick_numbers[None, :]).astype(jnp.float32)

    def deposit_part(part_rows, part_selector):
        part_blocks = part_rows.shape[1] // 128
        part_rows = part_rows.reshape(9, part_blocks, 128)
        factor_x, factor_y, factor_z = axis_factors(part_rows[8].astype(jnp.int32), part_rows[5:8])
        load_x = (part_rows[:5][:, None] * factor_x[None]).reshape(25, part_blocks, 128)
        weight_yz = (factor_y[:, None] * factor_z[None]).reshape(25, part_blocks, 128)
        spread = jnp.einsum("agp,bgp->gab", load_x, weight_yz, precision=lax.Precision.HIGH)
        part_sums = jnp.einsum(
            "gb,gfe->feb", part_selector, spread.reshape(part_blocks, 5, 125),
            precision=lax.Precision.HIGH,
        )
        return part_sums, factor_x, weight_yz

    stay_sums, stay_x, stay_yz = deposit_part(staying, selector[:staying_blocks])
    from_lower, from_upper, stay_sums = lax.optimization_barrier((from_lower, from_upper, stay_sums))
    moved = jnp.concatenate([from_lower, from_upper], 1)
    moved_sums, moved_x, moved_yz = deposit_part(moved, selector[staying_blocks:])
    brick_sums = stay_sums + moved_sums
    factor_x = jnp.concatenate([stay_x, moved_x], 1)
    weight_yz = jnp.concatenate([stay_yz, moved_yz], 1)
    if count_x == 1:
        laid = brick_sums.reshape(5, 25, 5, count_y, count_z)
        laid = jnp.einsum(
            "faeyk,ekz->fayz", laid, window_map(count_z, span_z), precision=lax.Precision.HIGH
        )
        laid = laid.reshape(5, 5, 5, count_y, span_z)
        deposit_grid = jnp.einsum(
            "fxwyz,wyn->fxnz", laid, window_map(count_y, span_y + 1),
            precision=lax.Precision.HIGH,
        )
    else:
        laid = jnp.transpose(brick_sums, (0, 2, 1))
        laid = laid.reshape(5, count_x, count_y, count_z, 5, 5, 5)
        laid = jnp.transpose(laid, (0, 1, 4, 2, 5, 3, 6))
        laid = merge_windows(laid, 1, count_x, True)
        laid = merge_windows(laid, 2, count_y, True)
        deposit_grid = merge_windows(laid, 3, count_z, False)
    incoming = passed_along(deposit_grid[:, span_x], "axial", 1)
    summed = deposit_grid[:, :span_x].at[:, 0].add(incoming)
    folded = radial_fold(summed)
    source = folded[:, :, :span_y]
    updated_gas = gas + COUPLE * source
    upper_face = passed_along(updated_gas[:, 0], "axial", -1)
    if count_x == 1:
        below_inner = passed_along(updated_gas[:, :, 0], "radial", -1)
        field_inner = jnp.concatenate([updated_gas, below_inner[:, :, None]], 2)
        below_face = passed_along(upper_face[:, 0], "radial", -1)
        field_face = jnp.concatenate([upper_face, below_face[:, None]], 1)[:, None]

        def window_part(field):
            layers = field.shape[1]
            part = jnp.einsum(
                "fxnz,wyn->fxwyz", field, window_map(count_y, span_y + 1),
                precision=lax.Precision.HIGH,
            )
            part = part.reshape(5, layers * 5, count_y, span_z)
            part = jnp.einsum(
                "fayz,ekz->faeyk", part, window_map(count_z, span_z),
                precision=lax.Precision.HIGH,
            )
            part = part.reshape(5, layers * 25, brick_total)
            return jnp.einsum("gb,feb->gfe", selector, part, precision=lax.Precision.HIGH)

        picked = jnp.concatenate([window_part(field_inner), window_part(field_face)], 2)
    else:
        extended = jnp.concatenate([updated_gas, upper_face[:, None]], 1)
        below_row = passed_along(extended[:, :, 0], "radial", -1)
        gas_field = jnp.concatenate([extended, below_row[:, :, None]], 2)
        gas_field = jnp.pad(gas_field, ((0, 0), (0, 0), (0, 0), (0, 1)))
        windows = split_windows(gas_field, 3, count_z)
        windows = split_windows(windows, 2, count_y)
        windows = split_windows(windows, 1, count_x)
        windows = jnp.transpose(windows, (0, 1, 3, 5, 2, 4, 6)).reshape(5, brick_total, 125)
        picked = jnp.einsum("gb,fbe->gfe", selector, windows, precision=lax.Precision.HIGH)
    picked = picked.reshape(block_count, 25, 25)
    partial = jnp.einsum("gab,bgp->agp", picked, weight_yz, precision=lax.Precision.HIGH)
    values = jnp.sum(partial.reshape(5, 5, block_count, 128) * factor_x[None], axis=1)
    parcel_gas = values.reshape(5, block_count * 128).astype(jnp.bfloat16)
    return (source, parcel_gas)


def solution(mesh):
    return jax.shard_map(
        per_device,
        mesh=mesh,
        in_specs=(
            P(None, ("axial", "radial")),
            P(None, ("axial", "radial")),
            P(("axial", "radial")),
            P(None, ("axial", "radial")),
            P(("axial", "radial")),
            P(None, "axial", "radial", None),
        ),
        out_specs=(P(None, "axial", "radial", None), P(None, ("axial", "radial"))),
        check_vma=False,
    )
```

```python
import math

import jax
import jax.numpy as jnp
from jax import lax
from jax.experimental import pallas as pl
from jax.experimental.pallas import tpu as pltpu
from jax.sharding import PartitionSpec as P

COUPLE = 0.5


def passed_along(block, axis, distance):
    devices = range(lax.axis_size(axis))
    route = [(i - distance, i) for i in devices if i - distance in devices]
    return lax.ppermute(block, axis, route)


def kernel_weights(cell_index, offsets):
    extent = jnp.arange(128, dtype=jnp.int32)
    brick_x = extent // 25
    brick_y = extent // 5 % 5
    brick_z = extent % 5
    inside = (extent < 125).astype(jnp.float32)

    def factor(cell_coord, brick_coord, fraction):
        cell_coord = cell_coord[:, :, None]
        fraction = fraction[:, :, None]
        return jnp.where(
            brick_coord == cell_coord,
            1.0 - fraction,
            jnp.where(brick_coord == cell_coord + 1, fraction, 0.0),
        )

    cell_x = cell_index // 16
    cell_y = cell_index // 4 % 4
    cell_z = cell_index % 4
    return (
        factor(cell_x, brick_x, offsets[0])
        * factor(cell_y, brick_y, offsets[1])
        * factor(cell_z, brick_z, offsets[2])
        * inside
    )


def axis_factors(cell_index, offsets):
    extent = jnp.arange(5, dtype=jnp.int32).reshape((5,) + (1,) * cell_index.ndim)

    def factor(cell_coord, fraction):
        return jnp.where(
            extent == cell_coord[None],
            1.0 - fraction[None],
            jnp.where(extent == cell_coord[None] + 1, fraction[None], 0.0),
        )

    return (
        factor(cell_index // 16, offsets[0]),
        factor(cell_index // 4 % 4, offsets[1]),
        factor(cell_index % 4, offsets[2]),
    )


def split_windows(field, axis, count):
    core = lax.slice_in_dim(field, 0, 4 * count, axis=axis)
    core = core.reshape(field.shape[:axis] + (count, 4) + field.shape[axis + 1 :])
    tail = lax.slice_in_dim(field, 4, 4 * count + 1, stride=4, axis=axis)
    tail = jnp.expand_dims(tail, axis + 1)
    return jnp.concatenate([core, tail], axis + 1)


def merge_windows(field, axis, count, keep_tail):
    core = lax.slice_in_dim(field, 0, 4, axis=axis + 1)
    tail = lax.slice_in_dim(field, 4, 5, axis=axis + 1)
    zero_brick = jnp.zeros_like(lax.slice_in_dim(core, 0, 1, axis=axis))
    core = jnp.concatenate([core, zero_brick], axis)
    zero_tail = jnp.zeros_like(lax.slice_in_dim(tail, 0, 1, axis=axis))
    tail = jnp.concatenate([zero_tail, tail], axis)
    first = lax.slice_in_dim(core, 0, 1, axis=axis + 1) + tail
    rest = lax.slice_in_dim(core, 1, 4, axis=axis + 1)
    joined = jnp.concatenate([first, rest], axis + 1)
    joined = joined.reshape(field.shape[:axis] + (4 * (count + 1),) + field.shape[axis + 2 :])
    length = 4 * count + 1 if keep_tail else 4 * count
    return lax.slice_in_dim(joined, 0, length, axis=axis)


def window_map(count, length):
    extent = jnp.arange(5, dtype=jnp.int32)[:, None, None]
    brick = jnp.arange(count, dtype=jnp.int32)[None, :, None]
    cell = jnp.arange(length, dtype=jnp.int32)[None, None, :]
    return (4 * brick + extent == cell).astype(jnp.float32)


def radial_fold(layers):
    arrived = passed_along(layers[:, :, -1], "radial", 1)
    return layers.at[:, :, 0].add(arrived)


def departed_mask(cross_rows, resident):
    rows = cross_rows.reshape(-1)
    lanes = 128
    high = jnp.where(rows >= 0, rows // lanes, -1)
    low = jnp.where(rows >= 0, rows % lanes, -1)
    high_hot = (high[None, :] == jnp.arange(resident // lanes, dtype=jnp.int32)[:, None]).astype(jnp.bfloat16)
    low_hot = (low[None, :] == jnp.arange(lanes, dtype=jnp.int32)[:, None]).astype(jnp.bfloat16)
    counts = jnp.einsum("hs,ls->hl", high_hot, low_hot, preferred_element_type=jnp.float32)
    return counts.reshape(resident)


def gather_rows(table, rows, interpret=False):
    slots = rows.shape[0]
    height, width = table.shape
    chunk = math.gcd(slots, 4096)
    steps = slots // chunk
    rows = jnp.clip(rows, 0, height - 1).reshape(steps, 1, chunk)

    def kernel(row_ref, table_ref, out_ref):
        def body(i, carry):
            row = row_ref[0, 0, i]
            out_ref[pl.ds(i, 1), :] = table_ref[pl.ds(row, 1), :]
            return carry

        lax.fori_loop(0, chunk, body, 0, unroll=64)

    return pl.pallas_call(
        kernel,
        out_shape=jax.ShapeDtypeStruct((slots, width), table.dtype),
        grid=(steps,),
        in_specs=[
            pl.BlockSpec((1, 1, chunk), lambda s: (s, 0, 0), memory_space=pltpu.SMEM),
            pl.BlockSpec((height, width), lambda s: (0, 0)),
        ],
        out_specs=pl.BlockSpec((chunk, width), lambda s: (s, 0)),
        compiler_params=pltpu.CompilerParams(vmem_limit_bytes=48 * 1024 * 1024),
        interpret=interpret,
    )(rows, table)


def per_device(parcel_load, parcel_offset, parcel_cell, cross_rows, block_brick, gas):
    span_x = gas.shape[1]
    span_y = gas.shape[2]
    span_z = gas.shape[3]
    count_x = span_x // 4
    count_y = span_y // 4
    count_z = span_z // 4
    brick_total = count_x * count_y * count_z
    resident = parcel_load.shape[1]
    block_count = block_brick.shape[0]
    brick_numbers = jnp.arange(brick_total, dtype=jnp.int32)
    attributes = jnp.concatenate(
        [parcel_load, parcel_offset, parcel_cell[None].astype(jnp.float32)], 0
    )
    usable = cross_rows >= 0
    safe_rows = jnp.maximum(cross_rows, 0)
    table = attributes.T
    flip = jnp.eye(table.shape[1], dtype=jnp.float32)

    def moving(side):
        picked = gather_rows(table, safe_rows[side])
        picked = jnp.einsum("fc,sc->fs", flip, picked, precision=lax.Precision.HIGHEST)
        return picked * usable[side].astype(jnp.float32)

    upward = moving(0)
    from_lower = passed_along(upward, "axial", 1)
    downward = moving(1)
    from_upper = passed_along(downward, "axial", -1)
    departed = departed_mask(cross_rows, resident)
    staying = jnp.concatenate([attributes[:8] * (1.0 - departed)[None], attributes[8:]], 0)
    staying_blocks = resident // 128
    selector = (brick_numbers[:, None] == block_brick[None, :]).astype(jnp.float32)

    def deposit_part(part_rows, part_selector):
        part_blocks = part_rows.shape[1] // 128
        part_rows = part_rows.reshape(9, part_blocks, 128)
        factor_x, factor_y, factor_z = axis_factors(part_rows[8].astype(jnp.int32), part_rows[5:8])
        load_x = (part_rows[:5][:, None] * factor_x[None]).reshape(25, part_blocks, 128)
        weight_yz = (factor_y[:, None] * factor_z[None]).reshape(25, part_blocks, 128)
        spread = jnp.einsum("agp,bgp->gab", load_x, weight_yz, precision=lax.Precision.HIGH)
        part_sums = jnp.einsum(
            "bg,gfe->feb", part_selector, spread.reshape(part_blocks, 5, 125),
            precision=lax.Precision.HIGH,
        )
        return part_sums, factor_x, weight_yz

    stay_sums, stay_x, stay_yz = deposit_part(staying, selector[:, :staying_blocks])
    from_lower, from_upper, stay_sums = lax.optimization_barrier((from_lower, from_upper, stay_sums))
    moved = jnp.concatenate([from_lower, from_upper], 1)
    moved_sums, moved_x, moved_yz = deposit_part(moved, selector[:, staying_blocks:])
    brick_sums = stay_sums + moved_sums
    factor_x = jnp.concatenate([stay_x, moved_x], 1)
    weight_yz = jnp.concatenate([stay_yz, moved_yz], 1)
    if count_x == 1:
        laid = brick_sums.reshape(5, 25, 5, count_y, count_z)
        laid = jnp.einsum(
            "faeyk,ekz->fayz", laid, window_map(count_z, span_z), precision=lax.Precision.HIGH
        )
        laid = laid.reshape(5, 5, 5, count_y, span_z)
        deposit_grid = jnp.einsum(
            "fxwyz,wyn->fxnz", laid, window_map(count_y, span_y + 1),
            precision=lax.Precision.HIGH,
        )
    else:
        laid = jnp.transpose(brick_sums, (0, 2, 1))
        laid = laid.reshape(5, count_x, count_y, count_z, 5, 5, 5)
        laid = jnp.transpose(laid, (0, 1, 4, 2, 5, 3, 6))
        laid = merge_windows(laid, 1, count_x, True)
        laid = merge_windows(laid, 2, count_y, True)
        deposit_grid = merge_windows(laid, 3, count_z, False)
    incoming = passed_along(deposit_grid[:, span_x], "axial", 1)
    summed = deposit_grid[:, :span_x].at[:, 0].add(incoming)
    folded = radial_fold(summed)
    source = folded[:, :, :span_y]
    updated_gas = gas + COUPLE * source
    upper_face = passed_along(updated_gas[:, 0], "axial", -1)
    if count_x == 1:
        below_inner = passed_along(updated_gas[:, :, 0], "radial", -1)
        field_inner = jnp.concatenate([updated_gas, below_inner[:, :, None]], 2)
        below_face = passed_along(upper_face[:, 0], "radial", -1)
        field_face = jnp.concatenate([upper_face, below_face[:, None]], 1)[:, None]

        def window_part(field):
            layers = field.shape[1]
            part = jnp.einsum(
                "fxnz,wyn->fxwyz", field, window_map(count_y, span_y + 1),
                precision=lax.Precision.HIGH,
            )
            part = part.reshape(5, layers * 5, count_y, span_z)
            part = jnp.einsum(
                "fayz,ekz->faeyk", part, window_map(count_z, span_z),
                precision=lax.Precision.HIGH,
            )
            part = part.reshape(5, layers * 25, brick_total)
            return jnp.einsum("bg,feb->gfe", selector, part, precision=lax.Precision.HIGH)

        picked = jnp.concatenate([window_part(field_inner), window_part(field_face)], 2)
    else:
        extended = jnp.concatenate([updated_gas, upper_face[:, None]], 1)
        below_row = passed_along(extended[:, :, 0], "radial", -1)
        gas_field = jnp.concatenate([extended, below_row[:, :, None]], 2)
        gas_field = jnp.pad(gas_field, ((0, 0), (0, 0), (0, 0), (0, 1)))
        windows = split_windows(gas_field, 3, count_z)
        windows = split_windows(windows, 2, count_y)
        windows = split_windows(windows, 1, count_x)
        windows = jnp.transpose(windows, (0, 1, 3, 5, 2, 4, 6)).reshape(5, brick_total, 125)
        picked = jnp.einsum("bg,fbe->gfe", selector, windows, precision=lax.Precision.HIGH)
    picked = picked.reshape(block_count, 25, 25)
    partial = jnp.einsum("gab,bgp->agp", picked, weight_yz, precision=lax.Precision.HIGH)
    values = jnp.sum(partial.reshape(5, 5, block_count, 128) * factor_x[None], axis=1)
    parcel_gas = values.reshape(5, block_count * 128).astype(jnp.bfloat16)
    return (source, parcel_gas)


def solution(mesh):
    return jax.shard_map(
        per_device,
        mesh=mesh,
        in_specs=(
            P(None, ("axial", "radial")),
            P(None, ("axial", "radial")),
            P(("axial", "radial")),
            P(None, ("axial", "radial")),
            P(("axial", "radial")),
            P(None, "axial", "radial", None),
        ),
        out_specs=(P(None, "axial", "radial", None), P(None, ("axial", "radial"))),
        check_vma=False,
    )
```

```python
import math

import jax
import jax.numpy as jnp
from jax import lax
from jax.experimental import pallas as pl
from jax.experimental.pallas import tpu as pltpu
from jax.sharding import PartitionSpec as P

COUPLE = 0.5


def passed_along(block, axis, distance):
    devices = range(lax.axis_size(axis))
    route = [(i - distance, i) for i in devices if i - distance in devices]
    return lax.ppermute(block, axis, route)


def kernel_weights(cell_index, offsets):
    extent = jnp.arange(128, dtype=jnp.int32)
    brick_x = extent // 25
    brick_y = extent // 5 % 5
    brick_z = extent % 5
    inside = (extent < 125).astype(jnp.float32)

    def factor(cell_coord, brick_coord, fraction):
        cell_coord = cell_coord[:, :, None]
        fraction = fraction[:, :, None]
        return jnp.where(
            brick_coord == cell_coord,
            1.0 - fraction,
            jnp.where(brick_coord == cell_coord + 1, fraction, 0.0),
        )

    cell_x = cell_index // 16
    cell_y = cell_index // 4 % 4
    cell_z = cell_index % 4
    return (
        factor(cell_x, brick_x, offsets[0])
        * factor(cell_y, brick_y, offsets[1])
        * factor(cell_z, brick_z, offsets[2])
        * inside
    )


def axis_factors(cell_index, offsets):
    extent = jnp.arange(5, dtype=jnp.int32).reshape((5,) + (1,) * cell_index.ndim)

    def factor(cell_coord, fraction):
        return jnp.where(
            extent == cell_coord[None],
            1.0 - fraction[None],
            jnp.where(extent == cell_coord[None] + 1, fraction[None], 0.0),
        )

    return (
        factor(cell_index // 16, offsets[0]),
        factor(cell_index // 4 % 4, offsets[1]),
        factor(cell_index % 4, offsets[2]),
    )


def split_windows(field, axis, count):
    core = lax.slice_in_dim(field, 0, 4 * count, axis=axis)
    core = core.reshape(field.shape[:axis] + (count, 4) + field.shape[axis + 1 :])
    tail = lax.slice_in_dim(field, 4, 4 * count + 1, stride=4, axis=axis)
    tail = jnp.expand_dims(tail, axis + 1)
    return jnp.concatenate([core, tail], axis + 1)


def merge_windows(field, axis, count, keep_tail):
    core = lax.slice_in_dim(field, 0, 4, axis=axis + 1)
    tail = lax.slice_in_dim(field, 4, 5, axis=axis + 1)
    zero_brick = jnp.zeros_like(lax.slice_in_dim(core, 0, 1, axis=axis))
    core = jnp.concatenate([core, zero_brick], axis)
    zero_tail = jnp.zeros_like(lax.slice_in_dim(tail, 0, 1, axis=axis))
    tail = jnp.concatenate([zero_tail, tail], axis)
    first = lax.slice_in_dim(core, 0, 1, axis=axis + 1) + tail
    rest = lax.slice_in_dim(core, 1, 4, axis=axis + 1)
    joined = jnp.concatenate([first, rest], axis + 1)
    joined = joined.reshape(field.shape[:axis] + (4 * (count + 1),) + field.shape[axis + 2 :])
    length = 4 * count + 1 if keep_tail else 4 * count
    return lax.slice_in_dim(joined, 0, length, axis=axis)


def window_map(count, length):
    extent = jnp.arange(5, dtype=jnp.int32)[:, None, None]
    brick = jnp.arange(count, dtype=jnp.int32)[None, :, None]
    cell = jnp.arange(length, dtype=jnp.int32)[None, None, :]
    return (4 * brick + extent == cell).astype(jnp.float32)


def radial_fold(layers):
    arrived = passed_along(layers[:, :, -1], "radial", 1)
    return layers.at[:, :, 0].add(arrived)


def departed_mask(cross_rows, resident):
    rows = cross_rows.reshape(-1)
    lanes = 128
    high = jnp.where(rows >= 0, rows // lanes, -1)
    low = jnp.where(rows >= 0, rows % lanes, -1)
    high_hot = (high[None, :] == jnp.arange(resident // lanes, dtype=jnp.int32)[:, None]).astype(jnp.bfloat16)
    low_hot = (low[None, :] == jnp.arange(lanes, dtype=jnp.int32)[:, None]).astype(jnp.bfloat16)
    counts = jnp.einsum("hs,ls->hl", high_hot, low_hot, preferred_element_type=jnp.float32)
    return counts.reshape(resident)


def gather_rows(table, rows, interpret=False):
    slots = rows.shape[0]
    height, width = table.shape
    chunk = math.gcd(slots, 8192)
    steps = slots // chunk
    rows = jnp.clip(rows, 0, height - 1).reshape(steps, 1, chunk)

    def kernel(row_ref, table_ref, out_ref):
        def body(i, carry):
            row = row_ref[0, 0, i]
            out_ref[pl.ds(i, 1), :] = table_ref[pl.ds(row, 1), :]
            return carry

        lax.fori_loop(0, chunk, body, 0, unroll=128)

    return pl.pallas_call(
        kernel,
        out_shape=jax.ShapeDtypeStruct((slots, width), table.dtype),
        grid=(steps,),
        in_specs=[
            pl.BlockSpec((1, 1, chunk), lambda s: (s, 0, 0), memory_space=pltpu.SMEM),
            pl.BlockSpec((height, width), lambda s: (0, 0)),
        ],
        out_specs=pl.BlockSpec((chunk, width), lambda s: (s, 0)),
        compiler_params=pltpu.CompilerParams(vmem_limit_bytes=48 * 1024 * 1024),
        interpret=interpret,
    )(rows, table)


def per_device(parcel_load, parcel_offset, parcel_cell, cross_rows, block_brick, gas):
    span_x = gas.shape[1]
    span_y = gas.shape[2]
    span_z = gas.shape[3]
    count_x = span_x // 4
    count_y = span_y // 4
    count_z = span_z // 4
    brick_total = count_x * count_y * count_z
    resident = parcel_load.shape[1]
    block_count = block_brick.shape[0]
    brick_numbers = jnp.arange(brick_total, dtype=jnp.int32)
    attributes = jnp.concatenate(
        [parcel_load, parcel_offset, parcel_cell[None].astype(jnp.float32)], 0
    )
    usable = cross_rows >= 0
    safe_rows = jnp.maximum(cross_rows, 0)
    table = attributes.T
    flip = jnp.eye(table.shape[1], dtype=jnp.float32)

    def moving(side):
        picked = gather_rows(table, safe_rows[side])
        picked = jnp.einsum("fc,sc->fs", flip, picked, precision=lax.Precision.HIGHEST)
        return picked * usable[side].astype(jnp.float32)

    upward = moving(0)
    from_lower = passed_along(upward, "axial", 1)
    downward = moving(1)
    from_upper = passed_along(downward, "axial", -1)
    departed = departed_mask(cross_rows, resident)
    staying = jnp.concatenate([attributes[:8] * (1.0 - departed)[None], attributes[8:]], 0)
    staying_blocks = resident // 128
    selector = (brick_numbers[:, None] == block_brick[None, :]).astype(jnp.float32)

    def deposit_part(part_rows, part_selector):
        part_blocks = part_rows.shape[1] // 128
        part_rows = part_rows.reshape(9, part_blocks, 128)
        factor_x, factor_y, factor_z = axis_factors(part_rows[8].astype(jnp.int32), part_rows[5:8])
        load_x = (part_rows[:5][:, None] * factor_x[None]).reshape(25, part_blocks, 128)
        weight_yz = (factor_y[:, None] * factor_z[None]).reshape(25, part_blocks, 128)
        spread = jnp.einsum("agp,bgp->gab", load_x, weight_yz, precision=lax.Precision.HIGH)
        part_sums = jnp.einsum(
            "bg,gfe->feb", part_selector, spread.reshape(part_blocks, 5, 125),
            precision=lax.Precision.HIGH,
        )
        return part_sums, factor_x, weight_yz

    stay_sums, stay_x, stay_yz = deposit_part(staying, selector[:, :staying_blocks])
    from_lower, from_upper, stay_sums = lax.optimization_barrier((from_lower, from_upper, stay_sums))
    moved = jnp.concatenate([from_lower, from_upper], 1)
    moved_sums, moved_x, moved_yz = deposit_part(moved, selector[:, staying_blocks:])
    brick_sums = stay_sums + moved_sums
    factor_x = jnp.concatenate([stay_x, moved_x], 1)
    weight_yz = jnp.concatenate([stay_yz, moved_yz], 1)
    if count_x == 1:
        laid = brick_sums.reshape(5, 25, 5, count_y, count_z)
        laid = jnp.einsum(
            "faeyk,ekz->fayz", laid, window_map(count_z, span_z), precision=lax.Precision.HIGH
        )
        laid = laid.reshape(5, 5, 5, count_y, span_z)
        deposit_grid = jnp.einsum(
            "fxwyz,wyn->fxnz", laid, window_map(count_y, span_y + 1),
            precision=lax.Precision.HIGH,
        )
    else:
        laid = jnp.transpose(brick_sums, (0, 2, 1))
        laid = laid.reshape(5, count_x, count_y, count_z, 5, 5, 5)
        laid = jnp.transpose(laid, (0, 1, 4, 2, 5, 3, 6))
        laid = merge_windows(laid, 1, count_x, True)
        laid = merge_windows(laid, 2, count_y, True)
        deposit_grid = merge_windows(laid, 3, count_z, False)
    incoming = passed_along(deposit_grid[:, span_x], "axial", 1)
    summed = deposit_grid[:, :span_x].at[:, 0].add(incoming)
    folded = radial_fold(summed)
    source = folded[:, :, :span_y]
    updated_gas = gas + COUPLE * source
    upper_face = passed_along(updated_gas[:, 0], "axial", -1)
    if count_x == 1:
        below_inner = passed_along(updated_gas[:, :, 0], "radial", -1)
        field_inner = jnp.concatenate([updated_gas, below_inner[:, :, None]], 2)
        below_face = passed_along(upper_face[:, 0], "radial", -1)
        field_face = jnp.concatenate([upper_face, below_face[:, None]], 1)[:, None]

        def window_part(field):
            layers = field.shape[1]
            part = jnp.einsum(
                "fxnz,wyn->fxwyz", field, window_map(count_y, span_y + 1),
                precision=lax.Precision.HIGH,
            )
            part = part.reshape(5, layers * 5, count_y, span_z)
            part = jnp.einsum(
                "fayz,ekz->faeyk", part, window_map(count_z, span_z),
                precision=lax.Precision.HIGH,
            )
            part = part.reshape(5, layers * 25, brick_total)
            return jnp.einsum("bg,feb->gfe", selector, part, precision=lax.Precision.HIGH)

        picked = jnp.concatenate([window_part(field_inner), window_part(field_face)], 2)
    else:
        extended = jnp.concatenate([updated_gas, upper_face[:, None]], 1)
        below_row = passed_along(extended[:, :, 0], "radial", -1)
        gas_field = jnp.concatenate([extended, below_row[:, :, None]], 2)
        gas_field = jnp.pad(gas_field, ((0, 0), (0, 0), (0, 0), (0, 1)))
        windows = split_windows(gas_field, 3, count_z)
        windows = split_windows(windows, 2, count_y)
        windows = split_windows(windows, 1, count_x)
        windows = jnp.transpose(windows, (0, 1, 3, 5, 2, 4, 6)).reshape(5, brick_total, 125)
        picked = jnp.einsum("bg,fbe->gfe", selector, windows, precision=lax.Precision.HIGH)
    picked = picked.reshape(block_count, 25, 25)
    partial = jnp.einsum("gab,bgp->agp", picked, weight_yz, precision=lax.Precision.HIGH)
    values = jnp.sum(partial.reshape(5, 5, block_count, 128) * factor_x[None], axis=1)
    parcel_gas = values.reshape(5, block_count * 128).astype(jnp.bfloat16)
    return (source, parcel_gas)


def solution(mesh):
    return jax.shard_map(
        per_device,
        mesh=mesh,
        in_specs=(
            P(None, ("axial", "radial")),
            P(None, ("axial", "radial")),
            P(("axial", "radial")),
            P(None, ("axial", "radial")),
            P(("axial", "radial")),
            P(None, "axial", "radial", None),
        ),
        out_specs=(P(None, "axial", "radial", None), P(None, ("axial", "radial"))),
        check_vma=False,
    )
```

```python
import math

import jax
import jax.numpy as jnp
from jax import lax
from jax.experimental import pallas as pl
from jax.experimental.pallas import tpu as pltpu
from jax.sharding import PartitionSpec as P

COUPLE = 0.5


def passed_along(block, axis, distance):
    devices = range(lax.axis_size(axis))
    route = [(i - distance, i) for i in devices if i - distance in devices]
    return lax.ppermute(block, axis, route)


def kernel_weights(cell_index, offsets):
    extent = jnp.arange(128, dtype=jnp.int32)
    brick_x = extent // 25
    brick_y = extent // 5 % 5
    brick_z = extent % 5
    inside = (extent < 125).astype(jnp.float32)

    def factor(cell_coord, brick_coord, fraction):
        cell_coord = cell_coord[:, :, None]
        fraction = fraction[:, :, None]
        return jnp.where(
            brick_coord == cell_coord,
            1.0 - fraction,
            jnp.where(brick_coord == cell_coord + 1, fraction, 0.0),
        )

    cell_x = cell_index // 16
    cell_y = cell_index // 4 % 4
    cell_z = cell_index % 4
    return (
        factor(cell_x, brick_x, offsets[0])
        * factor(cell_y, brick_y, offsets[1])
        * factor(cell_z, brick_z, offsets[2])
        * inside
    )


def axis_factors(cell_index, offsets):
    extent = jnp.arange(5, dtype=jnp.int32).reshape((5,) + (1,) * cell_index.ndim)

    def factor(cell_coord, fraction):
        return jnp.where(
            extent == cell_coord[None],
            1.0 - fraction[None],
            jnp.where(extent == cell_coord[None] + 1, fraction[None], 0.0),
        )

    return (
        factor(cell_index // 16, offsets[0]),
        factor(cell_index // 4 % 4, offsets[1]),
        factor(cell_index % 4, offsets[2]),
    )


def split_windows(field, axis, count):
    core = lax.slice_in_dim(field, 0, 4 * count, axis=axis)
    core = core.reshape(field.shape[:axis] + (count, 4) + field.shape[axis + 1 :])
    tail = lax.slice_in_dim(field, 4, 4 * count + 1, stride=4, axis=axis)
    tail = jnp.expand_dims(tail, axis + 1)
    return jnp.concatenate([core, tail], axis + 1)


def merge_windows(field, axis, count, keep_tail):
    core = lax.slice_in_dim(field, 0, 4, axis=axis + 1)
    tail = lax.slice_in_dim(field, 4, 5, axis=axis + 1)
    zero_brick = jnp.zeros_like(lax.slice_in_dim(core, 0, 1, axis=axis))
    core = jnp.concatenate([core, zero_brick], axis)
    zero_tail = jnp.zeros_like(lax.slice_in_dim(tail, 0, 1, axis=axis))
    tail = jnp.concatenate([zero_tail, tail], axis)
    first = lax.slice_in_dim(core, 0, 1, axis=axis + 1) + tail
    rest = lax.slice_in_dim(core, 1, 4, axis=axis + 1)
    joined = jnp.concatenate([first, rest], axis + 1)
    joined = joined.reshape(field.shape[:axis] + (4 * (count + 1),) + field.shape[axis + 2 :])
    length = 4 * count + 1 if keep_tail else 4 * count
    return lax.slice_in_dim(joined, 0, length, axis=axis)


def window_map(count, length):
    extent = jnp.arange(5, dtype=jnp.int32)[:, None, None]
    brick = jnp.arange(count, dtype=jnp.int32)[None, :, None]
    cell = jnp.arange(length, dtype=jnp.int32)[None, None, :]
    return (4 * brick + extent == cell).astype(jnp.float32)


def radial_fold(layers):
    arrived = passed_along(layers[:, :, -1], "radial", 1)
    return layers.at[:, :, 0].add(arrived)


def departed_mask(cross_rows, resident):
    rows = cross_rows.reshape(-1)
    lanes = 128
    high = jnp.where(rows >= 0, rows // lanes, -1)
    low = jnp.where(rows >= 0, rows % lanes, -1)
    high_hot = (high[None, :] == jnp.arange(resident // lanes, dtype=jnp.int32)[:, None]).astype(jnp.bfloat16)
    low_hot = (low[None, :] == jnp.arange(lanes, dtype=jnp.int32)[:, None]).astype(jnp.bfloat16)
    counts = jnp.einsum("hs,ls->hl", high_hot, low_hot, preferred_element_type=jnp.float32)
    return counts.reshape(resident)


def gather_rows(table, rows, interpret=False):
    slots = rows.shape[0]
    height, width = table.shape
    chunk = math.gcd(slots, 8192)
    steps = slots // chunk
    rows = jnp.clip(rows, 0, height - 1).reshape(steps, 1, chunk)

    def kernel(row_ref, table_ref, out_ref):
        def body(i, carry):
            row = row_ref[0, 0, i]
            out_ref[pl.ds(i, 1), :] = table_ref[pl.ds(row, 1), :]
            return carry

        lax.fori_loop(0, chunk, body, 0, unroll=128)

    return pl.pallas_call(
        kernel,
        out_shape=jax.ShapeDtypeStruct((slots, width), table.dtype),
        grid=(steps,),
        in_specs=[
            pl.BlockSpec((1, 1, chunk), lambda s: (s, 0, 0), memory_space=pltpu.SMEM),
            pl.BlockSpec((height, width), lambda s: (0, 0)),
        ],
        out_specs=pl.BlockSpec((chunk, width), lambda s: (s, 0)),
        compiler_params=pltpu.CompilerParams(vmem_limit_bytes=48 * 1024 * 1024),
        interpret=interpret,
    )(rows, table)


def per_device(parcel_load, parcel_offset, parcel_cell, cross_rows, block_brick, gas):
    span_x = gas.shape[1]
    span_y = gas.shape[2]
    span_z = gas.shape[3]
    count_x = span_x // 4
    count_y = span_y // 4
    count_z = span_z // 4
    brick_total = count_x * count_y * count_z
    resident = parcel_load.shape[1]
    block_count = block_brick.shape[0]
    brick_numbers = jnp.arange(brick_total, dtype=jnp.int32)
    attributes = jnp.concatenate(
        [parcel_load, parcel_offset, parcel_cell[None].astype(jnp.float32)], 0
    )
    usable = cross_rows >= 0
    safe_rows = jnp.maximum(cross_rows, 0)
    table = attributes.T
    flip = jnp.eye(table.shape[1], dtype=jnp.float32)

    def moving(side):
        picked = gather_rows(table, safe_rows[side])
        picked = jnp.einsum("fc,sc->fs", flip, picked, precision=lax.Precision.HIGHEST)
        return picked * usable[side].astype(jnp.float32)

    upward = moving(0)
    from_lower = passed_along(upward, "axial", 1)
    downward = moving(1)
    from_upper = passed_along(downward, "axial", -1)
    departed = departed_mask(cross_rows, resident)
    staying = jnp.concatenate([attributes[:8] * (1.0 - departed)[None], attributes[8:]], 0)
    staying_blocks = resident // 128
    selector = (brick_numbers[:, None] == block_brick[None, :]).astype(jnp.float32)

    def deposit_part(part_rows, part_selector):
        part_blocks = part_rows.shape[1] // 128
        part_rows = part_rows.reshape(9, part_blocks, 128)
        factor_x, factor_y, factor_z = axis_factors(part_rows[8].astype(jnp.int32), part_rows[5:8])
        load_x = (part_rows[:5][:, None] * factor_x[None]).reshape(25, part_blocks, 128)
        weight_yz = (factor_y[:, None] * factor_z[None]).reshape(25, part_blocks, 128)
        spread = jnp.einsum("agp,bgp->gab", load_x, weight_yz, precision=lax.Precision.HIGH)
        part_sums = jnp.einsum(
            "bg,gfe->feb", part_selector, spread.reshape(part_blocks, 5, 125),
            precision=lax.Precision.HIGH,
        )
        return part_sums, factor_x, weight_yz

    stay_sums, stay_x, stay_yz = deposit_part(staying, selector[:, :staying_blocks])
    from_lower, from_upper, stay_sums = lax.optimization_barrier((from_lower, from_upper, stay_sums))
    lower_blocks = staying_blocks + from_lower.shape[1] // 128
    lower_sums, lower_x, lower_yz = deposit_part(from_lower, selector[:, staying_blocks:lower_blocks])
    upper_sums, upper_x, upper_yz = deposit_part(from_upper, selector[:, lower_blocks:])
    brick_sums = stay_sums + lower_sums + upper_sums
    factor_x = jnp.concatenate([stay_x, lower_x, upper_x], 1)
    weight_yz = jnp.concatenate([stay_yz, lower_yz, upper_yz], 1)
    if count_x == 1:
        laid = brick_sums.reshape(5, 25, 5, count_y, count_z)
        laid = jnp.einsum(
            "faeyk,ekz->fayz", laid, window_map(count_z, span_z), precision=lax.Precision.HIGH
        )
        laid = laid.reshape(5, 5, 5, count_y, span_z)
        deposit_grid = jnp.einsum(
            "fxwyz,wyn->fxnz", laid, window_map(count_y, span_y + 1),
            precision=lax.Precision.HIGH,
        )
    else:
        laid = jnp.transpose(brick_sums, (0, 2, 1))
        laid = laid.reshape(5, count_x, count_y, count_z, 5, 5, 5)
        laid = jnp.transpose(laid, (0, 1, 4, 2, 5, 3, 6))
        laid = merge_windows(laid, 1, count_x, True)
        laid = merge_windows(laid, 2, count_y, True)
        deposit_grid = merge_windows(laid, 3, count_z, False)
    incoming = passed_along(deposit_grid[:, span_x], "axial", 1)
    summed = deposit_grid[:, :span_x].at[:, 0].add(incoming)
    folded = radial_fold(summed)
    source = folded[:, :, :span_y]
    updated_gas = gas + COUPLE * source
    upper_face = passed_along(updated_gas[:, 0], "axial", -1)
    if count_x == 1:
        below_inner = passed_along(updated_gas[:, :, 0], "radial", -1)
        field_inner = jnp.concatenate([updated_gas, below_inner[:, :, None]], 2)
        below_face = passed_along(upper_face[:, 0], "radial", -1)
        field_face = jnp.concatenate([upper_face, below_face[:, None]], 1)[:, None]

        def window_part(field):
            layers = field.shape[1]
            part = jnp.einsum(
                "fxnz,wyn->fxwyz", field, window_map(count_y, span_y + 1),
                precision=lax.Precision.HIGH,
            )
            part = part.reshape(5, layers * 5, count_y, span_z)
            part = jnp.einsum(
                "fayz,ekz->faeyk", part, window_map(count_z, span_z),
                precision=lax.Precision.HIGH,
            )
            part = part.reshape(5, layers * 25, brick_total)
            return jnp.einsum("bg,feb->gfe", selector, part, precision=lax.Precision.HIGH)

        picked = jnp.concatenate([window_part(field_inner), window_part(field_face)], 2)
    else:
        extended = jnp.concatenate([updated_gas, upper_face[:, None]], 1)
        below_row = passed_along(extended[:, :, 0], "radial", -1)
        gas_field = jnp.concatenate([extended, below_row[:, :, None]], 2)
        gas_field = jnp.pad(gas_field, ((0, 0), (0, 0), (0, 0), (0, 1)))
        windows = split_windows(gas_field, 3, count_z)
        windows = split_windows(windows, 2, count_y)
        windows = split_windows(windows, 1, count_x)
        windows = jnp.transpose(windows, (0, 1, 3, 5, 2, 4, 6)).reshape(5, brick_total, 125)
        picked = jnp.einsum("bg,fbe->gfe", selector, windows, precision=lax.Precision.HIGH)
    picked = picked.reshape(block_count, 25, 25)
    partial = jnp.einsum("gab,bgp->agp", picked, weight_yz, precision=lax.Precision.HIGH)
    values = jnp.sum(partial.reshape(5, 5, block_count, 128) * factor_x[None], axis=1)
    parcel_gas = values.reshape(5, block_count * 128).astype(jnp.bfloat16)
    return (source, parcel_gas)


def solution(mesh):
    return jax.shard_map(
        per_device,
        mesh=mesh,
        in_specs=(
            P(None, ("axial", "radial")),
            P(None, ("axial", "radial")),
            P(("axial", "radial")),
            P(None, ("axial", "radial")),
            P(("axial", "radial")),
            P(None, "axial", "radial", None),
        ),
        out_specs=(P(None, "axial", "radial", None), P(None, ("axial", "radial"))),
        check_vma=False,
    )
```

```python
import math

import jax
import jax.numpy as jnp
from jax import lax
from jax.experimental import pallas as pl
from jax.experimental.pallas import tpu as pltpu
from jax.sharding import PartitionSpec as P

COUPLE = 0.5


def passed_along(block, axis, distance):
    devices = range(lax.axis_size(axis))
    route = [(i - distance, i) for i in devices if i - distance in devices]
    return lax.ppermute(block, axis, route)


def kernel_weights(cell_index, offsets):
    extent = jnp.arange(128, dtype=jnp.int32)
    brick_x = extent // 25
    brick_y = extent // 5 % 5
    brick_z = extent % 5
    inside = (extent < 125).astype(jnp.float32)

    def factor(cell_coord, brick_coord, fraction):
        cell_coord = cell_coord[:, :, None]
        fraction = fraction[:, :, None]
        return jnp.where(
            brick_coord == cell_coord,
            1.0 - fraction,
            jnp.where(brick_coord == cell_coord + 1, fraction, 0.0),
        )

    cell_x = cell_index // 16
    cell_y = cell_index // 4 % 4
    cell_z = cell_index % 4
    return (
        factor(cell_x, brick_x, offsets[0])
        * factor(cell_y, brick_y, offsets[1])
        * factor(cell_z, brick_z, offsets[2])
        * inside
    )


def axis_factors(cell_index, offsets):
    extent = jnp.arange(5, dtype=jnp.int32).reshape((5,) + (1,) * cell_index.ndim)

    def factor(cell_coord, fraction):
        return jnp.where(
            extent == cell_coord[None],
            1.0 - fraction[None],
            jnp.where(extent == cell_coord[None] + 1, fraction[None], 0.0),
        )

    return (
        factor(cell_index // 16, offsets[0]),
        factor(cell_index // 4 % 4, offsets[1]),
        factor(cell_index % 4, offsets[2]),
    )


def split_windows(field, axis, count):
    core = lax.slice_in_dim(field, 0, 4 * count, axis=axis)
    core = core.reshape(field.shape[:axis] + (count, 4) + field.shape[axis + 1 :])
    tail = lax.slice_in_dim(field, 4, 4 * count + 1, stride=4, axis=axis)
    tail = jnp.expand_dims(tail, axis + 1)
    return jnp.concatenate([core, tail], axis + 1)


def merge_windows(field, axis, count, keep_tail):
    core = lax.slice_in_dim(field, 0, 4, axis=axis + 1)
    tail = lax.slice_in_dim(field, 4, 5, axis=axis + 1)
    zero_brick = jnp.zeros_like(lax.slice_in_dim(core, 0, 1, axis=axis))
    core = jnp.concatenate([core, zero_brick], axis)
    zero_tail = jnp.zeros_like(lax.slice_in_dim(tail, 0, 1, axis=axis))
    tail = jnp.concatenate([zero_tail, tail], axis)
    first = lax.slice_in_dim(core, 0, 1, axis=axis + 1) + tail
    rest = lax.slice_in_dim(core, 1, 4, axis=axis + 1)
    joined = jnp.concatenate([first, rest], axis + 1)
    joined = joined.reshape(field.shape[:axis] + (4 * (count + 1),) + field.shape[axis + 2 :])
    length = 4 * count + 1 if keep_tail else 4 * count
    return lax.slice_in_dim(joined, 0, length, axis=axis)


def window_map(count, length):
    extent = jnp.arange(5, dtype=jnp.int32)[:, None, None]
    brick = jnp.arange(count, dtype=jnp.int32)[None, :, None]
    cell = jnp.arange(length, dtype=jnp.int32)[None, None, :]
    return (4 * brick + extent == cell).astype(jnp.float32)


def radial_fold(layers):
    arrived = passed_along(layers[:, :, -1], "radial", 1)
    return layers.at[:, :, 0].add(arrived)


def departed_mask(cross_rows, resident):
    rows = cross_rows.reshape(-1)
    lanes = 128
    high = jnp.where(rows >= 0, rows // lanes, -1)
    low = jnp.where(rows >= 0, rows % lanes, -1)
    high_hot = (high[None, :] == jnp.arange(resident // lanes, dtype=jnp.int32)[:, None]).astype(jnp.bfloat16)
    low_hot = (low[None, :] == jnp.arange(lanes, dtype=jnp.int32)[:, None]).astype(jnp.bfloat16)
    counts = jnp.einsum("hs,ls->hl", high_hot, low_hot, preferred_element_type=jnp.float32)
    return counts.reshape(resident)


def gather_rows(table, rows, interpret=False):
    slots = rows.shape[0]
    height, width = table.shape
    chunk = math.gcd(slots, 8192)
    steps = slots // chunk
    rows = jnp.clip(rows, 0, height - 1).reshape(steps, 1, chunk)

    def kernel(row_ref, table_ref, out_ref):
        def body(i, carry):
            row = row_ref[0, 0, i]
            out_ref[pl.ds(i, 1), :] = table_ref[pl.ds(row, 1), :]
            return carry

        lax.fori_loop(0, chunk, body, 0, unroll=128)

    return pl.pallas_call(
        kernel,
        out_shape=jax.ShapeDtypeStruct((slots, width), table.dtype),
        grid=(steps,),
        in_specs=[
            pl.BlockSpec((1, 1, chunk), lambda s: (s, 0, 0), memory_space=pltpu.SMEM),
            pl.BlockSpec((height, width), lambda s: (0, 0)),
        ],
        out_specs=pl.BlockSpec((chunk, width), lambda s: (s, 0)),
        compiler_params=pltpu.CompilerParams(vmem_limit_bytes=48 * 1024 * 1024),
        interpret=interpret,
    )(rows, table)


def per_device(parcel_load, parcel_offset, parcel_cell, cross_rows, block_brick, gas):
    span_x = gas.shape[1]
    span_y = gas.shape[2]
    span_z = gas.shape[3]
    count_x = span_x // 4
    count_y = span_y // 4
    count_z = span_z // 4
    brick_total = count_x * count_y * count_z
    resident = parcel_load.shape[1]
    block_count = block_brick.shape[0]
    brick_numbers = jnp.arange(brick_total, dtype=jnp.int32)
    attributes = jnp.concatenate(
        [parcel_load, parcel_offset, parcel_cell[None].astype(jnp.float32)], 0
    )
    usable = cross_rows >= 0
    safe_rows = jnp.maximum(cross_rows, 0)
    table = attributes.T
    flip = jnp.eye(table.shape[1], dtype=jnp.float32)

    def moving(side):
        picked = gather_rows(table, safe_rows[side])
        picked = jnp.einsum("fc,sc->fs", flip, picked, precision=lax.Precision.HIGHEST)
        return picked * usable[side].astype(jnp.float32)

    upward = moving(0)
    from_lower = passed_along(upward, "axial", 1)
    downward = moving(1)
    from_upper = passed_along(downward, "axial", -1)
    departed = departed_mask(cross_rows, resident)
    staying = jnp.concatenate([attributes[:8] * (1.0 - departed)[None], attributes[8:]], 0)
    staying_blocks = resident // 128
    selector = (brick_numbers[:, None] == block_brick[None, :]).astype(jnp.float32)

    def deposit_part(part_rows, part_selector):
        part_blocks = part_rows.shape[1] // 128
        part_rows = part_rows.reshape(9, part_blocks, 128)
        factor_x, factor_y, factor_z = axis_factors(part_rows[8].astype(jnp.int32), part_rows[5:8])
        load_x = (part_rows[:5][:, None] * factor_x[None]).reshape(25, part_blocks, 128)
        weight_yz = (factor_y[:, None] * factor_z[None]).reshape(25, part_blocks, 128)
        spread = jnp.einsum("agp,bgp->gab", load_x, weight_yz, precision=lax.Precision.HIGH)
        part_sums = jnp.einsum(
            "bg,gfe->feb", part_selector, spread.reshape(part_blocks, 5, 125),
            precision=lax.Precision.HIGH,
        )
        return part_sums, factor_x, weight_yz

    stay_sums, stay_x, stay_yz = deposit_part(staying, selector[:, :staying_blocks])
    from_lower, from_upper, stay_sums = lax.optimization_barrier((from_lower, from_upper, stay_sums))
    moved = jnp.concatenate([from_lower, from_upper], 1)
    moved_sums, moved_x, moved_yz = deposit_part(moved, selector[:, staying_blocks:])
    brick_sums = stay_sums + moved_sums
    factor_x = jnp.concatenate([stay_x, moved_x], 1)
    weight_yz = jnp.concatenate([stay_yz, moved_yz], 1)
    if count_x == 1:
        laid = brick_sums.reshape(5, 25, 5, count_y, count_z)
        laid = jnp.einsum(
            "faeyk,ekz->fayz", laid, window_map(count_z, span_z), precision=lax.Precision.HIGH
        )
        laid = laid.reshape(5, 5, 5, count_y, span_z)
        deposit_grid = jnp.einsum(
            "fxwyz,wyn->fxnz", laid, window_map(count_y, span_y + 1),
            precision=lax.Precision.HIGH,
        )
    else:
        laid = jnp.transpose(brick_sums, (0, 2, 1))
        laid = laid.reshape(5, count_x, count_y, count_z, 5, 5, 5)
        laid = jnp.transpose(laid, (0, 1, 4, 2, 5, 3, 6))
        laid = merge_windows(laid, 1, count_x, True)
        laid = merge_windows(laid, 2, count_y, True)
        deposit_grid = merge_windows(laid, 3, count_z, False)
    incoming = passed_along(deposit_grid[:, span_x], "axial", 1)
    summed = deposit_grid[:, :span_x].at[:, 0].add(incoming)
    folded = radial_fold(summed)
    source = folded[:, :, :span_y]
    updated_gas = gas + COUPLE * source
    upper_face = passed_along(updated_gas[:, 0], "axial", -1)
    if count_x == 1:
        below_inner = passed_along(updated_gas[:, :, 0], "radial", -1)
        field_inner = jnp.concatenate([updated_gas, below_inner[:, :, None]], 2)
        below_face = passed_along(upper_face[:, 0], "radial", -1)
        field_face = jnp.concatenate([upper_face, below_face[:, None]], 1)[:, None]

        def window_part(field):
            layers = field.shape[1]
            part = jnp.einsum(
                "fxnz,wyn->fxwyz", field, window_map(count_y, span_y + 1),
                precision=lax.Precision.HIGH,
            )
            part = part.reshape(5, layers * 5, count_y, span_z)
            part = jnp.einsum(
                "fayz,ekz->faeyk", part, window_map(count_z, span_z),
                precision=lax.Precision.HIGH,
            )
            part = part.reshape(5, layers, 25, brick_total)
            return jnp.einsum("bg,fxwb->gfxw", selector, part, precision=lax.Precision.HIGH)

        picked = jnp.concatenate([window_part(field_inner), window_part(field_face)], 2)
        picked = picked.reshape(block_count, 5, 5, 25)
    else:
        extended = jnp.concatenate([updated_gas, upper_face[:, None]], 1)
        below_row = passed_along(extended[:, :, 0], "radial", -1)
        gas_field = jnp.concatenate([extended, below_row[:, :, None]], 2)
        gas_field = jnp.pad(gas_field, ((0, 0), (0, 0), (0, 0), (0, 1)))
        windows = split_windows(gas_field, 3, count_z)
        windows = split_windows(windows, 2, count_y)
        windows = split_windows(windows, 1, count_x)
        windows = jnp.transpose(windows, (0, 1, 3, 5, 2, 4, 6)).reshape(5, brick_total, 125)
        picked = jnp.einsum("bg,fbe->gfe", selector, windows, precision=lax.Precision.HIGH)
    picked = picked.reshape(block_count, 5, 5, 25)
    partial = jnp.einsum("gfxw,wgp->fxgp", picked, weight_yz, precision=lax.Precision.HIGH)
    values = jnp.sum(partial * factor_x[None], axis=1)
    parcel_gas = values.reshape(5, block_count * 128).astype(jnp.bfloat16)
    return (source, parcel_gas)


def solution(mesh):
    return jax.shard_map(
        per_device,
        mesh=mesh,
        in_specs=(
            P(None, ("axial", "radial")),
            P(None, ("axial", "radial")),
            P(("axial", "radial")),
            P(None, ("axial", "radial")),
            P(("axial", "radial")),
            P(None, "axial", "radial", None),
        ),
        out_specs=(P(None, "axial", "radial", None), P(None, ("axial", "radial"))),
        check_vma=False,
    )
```

```python
import math

import jax
import jax.numpy as jnp
from jax import lax
from jax.experimental import pallas as pl
from jax.experimental.pallas import tpu as pltpu
from jax.sharding import PartitionSpec as P

COUPLE = 0.5


def passed_along(block, axis, distance):
    devices = range(lax.axis_size(axis))
    route = [(i - distance, i) for i in devices if i - distance in devices]
    return lax.ppermute(block, axis, route)


def kernel_weights(cell_index, offsets):
    extent = jnp.arange(128, dtype=jnp.int32)
    brick_x = extent // 25
    brick_y = extent // 5 % 5
    brick_z = extent % 5
    inside = (extent < 125).astype(jnp.float32)

    def factor(cell_coord, brick_coord, fraction):
        cell_coord = cell_coord[:, :, None]
        fraction = fraction[:, :, None]
        return jnp.where(
            brick_coord == cell_coord,
            1.0 - fraction,
            jnp.where(brick_coord == cell_coord + 1, fraction, 0.0),
        )

    cell_x = cell_index // 16
    cell_y = cell_index // 4 % 4
    cell_z = cell_index % 4
    return (
        factor(cell_x, brick_x, offsets[0])
        * factor(cell_y, brick_y, offsets[1])
        * factor(cell_z, brick_z, offsets[2])
        * inside
    )


def axis_factors(cell_index, offsets):
    extent = jnp.arange(5, dtype=jnp.int32).reshape((5,) + (1,) * cell_index.ndim)

    def factor(cell_coord, fraction):
        return jnp.where(
            extent == cell_coord[None],
            1.0 - fraction[None],
            jnp.where(extent == cell_coord[None] + 1, fraction[None], 0.0),
        )

    return (
        factor(cell_index // 16, offsets[0]),
        factor(cell_index // 4 % 4, offsets[1]),
        factor(cell_index % 4, offsets[2]),
    )


def split_windows(field, axis, count):
    core = lax.slice_in_dim(field, 0, 4 * count, axis=axis)
    core = core.reshape(field.shape[:axis] + (count, 4) + field.shape[axis + 1 :])
    tail = lax.slice_in_dim(field, 4, 4 * count + 1, stride=4, axis=axis)
    tail = jnp.expand_dims(tail, axis + 1)
    return jnp.concatenate([core, tail], axis + 1)


def merge_windows(field, axis, count, keep_tail):
    core = lax.slice_in_dim(field, 0, 4, axis=axis + 1)
    tail = lax.slice_in_dim(field, 4, 5, axis=axis + 1)
    zero_brick = jnp.zeros_like(lax.slice_in_dim(core, 0, 1, axis=axis))
    core = jnp.concatenate([core, zero_brick], axis)
    zero_tail = jnp.zeros_like(lax.slice_in_dim(tail, 0, 1, axis=axis))
    tail = jnp.concatenate([zero_tail, tail], axis)
    first = lax.slice_in_dim(core, 0, 1, axis=axis + 1) + tail
    rest = lax.slice_in_dim(core, 1, 4, axis=axis + 1)
    joined = jnp.concatenate([first, rest], axis + 1)
    joined = joined.reshape(field.shape[:axis] + (4 * (count + 1),) + field.shape[axis + 2 :])
    length = 4 * count + 1 if keep_tail else 4 * count
    return lax.slice_in_dim(joined, 0, length, axis=axis)


def window_map(count, length):
    extent = jnp.arange(5, dtype=jnp.int32)[:, None, None]
    brick = jnp.arange(count, dtype=jnp.int32)[None, :, None]
    cell = jnp.arange(length, dtype=jnp.int32)[None, None, :]
    return (4 * brick + extent == cell).astype(jnp.float32)


def radial_fold(layers):
    arrived = passed_along(layers[:, :, -1], "radial", 1)
    return layers.at[:, :, 0].add(arrived)


def departed_mask(cross_rows, resident):
    rows = cross_rows.reshape(-1)
    lanes = 128
    high = jnp.where(rows >= 0, rows // lanes, -1)
    low = jnp.where(rows >= 0, rows % lanes, -1)
    high_hot = (high[None, :] == jnp.arange(resident // lanes, dtype=jnp.int32)[:, None]).astype(jnp.bfloat16)
    low_hot = (low[None, :] == jnp.arange(lanes, dtype=jnp.int32)[:, None]).astype(jnp.bfloat16)
    counts = jnp.einsum("hs,ls->hl", high_hot, low_hot, preferred_element_type=jnp.float32)
    return counts.reshape(resident)


def gather_rows(table, rows, interpret=False):
    slots = rows.shape[0]
    height, width = table.shape
    chunk = math.gcd(slots, 8192)
    steps = slots // chunk
    rows = jnp.clip(rows, 0, height - 1).reshape(steps, 1, chunk)

    def kernel(row_ref, table_ref, out_ref):
        def body(i, carry):
            row = row_ref[0, 0, i]
            out_ref[pl.ds(i, 1), :] = table_ref[pl.ds(row, 1), :]
            return carry

        lax.fori_loop(0, chunk, body, 0, unroll=256)

    return pl.pallas_call(
        kernel,
        out_shape=jax.ShapeDtypeStruct((slots, width), table.dtype),
        grid=(steps,),
        in_specs=[
            pl.BlockSpec((1, 1, chunk), lambda s: (s, 0, 0), memory_space=pltpu.SMEM),
            pl.BlockSpec((height, width), lambda s: (0, 0)),
        ],
        out_specs=pl.BlockSpec((chunk, width), lambda s: (s, 0)),
        compiler_params=pltpu.CompilerParams(vmem_limit_bytes=48 * 1024 * 1024),
        interpret=interpret,
    )(rows, table)


def per_device(parcel_load, parcel_offset, parcel_cell, cross_rows, block_brick, gas):
    span_x = gas.shape[1]
    span_y = gas.shape[2]
    span_z = gas.shape[3]
    count_x = span_x // 4
    count_y = span_y // 4
    count_z = span_z // 4
    brick_total = count_x * count_y * count_z
    resident = parcel_load.shape[1]
    block_count = block_brick.shape[0]
    brick_numbers = jnp.arange(brick_total, dtype=jnp.int32)
    attributes = jnp.concatenate(
        [parcel_load, parcel_offset, parcel_cell[None].astype(jnp.float32)], 0
    )
    usable = cross_rows >= 0
    safe_rows = jnp.maximum(cross_rows, 0)
    table = attributes.T
    flip = jnp.eye(table.shape[1], dtype=jnp.float32)

    def moving(side):
        picked = gather_rows(table, safe_rows[side])
        picked = jnp.einsum("fc,sc->fs", flip, picked, precision=lax.Precision.HIGHEST)
        return picked * usable[side].astype(jnp.float32)

    upward = moving(0)
    from_lower = passed_along(upward, "axial", 1)
    downward = moving(1)
    from_upper = passed_along(downward, "axial", -1)
    departed = departed_mask(cross_rows, resident)
    staying = jnp.concatenate([attributes[:8] * (1.0 - departed)[None], attributes[8:]], 0)
    staying_blocks = resident // 128
    selector = (brick_numbers[:, None] == block_brick[None, :]).astype(jnp.float32)

    def deposit_part(part_rows, part_selector):
        part_blocks = part_rows.shape[1] // 128
        part_rows = part_rows.reshape(9, part_blocks, 128)
        factor_x, factor_y, factor_z = axis_factors(part_rows[8].astype(jnp.int32), part_rows[5:8])
        load_x = (part_rows[:5][:, None] * factor_x[None]).reshape(25, part_blocks, 128)
        weight_yz = (factor_y[:, None] * factor_z[None]).reshape(25, part_blocks, 128)
        spread = jnp.einsum("agp,bgp->gab", load_x, weight_yz, precision=lax.Precision.HIGH)
        part_sums = jnp.einsum(
            "bg,gfe->feb", part_selector, spread.reshape(part_blocks, 5, 125),
            precision=lax.Precision.HIGH,
        )
        return part_sums, factor_x, weight_yz

    stay_sums, stay_x, stay_yz = deposit_part(staying, selector[:, :staying_blocks])
    from_lower, from_upper, stay_sums = lax.optimization_barrier((from_lower, from_upper, stay_sums))
    moved = jnp.concatenate([from_lower, from_upper], 1)
    moved_sums, moved_x, moved_yz = deposit_part(moved, selector[:, staying_blocks:])
    brick_sums = stay_sums + moved_sums
    factor_x = jnp.concatenate([stay_x, moved_x], 1)
    weight_yz = jnp.concatenate([stay_yz, moved_yz], 1)
    if count_x == 1:
        laid = brick_sums.reshape(5, 25, 5, count_y, count_z)
        laid = jnp.einsum(
            "faeyk,ekz->fayz", laid, window_map(count_z, span_z), precision=lax.Precision.HIGH
        )
        laid = laid.reshape(5, 5, 5, count_y, span_z)
        deposit_grid = jnp.einsum(
            "fxwyz,wyn->fxnz", laid, window_map(count_y, span_y + 1),
            precision=lax.Precision.HIGH,
        )
    else:
        laid = jnp.transpose(brick_sums, (0, 2, 1))
        laid = laid.reshape(5, count_x, count_y, count_z, 5, 5, 5)
        laid = jnp.transpose(laid, (0, 1, 4, 2, 5, 3, 6))
        laid = merge_windows(laid, 1, count_x, True)
        laid = merge_windows(laid, 2, count_y, True)
        deposit_grid = merge_windows(laid, 3, count_z, False)
    incoming = passed_along(deposit_grid[:, span_x], "axial", 1)
    summed = deposit_grid[:, :span_x].at[:, 0].add(incoming)
    folded = radial_fold(summed)
    source = folded[:, :, :span_y]
    updated_gas = gas + COUPLE * source
    upper_face = passed_along(updated_gas[:, 0], "axial", -1)
    if count_x == 1:
        below_inner = passed_along(updated_gas[:, :, 0], "radial", -1)
        field_inner = jnp.concatenate([updated_gas, below_inner[:, :, None]], 2)
        below_face = passed_along(upper_face[:, 0], "radial", -1)
        field_face = jnp.concatenate([upper_face, below_face[:, None]], 1)[:, None]

        def window_part(field):
            layers = field.shape[1]
            part = jnp.einsum(
                "fxnz,wyn->fxwyz", field, window_map(count_y, span_y + 1),
                precision=lax.Precision.HIGH,
            )
            part = part.reshape(5, layers * 5, count_y, span_z)
            part = jnp.einsum(
                "fayz,ekz->faeyk", part, window_map(count_z, span_z),
                precision=lax.Precision.HIGH,
            )
            part = part.reshape(5, layers * 25, brick_total)
            return jnp.einsum("bg,feb->gfe", selector, part, precision=lax.Precision.HIGH)

        picked = jnp.concatenate([window_part(field_inner), window_part(field_face)], 2)
    else:
        extended = jnp.concatenate([updated_gas, upper_face[:, None]], 1)
        below_row = passed_along(extended[:, :, 0], "radial", -1)
        gas_field = jnp.concatenate([extended, below_row[:, :, None]], 2)
        gas_field = jnp.pad(gas_field, ((0, 0), (0, 0), (0, 0), (0, 1)))
        windows = split_windows(gas_field, 3, count_z)
        windows = split_windows(windows, 2, count_y)
        windows = split_windows(windows, 1, count_x)
        windows = jnp.transpose(windows, (0, 1, 3, 5, 2, 4, 6)).reshape(5, brick_total, 125)
        picked = jnp.einsum("bg,fbe->gfe", selector, windows, precision=lax.Precision.HIGH)
    picked = picked.reshape(block_count, 25, 25)
    partial = jnp.einsum("gab,bgp->agp", picked, weight_yz, precision=lax.Precision.HIGH)
    values = jnp.sum(partial.reshape(5, 5, block_count, 128) * factor_x[None], axis=1)
    parcel_gas = values.reshape(5, block_count * 128).astype(jnp.bfloat16)
    return (source, parcel_gas)


def solution(mesh):
    return jax.shard_map(
        per_device,
        mesh=mesh,
        in_specs=(
            P(None, ("axial", "radial")),
            P(None, ("axial", "radial")),
            P(("axial", "radial")),
            P(None, ("axial", "radial")),
            P(("axial", "radial")),
            P(None, "axial", "radial", None),
        ),
        out_specs=(P(None, "axial", "radial", None), P(None, ("axial", "radial"))),
        check_vma=False,
    )
```
